32 devices in a mesh: seq: 16 (over z, y, core), head: 2 (over x).
Axes of the slice: x: 2, y: 2, z: 4, core: 2. Of those that a mesh axis runs over, the one named last changes fastest.
Arguments:
- queries: bfloat16 [4096, 4096], P(('seq', 'head')), may hold values from -6 to 6
- keys: bfloat16 [4096, 4096], P(('seq', 'head')), may hold values from -6 to 6
- values: bfloat16 [4096, 4096], P(('seq', 'head')), may hold values from -75 to 75
- out_weight: bfloat16 [4096, 4096], P('seq', 'head'), may hold values from -0.09375 to 0.09375
- norm_gain: float32 [4096], P('head'), may hold values from 0.5 to 1.5
Outputs:
- projected: bfloat16 [4096, 4096], P('seq', 'head')
The draws below stay inside these ranges and needn't reach their ends.
All inputs are finite; a program needn't handle non-finite values.
Results may differ from the reference program's by a relative error of at most 0.0058.
Values may be sent and summed in bfloat16 or wider, within the bound.
No kernel may reach another device: no remote copies, remote signals or barrier semaphores. Data moves between devices by JAX's collectives and lax.ppermute only.
A program may use at most 128 MiB of HBM per device.

```python
import jax
import jax.numpy as jnp
from jax import lax

D = 4096
HEADS = 32
HEAD_DIM = 128
HD = 4096
BLOCK = 256
TOKENS = 4096
N_SEQ = 16


def draw_values(key, part):
    key_main = jax.random.fold_in(key, 11)
    key_rows = jax.random.fold_in(key, 12)
    key_cols = jax.random.fold_in(key, 13)
    spread = 0.5
    base = jnp.clip(jax.random.normal(key_main, (TOKENS, HD), jnp.float32), -4.0, 4.0)
    row_scale = 10.0 ** jax.random.uniform(key_rows, (TOKENS, 1), jnp.float32, -spread, spread)
    col_scale = 10.0 ** jax.random.uniform(key_cols, (1, HD), jnp.float32, -spread, spread)
    return (base * row_scale * col_scale).astype(jnp.bfloat16)


def block_levels(stream_key, extent, shards, least, high):
    def one(position, blocks):
        heights = jax.random.uniform(jax.random.fold_in(jax.random.fold_in(stream_key, 6), position), (blocks,), jnp.float32, least / len(shards), high / len(shards))
        return jnp.repeat(jnp.exp(heights), extent[position] // blocks).reshape((-1,) + (1,) * (len(extent) - position - 1))

    level = one(*shards[0])
    for cut in shards[1:]:
        level = level * one(*cut)
    return level


def noise(key, shape, width, most, cuts=(), kind=jnp.bfloat16):
    array = jax.random.normal(key, shape, jnp.float32) * width
    if len(cuts) > 0:
        array = block_levels(key, shape, cuts, -0.22, 0.18) * array
    return jnp.clip(array, min=-most, max=most).astype(kind)


def setup_inputs(seed: int = 0) -> dict:
    seeds = jax.random.split(jax.random.key(seed), 6)
    return {
        "queries": noise(seeds[0], (TOKENS, HD), 1.0, 6.0, ((0, 32),)),
        "keys": noise(seeds[1], (TOKENS, HD), 1.0, 6.0, ((0, 32),)),
        "values": draw_values(jax.random.fold_in(seeds[5], 71), 0),
        "out_weight": noise(seeds[3], (HD, D), HD ** -0.5, 0.09375, ((0, 16), (1, 2))),
        "norm_gain": jnp.clip(1.0 + 0.1 * jax.random.normal(seeds[4], (HD,), jnp.float32), 0.5, 1.5),
    }


def reference(queries, keys, values, out_weight, norm_gain):
    shaped = (N_SEQ, BLOCK, HEADS, HEAD_DIM)
    query_blocks = queries.reshape(shaped)
    key_blocks = keys.reshape(shaped)
    value_blocks = values.reshape(shaped)
    gain_heads = norm_gain.reshape(HEADS, HEAD_DIM)
    positions = jnp.arange(BLOCK, dtype=jnp.int32)
    causal_mask = positions[None, :] <= positions[:, None]

    def advance(kv_state, inputs):
        query_now, key_now, value_now = inputs
        query_wide = query_now.astype(jnp.float32)
        key_wide = key_now.astype(jnp.float32)
        value_wide = value_now.astype(jnp.float32)
        prefix = lax.optimization_barrier(kv_state.astype(jnp.bfloat16)).astype(jnp.float32)
        carried = jnp.einsum('thd,hde->the', query_wide, prefix)
        scores = jnp.einsum('thd,shd->hts', query_wide, key_wide)
        scores = jnp.where(causal_mask[None], scores, jnp.zeros_like(scores))
        scores = lax.optimization_barrier(scores.astype(jnp.bfloat16)).astype(jnp.float32)
        within_block = jnp.einsum('hts,she->the', scores, value_wide)
        attended = carried + within_block
        mean_square = lax.optimization_barrier(jnp.mean(attended * attended, axis=2, keepdims=True))
        normed = (attended * lax.rsqrt(mean_square + 1e-06) * gain_heads[None]).astype(jnp.bfloat16)
        outcome = jnp.dot(normed.reshape(BLOCK, HD), out_weight, preferred_element_type=jnp.float32)
        next_state = kv_state + jnp.einsum('thd,the->hde', key_wide, value_wide)
        return (next_state, outcome.astype(jnp.bfloat16))
    initial = jnp.zeros((HEADS, HEAD_DIM, HEAD_DIM), jnp.float32)
    final_state, outputs = lax.scan(advance, initial, (query_blocks, key_blocks, value_blocks))
    return outputs.reshape(TOKENS, D)
```

```python
import functools

import jax
import jax.numpy as jnp
from jax import lax
from jax.sharding import PartitionSpec as P

HEAD_DIM = 128


def exclusive_prefix(state, axis, size):
    total = state
    shift = 1
    while shift < size:
        pairs = [(i, i + shift) for i in range(size - shift)]
        total = total + lax.ppermute(total, axis, pairs)
        shift *= 2
    return total - state


def pair_order(own, other, place, axis):
    first = jnp.where(place == 0, own, other)
    second = jnp.where(place == 0, other, own)
    return jnp.concatenate([first, second], axis=axis)


def local(queries, keys, values, out_weight, norm_gain, n_seq, n_head):
    heads_dev = norm_gain.shape[0] // HEAD_DIM
    width = heads_dev * HEAD_DIM
    rows = queries.shape[0]
    weight_full = lax.all_gather(out_weight, "seq", axis=0, tiled=True)
    if n_head == 2:
        place = lax.axis_index("head")
        stacked = jnp.stack([queries, keys, values]).reshape(3, rows, 2, width)
        own = lax.dynamic_index_in_dim(stacked, place, 2, False)
        sent = lax.dynamic_index_in_dim(stacked, 1 - place, 2, False)
        other = lax.ppermute(sent, "head", [(0, 1), (1, 0)])
        block = pair_order(own, other, place, 1)
        query_block, key_block, value_block = block[0], block[1], block[2]
    else:
        query_block, key_block, value_block = (
            lax.all_to_all(queries, "head", split_axis=1, concat_axis=0, tiled=True),
            lax.all_to_all(keys, "head", split_axis=1, concat_axis=0, tiled=True),
            lax.all_to_all(values, "head", split_axis=1, concat_axis=0, tiled=True),
        )
    row_count = query_block.shape[0]
    query_heads = query_block.reshape(row_count, heads_dev, HEAD_DIM)
    key_heads = key_block.reshape(row_count, heads_dev, HEAD_DIM)
    value_heads = value_block.reshape(row_count, heads_dev, HEAD_DIM)
    kv_state = jnp.einsum(
        "thd,the->hde", key_heads, value_heads, preferred_element_type=jnp.float32
    )
    prefix = exclusive_prefix(kv_state, "seq", n_seq)
    carried = jnp.einsum(
        "thd,hde->the", query_heads, prefix.astype(jnp.bfloat16), preferred_element_type=jnp.float32
    )
    block_rows = min(512, row_count)
    parts_list = []
    for first_row in range(0, row_count, block_rows):
        last_row = min(first_row + block_rows, row_count)
        scores = jnp.einsum(
            "thd,shd->hts",
            query_heads[first_row:last_row],
            key_heads[:last_row],
            preferred_element_type=jnp.float32,
        )
        row_index = first_row + lax.broadcasted_iota(jnp.int32, (last_row - first_row, last_row), 0)
        col_index = lax.broadcasted_iota(jnp.int32, (last_row - first_row, last_row), 1)
        scores = jnp.where((col_index <= row_index)[None], scores, jnp.zeros_like(scores)).astype(
            jnp.bfloat16
        )
        parts_list.append(
            jnp.einsum(
                "hts,she->the", scores, value_heads[:last_row], preferred_element_type=jnp.float32
            )
        )
    within_block = jnp.concatenate(parts_list, axis=0)
    attended = carried + within_block
    mean_square = jnp.mean(attended * attended, axis=2, keepdims=True)
    gain_heads = norm_gain.reshape(heads_dev, HEAD_DIM)
    normed = (attended * lax.rsqrt(mean_square + 1e-06) * gain_heads[None]).astype(jnp.bfloat16)
    normed = normed.reshape(row_count, width)
    if n_head == 2:
        other = lax.ppermute(normed, "head", [(0, 1), (1, 0)])
        gathered = pair_order(normed, other, place, 1)
    else:
        gathered = lax.all_gather(normed, "head", axis=1, tiled=True)
    outcome = jnp.dot(gathered, weight_full, preferred_element_type=jnp.float32)
    return outcome.astype(jnp.bfloat16)


def solution(mesh):
    body = functools.partial(local, n_seq=mesh.shape["seq"], n_head=mesh.shape["head"])
    return jax.shard_map(
        body,
        mesh=mesh,
        in_specs=(
            P(("seq", "head"), None),
            P(("seq", "head"), None),
            P(("seq", "head"), None),
            P("seq", "head"),
            P("head"),
        ),
        out_specs=P("seq", "head"),
        check_vma=False,
    )
```

```python
import functools

import jax
import jax.numpy as jnp
from jax import lax
from jax.sharding import Mesh
from jax.sharding import PartitionSpec as P

HEAD_DIM = 128
SWAP = [(0, 1), (1, 0)]


def exclusive_prefix(state, axis, size):
    total = state
    shift = 1
    while shift < size:
        pairs = [(i, i + shift) for i in range(size - shift)]
        total = total + lax.ppermute(total, axis, pairs)
        shift *= 2
    return total - state


def pair_order(own, other, place, axis):
    first = jnp.where(place == 0, own, other)
    second = jnp.where(place == 0, other, own)
    return jnp.concatenate([first, second], axis=axis)


def head_blocks(arrays, n_head, place):
    if n_head == 2:
        rows = arrays[0].shape[0]
        width = arrays[0].shape[1] // 2
        stacked = jnp.stack(arrays).reshape(len(arrays), rows, 2, width)
        own = lax.dynamic_index_in_dim(stacked, place, 2, False)
        sent = lax.dynamic_index_in_dim(stacked, 1 - place, 2, False)
        other = lax.ppermute(sent, "head", SWAP)
        block = pair_order(own, other, place, 1)
        return [block[i] for i in range(len(arrays))]
    return [
        lax.all_to_all(a, "head", split_axis=1, concat_axis=0, tiled=True) for a in arrays
    ]


def local(queries, keys, values, out_weight, norm_gain, n_chip, n_head):
    heads_dev = norm_gain.shape[0] // HEAD_DIM
    width = heads_dev * HEAD_DIM
    core = lax.axis_index("core")
    place = lax.axis_index("head") if n_head == 2 else 0
    weight_own = lax.all_gather(out_weight, "chip", axis=0, tiled=True)
    weight_other = lax.ppermute(weight_own, "core", SWAP)

    key_block, value_block = head_blocks([keys, values], n_head, place)
    (query_block,) = head_blocks([queries], n_head, place)
    row_count = query_block.shape[0]
    query_heads = query_block.reshape(row_count, heads_dev, HEAD_DIM)
    key_heads = key_block.reshape(row_count, heads_dev, HEAD_DIM)
    value_heads = value_block.reshape(row_count, heads_dev, HEAD_DIM)
    kv_state = jnp.einsum(
        "thd,the->hde", key_heads, value_heads, preferred_element_type=jnp.float32
    )
    partner_state = lax.ppermute(kv_state, "core", SWAP)
    chip_state = kv_state + partner_state
    half = heads_dev // 2
    chip_half = lax.dynamic_slice_in_dim(chip_state, core * half, half, 0)
    chip_prefix_half = exclusive_prefix(chip_half, "chip", n_chip)
    other_half = lax.ppermute(chip_prefix_half, "core", SWAP)
    chip_prefix = pair_order(chip_prefix_half, other_half, core, 0)
    prefix = chip_prefix + jnp.where(core == 1, partner_state, jnp.zeros_like(partner_state))

    carried = jnp.einsum(
        "thd,hde->the", query_heads, prefix.astype(jnp.bfloat16), preferred_element_type=jnp.float32
    )
    block_rows = min(512, row_count)
    parts_list = []
    for first_row in range(0, row_count, block_rows):
        last_row = min(first_row + block_rows, row_count)
        scores = jnp.einsum(
            "thd,shd->hts",
            query_heads[first_row:last_row],
            key_heads[:last_row],
            preferred_element_type=jnp.float32,
        )
        row_index = first_row + lax.broadcasted_iota(jnp.int32, (last_row - first_row, last_row), 0)
        col_index = lax.broadcasted_iota(jnp.int32, (last_row - first_row, last_row), 1)
        scores = jnp.where((col_index <= row_index)[None], scores, jnp.zeros_like(scores)).astype(
            jnp.bfloat16
        )
        parts_list.append(
            jnp.einsum(
                "hts,she->the", scores, value_heads[:last_row], preferred_element_type=jnp.float32
            )
        )
    within_block = jnp.concatenate(parts_list, axis=0)
    attended = carried + within_block
    mean_square = jnp.mean(attended * attended, axis=2, keepdims=True)
    gain_heads = norm_gain.reshape(heads_dev, HEAD_DIM)
    normed = (attended * lax.rsqrt(mean_square + 1e-06) * gain_heads[None]).astype(jnp.bfloat16)
    normed = normed.reshape(row_count, width)
    if n_head == 2:
        other = lax.ppermute(normed, "head", SWAP)
        gathered = pair_order(normed, other, place, 1)
    else:
        gathered = lax.all_gather(normed, "head", axis=1, tiled=True)
    weight_rows = out_weight.shape[0]
    split = gathered.reshape(row_count, n_chip, 2, weight_rows)
    normed_own = lax.dynamic_index_in_dim(split, core, 2, False).reshape(row_count, -1)
    normed_other = lax.dynamic_index_in_dim(split, 1 - core, 2, False).reshape(row_count, -1)
    outcome = jnp.dot(normed_own, weight_own, preferred_element_type=jnp.float32)
    outcome = outcome + jnp.dot(normed_other, weight_other, preferred_element_type=jnp.float32)
    return outcome.astype(jnp.bfloat16)


def solution(mesh):
    n_seq = mesh.shape["seq"]
    n_head = mesh.shape["head"]
    fine = Mesh(mesh.devices.reshape(n_seq // 2, 2, n_head), ("chip", "core", "head"))
    rows = ("chip", "core", "head")
    body = functools.partial(local, n_chip=n_seq // 2, n_head=n_head)
    return jax.shard_map(
        body,
        mesh=fine,
        in_specs=(
            P(rows, None),
            P(rows, None),
            P(rows, None),
            P(("chip", "core"), "head"),
            P("head"),
        ),
        out_specs=P(("chip", "core"), "head"),
        check_vma=False,
    )
```

```python
import functools

import jax
import jax.numpy as jnp
from jax import lax
from jax.sharding import Mesh
from jax.sharding import PartitionSpec as P

HEAD_DIM = 128
SWAP = [(0, 1), (1, 0)]


def exclusive_prefix(state, axis, size):
    total = state
    shift = 1
    while shift < size:
        pairs = [(i, i + shift) for i in range(size - shift)]
        total = total + lax.ppermute(total, axis, pairs)
        shift *= 2
    return total - state


def pair_order(own, other, place, axis):
    first = jnp.where(place == 0, own, other)
    second = jnp.where(place == 0, other, own)
    return jnp.concatenate([first, second], axis=axis)


def head_blocks(arrays, n_head, place):
    if n_head == 2:
        rows = arrays[0].shape[0]
        width = arrays[0].shape[1] // 2
        stacked = jnp.stack(arrays).reshape(len(arrays), rows, 2, width)
        own = lax.dynamic_index_in_dim(stacked, place, 2, False)
        sent = lax.dynamic_index_in_dim(stacked, 1 - place, 2, False)
        other = lax.ppermute(sent, "head", SWAP)
        block = pair_order(own, other, place, 1)
        return [block[i] for i in range(len(arrays))]
    return [
        lax.all_to_all(a, "head", split_axis=1, concat_axis=0, tiled=True) for a in arrays
    ]


def local(queries, keys, values, out_weight, norm_gain, n_chip, n_head):
    heads_dev = norm_gain.shape[0] // HEAD_DIM
    width = heads_dev * HEAD_DIM
    core = lax.axis_index("core")
    place = lax.axis_index("head") if n_head == 2 else 0
    weight_own = lax.all_gather(out_weight, "chip", axis=0, tiled=True)

    key_block, value_block = head_blocks([keys, values], n_head, place)
    (query_block,) = head_blocks([queries], n_head, place)
    row_count = query_block.shape[0]
    query_heads = query_block.reshape(row_count, heads_dev, HEAD_DIM)
    key_heads = key_block.reshape(row_count, heads_dev, HEAD_DIM)
    value_heads = value_block.reshape(row_count, heads_dev, HEAD_DIM)
    kv_state = jnp.einsum(
        "thd,the->hde", key_heads, value_heads, preferred_element_type=jnp.float32
    )
    partner_state = lax.ppermute(kv_state, "core", SWAP)
    chip_state = kv_state + partner_state
    half = heads_dev // 2
    chip_half = lax.dynamic_slice_in_dim(chip_state, core * half, half, 0)
    chip_prefix_half = exclusive_prefix(chip_half, "chip", n_chip)
    other_half = lax.ppermute(chip_prefix_half, "core", SWAP)
    chip_prefix = pair_order(chip_prefix_half, other_half, core, 0)
    prefix = chip_prefix + jnp.where(core == 1, partner_state, jnp.zeros_like(partner_state))

    carried = jnp.einsum(
        "thd,hde->the", query_heads, prefix.astype(jnp.bfloat16), preferred_element_type=jnp.float32
    )
    block_rows = min(512, row_count)
    parts_list = []
    for first_row in range(0, row_count, block_rows):
        last_row = min(first_row + block_rows, row_count)
        scores = jnp.einsum(
            "thd,shd->hts",
            query_heads[first_row:last_row],
            key_heads[:last_row],
            preferred_element_type=jnp.float32,
        )
        row_index = first_row + lax.broadcasted_iota(jnp.int32, (last_row - first_row, last_row), 0)
        col_index = lax.broadcasted_iota(jnp.int32, (last_row - first_row, last_row), 1)
        scores = jnp.where((col_index <= row_index)[None], scores, jnp.zeros_like(scores)).astype(
            jnp.bfloat16
        )
        parts_list.append(
            jnp.einsum(
                "hts,she->the", scores, value_heads[:last_row], preferred_element_type=jnp.float32
            )
        )
    within_block = jnp.concatenate(parts_list, axis=0)
    attended = carried + within_block
    mean_square = jnp.mean(attended * attended, axis=2, keepdims=True)
    gain_heads = norm_gain.reshape(heads_dev, HEAD_DIM)
    normed = (attended * lax.rsqrt(mean_square + 1e-06) * gain_heads[None]).astype(jnp.bfloat16)
    normed = normed.reshape(row_count, width)
    if n_head == 2:
        other = lax.ppermute(normed, "head", SWAP)
        gathered = pair_order(normed, other, place, 1)
    else:
        gathered = lax.all_gather(normed, "head", axis=1, tiled=True)
    weight_own, gathered = lax.optimization_barrier((weight_own, gathered))
    weight_other = lax.ppermute(weight_own, "core", SWAP)
    weight_rows = out_weight.shape[0]
    split = gathered.reshape(row_count, n_chip, 2, weight_rows)
    normed_own = lax.dynamic_index_in_dim(split, core, 2, False).reshape(row_count, -1)
    normed_other = lax.dynamic_index_in_dim(split, 1 - core, 2, False).reshape(row_count, -1)
    outcome = jnp.dot(normed_own, weight_own, preferred_element_type=jnp.float32)
    outcome = outcome + jnp.dot(normed_other, weight_other, preferred_element_type=jnp.float32)
    return outcome.astype(jnp.bfloat16)


def solution(mesh):
    n_seq = mesh.shape["seq"]
    n_head = mesh.shape["head"]
    fine = Mesh(mesh.devices.reshape(n_seq // 2, 2, n_head), ("chip", "core", "head"))
    rows = ("chip", "core", "head")
    body = functools.partial(local, n_chip=n_seq // 2, n_head=n_head)
    return jax.shard_map(
        body,
        mesh=fine,
        in_specs=(
            P(rows, None),
            P(rows, None),
            P(rows, None),
            P(("chip", "core"), "head"),
            P("head"),
        ),
        out_specs=P(("chip", "core"), "head"),
        check_vma=False,
    )
```

```python
import functools

import jax
import jax.numpy as jnp
from jax import lax
from jax.sharding import Mesh
from jax.sharding import PartitionSpec as P

HEAD_DIM = 128
SWAP = [(0, 1), (1, 0)]


def exclusive_prefix(state, axis, size):
    total = state
    shift = 1
    while shift < size:
        pairs = [(i, i + shift) for i in range(size - shift)]
        total = total + lax.ppermute(total, axis, pairs)
        shift *= 2
    return total - state


def pair_order(own, other, place, axis):
    first = jnp.where(place == 0, own, other)
    second = jnp.where(place == 0, other, own)
    return jnp.concatenate([first, second], axis=axis)


def head_blocks(arrays, n_head, place):
    if n_head == 2:
        rows = arrays[0].shape[0]
        width = arrays[0].shape[1] // 2
        stacked = jnp.stack(arrays).reshape(len(arrays), rows, 2, width)
        own = lax.dynamic_index_in_dim(stacked, place, 2, False)
        sent = lax.dynamic_index_in_dim(stacked, 1 - place, 2, False)
        other = lax.ppermute(sent, "head", SWAP)
        block = pair_order(own, other, place, 1)
        return [block[i] for i in range(len(arrays))]
    return [
        lax.all_to_all(a, "head", split_axis=1, concat_axis=0, tiled=True) for a in arrays
    ]


def chip_cycle(devices):
    n = devices.shape[0]
    coords = [getattr(devices[j, 0, 0], "coords", None) for j in range(n)]
    if n > 16 or any(c is None for c in coords):
        return None

    def adjacent(a, b):
        return sum(abs(int(u) - int(v)) for u, v in zip(coords[a], coords[b])) == 1

    path = [0]

    def search():
        if len(path) == n:
            return adjacent(path[-1], path[0])
        for k in range(n):
            if k not in path and adjacent(path[-1], k):
                path.append(k)
                if search():
                    return True
                path.pop()
        return False

    return list(path) if search() else None


def ring_gather(block, order):
    n = len(order)
    forward = [(order[i], order[(i + 1) % n]) for i in range(n)]
    backward = [(order[(i + 1) % n], order[i]) for i in range(n)]
    half_rows = block.shape[0] // 2
    got, offsets = [block], [0]
    ahead, behind = block, block
    for step in range(1, n // 2):
        ahead = lax.ppermute(ahead, "chip", forward)
        behind = lax.ppermute(behind, "chip", backward)
        got += [ahead, behind]
        offsets += [step, -step]
    last_ahead = lax.ppermute(ahead[:half_rows], "chip", forward)
    last_behind = lax.ppermute(behind[half_rows:], "chip", backward)
    got.append(jnp.concatenate([last_ahead, last_behind], 0))
    offsets.append(n // 2)
    return got, offsets


def local(queries, keys, values, out_weight, norm_gain, n_chip, n_head, order):
    heads_dev = norm_gain.shape[0] // HEAD_DIM
    width = heads_dev * HEAD_DIM
    core = lax.axis_index("core")
    place = lax.axis_index("head") if n_head == 2 else 0
    if order is None:
        weight_own, offsets = [lax.all_gather(out_weight, "chip", axis=0, tiled=True)], [0]
    else:
        weight_own, offsets = ring_gather(out_weight, order)
        weight_other = [lax.ppermute(w, "core", SWAP) for w in weight_own]

    key_block, value_block = head_blocks([keys, values], n_head, place)
    (query_block,) = head_blocks([queries], n_head, place)
    row_count = query_block.shape[0]
    query_heads = query_block.reshape(row_count, heads_dev, HEAD_DIM)
    key_heads = key_block.reshape(row_count, heads_dev, HEAD_DIM)
    value_heads = value_block.reshape(row_count, heads_dev, HEAD_DIM)
    kv_state = jnp.einsum(
        "thd,the->hde", key_heads, value_heads, preferred_element_type=jnp.float32
    )
    partner_state = lax.ppermute(kv_state, "core", SWAP)
    chip_state = kv_state + partner_state
    half = heads_dev // 2
    chip_half = lax.dynamic_slice_in_dim(chip_state, core * half, half, 0)
    chip_prefix_half = exclusive_prefix(chip_half, "chip", n_chip)
    other_half = lax.ppermute(chip_prefix_half, "core", SWAP)
    chip_prefix = pair_order(chip_prefix_half, other_half, core, 0)
    prefix = chip_prefix + jnp.where(core == 1, partner_state, jnp.zeros_like(partner_state))

    carried = jnp.einsum(
        "thd,hde->the", query_heads, prefix.astype(jnp.bfloat16), preferred_element_type=jnp.float32
    )
    block_rows = min(512, row_count)
    parts_list = []
    for first_row in range(0, row_count, block_rows):
        last_row = min(first_row + block_rows, row_count)
        scores = jnp.einsum(
            "thd,shd->hts",
            query_heads[first_row:last_row],
            key_heads[:last_row],
            preferred_element_type=jnp.float32,
        )
        row_index = first_row + lax.broadcasted_iota(jnp.int32, (last_row - first_row, last_row), 0)
        col_index = lax.broadcasted_iota(jnp.int32, (last_row - first_row, last_row), 1)
        scores = jnp.where((col_index <= row_index)[None], scores, jnp.zeros_like(scores)).astype(
            jnp.bfloat16
        )
        parts_list.append(
            jnp.einsum(
                "hts,she->the", scores, value_heads[:last_row], preferred_element_type=jnp.float32
            )
        )
    within_block = jnp.concatenate(parts_list, axis=0)
    attended = carried + within_block
    mean_square = jnp.mean(attended * attended, axis=2, keepdims=True)
    gain_heads = norm_gain.reshape(heads_dev, HEAD_DIM)
    normed = (attended * lax.rsqrt(mean_square + 1e-06) * gain_heads[None]).astype(jnp.bfloat16)
    normed = normed.reshape(row_count, width)
    if n_head == 2:
        other = lax.ppermute(normed, "head", SWAP)
        gathered = pair_order(normed, other, place, 1)
    else:
        gathered = lax.all_gather(normed, "head", axis=1, tiled=True)
    weight_rows = out_weight.shape[0]
    split = gathered.reshape(row_count, n_chip, 2, weight_rows)
    if order is None:
        weight_own, split = lax.optimization_barrier((weight_own[0], split))
        weight_other = lax.ppermute(weight_own, "core", SWAP)
        normed_own = lax.dynamic_index_in_dim(split, core, 2, False).reshape(row_count, -1)
        normed_other = lax.dynamic_index_in_dim(split, 1 - core, 2, False).reshape(row_count, -1)
        outcome = jnp.dot(normed_own, weight_own, preferred_element_type=jnp.float32)
        outcome = outcome + jnp.dot(normed_other, weight_other, preferred_element_type=jnp.float32)
        return outcome.astype(jnp.bfloat16)
    ring_place = jnp.asarray([order.index(j) for j in range(n_chip)], jnp.int32)[lax.axis_index("chip")]
    sources = jnp.asarray(order, jnp.int32)[(ring_place - jnp.asarray(offsets, jnp.int32)) % n_chip]
    by_offset = jnp.take(split, sources, axis=1)
    normed_own = lax.dynamic_index_in_dim(by_offset, core, 2, False)
    normed_other = lax.dynamic_index_in_dim(by_offset, 1 - core, 2, False)
    outcome = None
    for i in range(len(offsets)):
        part = jnp.dot(normed_own[:, i], weight_own[i], preferred_element_type=jnp.float32)
        part = part + jnp.dot(normed_other[:, i], weight_other[i], preferred_element_type=jnp.float32)
        outcome = part if outcome is None else outcome + part
    return outcome.astype(jnp.bfloat16)


def solution(mesh):
    n_seq = mesh.shape["seq"]
    n_head = mesh.shape["head"]
    fine = Mesh(mesh.devices.reshape(n_seq // 2, 2, n_head), ("chip", "core", "head"))
    rows = ("chip", "core", "head")
    order = chip_cycle(fine.devices)
    body = functools.partial(local, n_chip=n_seq // 2, n_head=n_head, order=order)
    return jax.shard_map(
        body,
        mesh=fine,
        in_specs=(
            P(rows, None),
            P(rows, None),
            P(rows, None),
            P(("chip", "core"), "head"),
            P("head"),
        ),
        out_specs=P(("chip", "core"), "head"),
        check_vma=False,
    )
```

```python
import functools

import jax
import jax.numpy as jnp
from jax import lax
from jax.sharding import Mesh
from jax.sharding import PartitionSpec as P

HEAD_DIM = 128
SWAP = [(0, 1), (1, 0)]


def exclusive_prefix(state, axis, size):
    total = state
    shift = 1
    while shift < size:
        pairs = [(i, i + shift) for i in range(size - shift)]
        total = total + lax.ppermute(total, axis, pairs)
        shift *= 2
    return total - state


def pair_order(own, other, place, axis):
    first = jnp.where(place == 0, own, other)
    second = jnp.where(place == 0, other, own)
    return jnp.concatenate([first, second], axis=axis)


def head_blocks(arrays, n_head, place):
    if n_head == 2:
        rows = arrays[0].shape[0]
        width = arrays[0].shape[1] // 2
        stacked = jnp.stack(arrays).reshape(len(arrays), rows, 2, width)
        own = lax.dynamic_index_in_dim(stacked, place, 2, False)
        sent = lax.dynamic_index_in_dim(stacked, 1 - place, 2, False)
        other = lax.ppermute(sent, "head", SWAP)
        block = pair_order(own, other, place, 1)
        return [block[i] for i in range(len(arrays))]
    return [
        lax.all_to_all(a, "head", split_axis=1, concat_axis=0, tiled=True) for a in arrays
    ]


def chip_cycle(devices):
    n = devices.shape[0]
    coords = [getattr(devices[j, 0, 0], "coords", None) for j in range(n)]
    if n > 16 or any(c is None for c in coords):
        return None

    def adjacent(a, b):
        return sum(abs(int(u) - int(v)) for u, v in zip(coords[a], coords[b])) == 1

    path = [0]

    def search():
        if len(path) == n:
            return adjacent(path[-1], path[0])
        for k in range(n):
            if k not in path and adjacent(path[-1], k):
                path.append(k)
                if search():
                    return True
                path.pop()
        return False

    return list(path) if search() else None


def ring_links(order):
    n = len(order)
    forward = [(order[i], order[(i + 1) % n]) for i in range(n)]
    backward = [(order[(i + 1) % n], order[i]) for i in range(n)]
    return forward, backward


def ring_step(ahead, behind, order, last=False):
    forward, backward = ring_links(order)
    if last:
        half_rows = ahead.shape[0] // 2
        return lax.ppermute(ahead[:half_rows], "chip", forward), lax.ppermute(
            behind[half_rows:], "chip", backward
        )
    return lax.ppermute(ahead, "chip", forward), lax.ppermute(behind, "chip", backward)


def local(queries, keys, values, out_weight, norm_gain, n_chip, n_head, order):
    heads_dev = norm_gain.shape[0] // HEAD_DIM
    width = heads_dev * HEAD_DIM
    core = lax.axis_index("core")
    place = lax.axis_index("head") if n_head == 2 else 0
    key_block, value_block = head_blocks([keys, values], n_head, place)
    if order is None:
        weight_own, offsets = [lax.all_gather(out_weight, "chip", axis=0, tiled=True)], [0]
    else:
        ahead, behind = ring_step(out_weight, out_weight, order, last=len(order) == 2)
        ahead, behind, key_block, value_block = lax.optimization_barrier(
            (ahead, behind, key_block, value_block)
        )
    (query_block,) = head_blocks([queries], n_head, place)
    row_count = query_block.shape[0]
    query_heads = query_block.reshape(row_count, heads_dev, HEAD_DIM)
    key_heads = key_block.reshape(row_count, heads_dev, HEAD_DIM)
    value_heads = value_block.reshape(row_count, heads_dev, HEAD_DIM)
    kv_state = jnp.einsum(
        "thd,the->hde", key_heads, value_heads, preferred_element_type=jnp.float32
    )
    partner_state = lax.ppermute(kv_state, "core", SWAP)
    chip_state = kv_state + partner_state
    half = heads_dev // 2
    chip_half = lax.dynamic_slice_in_dim(chip_state, core * half, half, 0)
    chip_prefix_half = exclusive_prefix(chip_half, "chip", n_chip)
    other_half = lax.ppermute(chip_prefix_half, "core", SWAP)
    chip_prefix = pair_order(chip_prefix_half, other_half, core, 0)
    prefix = chip_prefix + jnp.where(core == 1, partner_state, jnp.zeros_like(partner_state))
    if order is not None:
        n_steps = len(order) // 2
        got, offsets = [out_weight], [0]
        if n_steps > 1:
            got += [ahead, behind]
            offsets += [1, -1]
        ahead, behind, prefix = lax.optimization_barrier((ahead, behind, prefix))
        pending = []
        for step in range(2, n_steps + 1):
            ahead, behind = ring_step(ahead, behind, order, last=step == n_steps)
            if step == n_steps:
                got.append(jnp.concatenate([ahead, behind], 0))
                offsets.append(step)
            else:
                got += [ahead, behind]
                offsets += [step, -step]
            pending.append(len(got))
        if n_steps == 1:
            got.append(jnp.concatenate([ahead, behind], 0))
            offsets.append(1)
        swapped = [lax.ppermute(w, "core", SWAP) for w in got]

    carried = jnp.einsum(
        "thd,hde->the", query_heads, prefix.astype(jnp.bfloat16), preferred_element_type=jnp.float32
    )
    block_rows = min(512, row_count)
    parts_list = []
    for first_row in range(0, row_count, block_rows):
        last_row = min(first_row + block_rows, row_count)
        scores = jnp.einsum(
            "thd,shd->hts",
            query_heads[first_row:last_row],
            key_heads[:last_row],
            preferred_element_type=jnp.float32,
        )
        row_index = first_row + lax.broadcasted_iota(jnp.int32, (last_row - first_row, last_row), 0)
        col_index = lax.broadcasted_iota(jnp.int32, (last_row - first_row, last_row), 1)
        scores = jnp.where((col_index <= row_index)[None], scores, jnp.zeros_like(scores)).astype(
            jnp.bfloat16
        )
        parts_list.append(
            jnp.einsum(
                "hts,she->the", scores, value_heads[:last_row], preferred_element_type=jnp.float32
            )
        )
    within_block = jnp.concatenate(parts_list, axis=0)
    attended = carried + within_block
    mean_square = jnp.mean(attended * attended, axis=2, keepdims=True)
    gain_heads = norm_gain.reshape(heads_dev, HEAD_DIM)
    normed = (attended * lax.rsqrt(mean_square + 1e-06) * gain_heads[None]).astype(jnp.bfloat16)
    normed = normed.reshape(row_count, width)
    if order is not None and len(pending) > 1:
        first = pending[0]
        pinned = lax.optimization_barrier((got[:first], swapped[:first], normed))
        got[:first], swapped[:first], normed = list(pinned[0]), list(pinned[1]), pinned[2]
    if n_head == 2:
        other = lax.ppermute(normed, "head", SWAP)
        gathered = pair_order(normed, other, place, 1)
    else:
        gathered = lax.all_gather(normed, "head", axis=1, tiled=True)
    weight_rows = out_weight.shape[0]
    split = gathered.reshape(row_count, n_chip, 2, weight_rows)
    if order is None:
        weight_own, split = lax.optimization_barrier((weight_own[0], split))
        weight_other = lax.ppermute(weight_own, "core", SWAP)
        normed_own = lax.dynamic_index_in_dim(split, core, 2, False).reshape(row_count, -1)
        normed_other = lax.dynamic_index_in_dim(split, 1 - core, 2, False).reshape(row_count, -1)
        outcome = jnp.dot(normed_own, weight_own, preferred_element_type=jnp.float32)
        outcome = outcome + jnp.dot(normed_other, weight_other, preferred_element_type=jnp.float32)
        return outcome.astype(jnp.bfloat16)
    weight_own, weight_other = got, swapped
    ring_place = jnp.asarray([order.index(j) for j in range(n_chip)], jnp.int32)[lax.axis_index("chip")]
    sources = jnp.asarray(order, jnp.int32)[(ring_place - jnp.asarray(offsets, jnp.int32)) % n_chip]
    by_offset = jnp.take(split, sources, axis=1)
    normed_own = lax.dynamic_index_in_dim(by_offset, core, 2, False)
    normed_other = lax.dynamic_index_in_dim(by_offset, 1 - core, 2, False)
    outcome = None
    for i in range(len(offsets)):
        part = jnp.dot(normed_own[:, i], weight_own[i], preferred_element_type=jnp.float32)
        part = part + jnp.dot(normed_other[:, i], weight_other[i], preferred_element_type=jnp.float32)
        outcome = part if outcome is None else outcome + part
    return outcome.astype(jnp.bfloat16)


def solution(mesh):
    n_seq = mesh.shape["seq"]
    n_head = mesh.shape["head"]
    fine = Mesh(mesh.devices.reshape(n_seq // 2, 2, n_head), ("chip", "core", "head"))
    rows = ("chip", "core", "head")
    order = chip_cycle(fine.devices)
    body = functools.partial(local, n_chip=n_seq // 2, n_head=n_head, order=order)
    return jax.shard_map(
        body,
        mesh=fine,
        in_specs=(
            P(rows, None),
            P(rows, None),
            P(rows, None),
            P(("chip", "core"), "head"),
            P("head"),
        ),
        out_specs=P(("chip", "core"), "head"),
        check_vma=False,
    )
```

```python
import functools

import jax
import jax.numpy as jnp
from jax import lax
from jax.sharding import Mesh
from jax.sharding import PartitionSpec as P

HEAD_DIM = 128
SWAP = [(0, 1), (1, 0)]


def exclusive_prefix(state, axis, size):
    total = state
    shift = 1
    while shift < size:
        pairs = [(i, i + shift) for i in range(size - shift)]
        total = total + lax.ppermute(total, axis, pairs)
        shift *= 2
    return total - state


def pair_order(own, other, place, axis):
    first = jnp.where(place == 0, own, other)
    second = jnp.where(place == 0, other, own)
    return jnp.concatenate([first, second], axis=axis)


def head_blocks(arrays, n_head, place):
    if n_head == 2:
        rows = arrays[0].shape[0]
        width = arrays[0].shape[1] // 2
        stacked = jnp.stack(arrays).reshape(len(arrays), rows, 2, width)
        own = lax.dynamic_index_in_dim(stacked, place, 2, False)
        sent = lax.dynamic_index_in_dim(stacked, 1 - place, 2, False)
        other = lax.ppermute(sent, "head", SWAP)
        block = pair_order(own, other, place, 1)
        return [block[i] for i in range(len(arrays))]
    return [
        lax.all_to_all(a, "head", split_axis=1, concat_axis=0, tiled=True) for a in arrays
    ]


def chip_cycle(devices):
    n = devices.shape[0]
    coords = [getattr(devices[j, 0, 0], "coords", None) for j in range(n)]
    if n < 4 or n > 16 or any(c is None for c in coords):
        return None

    def adjacent(a, b):
        return sum(abs(int(u) - int(v)) for u, v in zip(coords[a], coords[b])) == 1

    path = [0]

    def search():
        if len(path) == n:
            return adjacent(path[-1], path[0])
        for k in range(n):
            if k not in path and adjacent(path[-1], k):
                path.append(k)
                if search():
                    return True
                path.pop()
        return False

    return list(path) if search() else None


def ring_links(order):
    n = len(order)
    forward = [(order[i], order[(i + 1) % n]) for i in range(n)]
    backward = [(order[(i + 1) % n], order[i]) for i in range(n)]
    return forward, backward


def ring_step(ahead, behind, order, last=False):
    forward, backward = ring_links(order)
    if last:
        half_rows = ahead.shape[0] // 2
        return lax.ppermute(ahead[:half_rows], "chip", forward), lax.ppermute(
            behind[half_rows:], "chip", backward
        )
    return lax.ppermute(ahead, "chip", forward), lax.ppermute(behind, "chip", backward)


def local(queries, keys, values, out_weight, norm_gain, n_chip, n_head, order):
    heads_dev = norm_gain.shape[0] // HEAD_DIM
    width = heads_dev * HEAD_DIM
    core = lax.axis_index("core")
    place = lax.axis_index("head") if n_head == 2 else 0
    query_block, key_block, value_block = head_blocks([queries, keys, values], n_head, place)
    if order is None:
        weight_own, offsets = [lax.all_gather(out_weight, "chip", axis=0, tiled=True)], [0]
    else:
        ahead, behind = ring_step(out_weight, out_weight, order, last=len(order) == 2)
        ahead, behind, key_block, value_block = lax.optimization_barrier(
            (ahead, behind, key_block, value_block)
        )
    row_count = query_block.shape[0]
    query_heads = query_block.reshape(row_count, heads_dev, HEAD_DIM)
    key_heads = key_block.reshape(row_count, heads_dev, HEAD_DIM)
    value_heads = value_block.reshape(row_count, heads_dev, HEAD_DIM)
    kv_state = jnp.einsum(
        "thd,the->hde", key_heads, value_heads, preferred_element_type=jnp.float32
    )
    partner_state = lax.ppermute(kv_state, "core", SWAP)
    chip_state = kv_state + partner_state
    half = heads_dev // 2
    chip_half = lax.dynamic_slice_in_dim(chip_state, core * half, half, 0)
    if order is not None:
        n_steps = len(order) // 2
        got, offsets = [out_weight], [0]
        if n_steps > 1:
            got += [ahead, behind]
            offsets += [1, -1]
        if n_steps > 2:
            ahead, behind = ring_step(ahead, behind, order, last=n_steps == 2)
            got += [ahead, behind]
            offsets += [2, -2]
        ahead, behind, chip_half = lax.optimization_barrier((ahead, behind, chip_half))
        got[-2:] = [ahead, behind]
    chip_prefix_half = exclusive_prefix(chip_half, "chip", n_chip)
    other_half = lax.ppermute(chip_prefix_half, "core", SWAP)
    chip_prefix = pair_order(chip_prefix_half, other_half, core, 0)
    prefix = chip_prefix + jnp.where(core == 1, partner_state, jnp.zeros_like(partner_state))
    if order is not None:
        ahead, behind, prefix = lax.optimization_barrier((ahead, behind, prefix))
        pending = []
        for step in range(min(3, n_steps), n_steps + 1):
            ahead, behind = ring_step(ahead, behind, order, last=step == n_steps)
            if step == n_steps:
                got.append(jnp.concatenate([ahead, behind], 0))
                offsets.append(step)
            else:
                got += [ahead, behind]
                offsets += [step, -step]
            pending.append(len(got))
        if n_steps == 1:
            got.append(jnp.concatenate([ahead, behind], 0))
            offsets.append(1)
        swapped = [lax.ppermute(w, "core", SWAP) for w in got]

    carried = jnp.einsum(
        "thd,hde->the", query_heads, prefix.astype(jnp.bfloat16), preferred_element_type=jnp.float32
    )
    block_rows = min(512, row_count)
    parts_list = []
    for first_row in range(0, row_count, block_rows):
        last_row = min(first_row + block_rows, row_count)
        scores = jnp.einsum(
            "thd,shd->hts",
            query_heads[first_row:last_row],
            key_heads[:last_row],
            preferred_element_type=jnp.float32,
        )
        row_index = first_row + lax.broadcasted_iota(jnp.int32, (last_row - first_row, last_row), 0)
        col_index = lax.broadcasted_iota(jnp.int32, (last_row - first_row, last_row), 1)
        scores = jnp.where((col_index <= row_index)[None], scores, jnp.zeros_like(scores)).astype(
            jnp.bfloat16
        )
        parts_list.append(
            jnp.einsum(
                "hts,she->the", scores, value_heads[:last_row], preferred_element_type=jnp.float32
            )
        )
    within_block = jnp.concatenate(parts_list, axis=0)
    attended = carried + within_block
    mean_square = jnp.mean(attended * attended, axis=2, keepdims=True)
    gain_heads = norm_gain.reshape(heads_dev, HEAD_DIM)
    normed = (attended * lax.rsqrt(mean_square + 1e-06) * gain_heads[None]).astype(jnp.bfloat16)
    normed = normed.reshape(row_count, width)
    if order is not None and len(pending) > 1:
        first = pending[0]
        pinned = lax.optimization_barrier((got[:first], swapped[:first], normed))
        got[:first], swapped[:first], normed = list(pinned[0]), list(pinned[1]), pinned[2]
    if n_head == 2:
        other = lax.ppermute(normed, "head", SWAP)
        gathered = pair_order(normed, other, place, 1)
    else:
        gathered = lax.all_gather(normed, "head", axis=1, tiled=True)
    weight_rows = out_weight.shape[0]
    split = gathered.reshape(row_count, n_chip, 2, weight_rows)
    if order is None:
        weight_own, split = lax.optimization_barrier((weight_own[0], split))
        weight_other = lax.ppermute(weight_own, "core", SWAP)
        normed_own = lax.dynamic_index_in_dim(split, core, 2, False).reshape(row_count, -1)
        normed_other = lax.dynamic_index_in_dim(split, 1 - core, 2, False).reshape(row_count, -1)
        outcome = jnp.dot(normed_own, weight_own, preferred_element_type=jnp.float32)
        outcome = outcome + jnp.dot(normed_other, weight_other, preferred_element_type=jnp.float32)
        return outcome.astype(jnp.bfloat16)
    weight_own, weight_other = got, swapped
    ring_place = jnp.asarray([order.index(j) for j in range(n_chip)], jnp.int32)[lax.axis_index("chip")]
    sources = jnp.asarray(order, jnp.int32)[(ring_place - jnp.asarray(offsets, jnp.int32)) % n_chip]
    by_offset = jnp.take(split, sources, axis=1)
    by_offset = jnp.where(core == 0, by_offset, by_offset[:, :, ::-1])
    weight_all = jnp.concatenate([w for pair in zip(weight_own, weight_other) for w in pair], 0)
    outcome = jnp.dot(
        by_offset.reshape(row_count, -1), weight_all, preferred_element_type=jnp.float32
    )
    return outcome.astype(jnp.bfloat16)


def solution(mesh):
    n_seq = mesh.shape["seq"]
    n_head = mesh.shape["head"]
    fine = Mesh(mesh.devices.reshape(n_seq // 2, 2, n_head), ("chip", "core", "head"))
    rows = ("chip", "core", "head")
    order = chip_cycle(fine.devices)
    body = functools.partial(local, n_chip=n_seq // 2, n_head=n_head, order=order)
    return jax.shard_map(
        body,
        mesh=fine,
        in_specs=(
            P(rows, None),
            P(rows, None),
            P(rows, None),
            P(("chip", "core"), "head"),
            P("head"),
        ),
        out_specs=P(("chip", "core"), "head"),
        check_vma=False,
    )
```

```python
import functools

import jax
import jax.numpy as jnp
from jax import lax
from jax.sharding import Mesh
from jax.sharding import PartitionSpec as P

HEAD_DIM = 128
SWAP = [(0, 1), (1, 0)]


def exclusive_prefix(state, axis, size):
    total = state
    shift = 1
    while shift < size:
        pairs = [(i, i + shift) for i in range(size - shift)]
        total = total + lax.ppermute(total, axis, pairs)
        shift *= 2
    return total - state


def pair_order(own, other, place, axis):
    first = jnp.where(place == 0, own, other)
    second = jnp.where(place == 0, other, own)
    return jnp.concatenate([first, second], axis=axis)


def head_blocks(arrays, n_head, place):
    if n_head == 2:
        rows = arrays[0].shape[0]
        width = arrays[0].shape[1] // 2
        stacked = jnp.stack(arrays).reshape(len(arrays), rows, 2, width)
        own = lax.dynamic_index_in_dim(stacked, place, 2, False)
        sent = lax.dynamic_index_in_dim(stacked, 1 - place, 2, False)
        other = lax.ppermute(sent, "head", SWAP)
        block = pair_order(own, other, place, 1)
        return [block[i] for i in range(len(arrays))]
    return [
        lax.all_to_all(a, "head", split_axis=1, concat_axis=0, tiled=True) for a in arrays
    ]


def chip_cycle(devices):
    n = devices.shape[0]
    coords = [getattr(devices[j, 0, 0], "coords", None) for j in range(n)]
    if n < 4 or n > 16 or any(c is None for c in coords):
        return None

    def adjacent(a, b):
        return sum(abs(int(u) - int(v)) for u, v in zip(coords[a], coords[b])) == 1

    path = [0]

    def search():
        if len(path) == n:
            return adjacent(path[-1], path[0])
        for k in range(n):
            if k not in path and adjacent(path[-1], k):
                path.append(k)
                if search():
                    return True
                path.pop()
        return False

    return list(path) if search() else None


def ring_links(order):
    n = len(order)
    forward = [(order[i], order[(i + 1) % n]) for i in range(n)]
    backward = [(order[(i + 1) % n], order[i]) for i in range(n)]
    return forward, backward


def ring_step(ahead, behind, order, last=False):
    forward, backward = ring_links(order)
    if last:
        half_rows = ahead.shape[0] // 2
        return lax.ppermute(ahead[:half_rows], "chip", forward), lax.ppermute(
            behind[half_rows:], "chip", backward
        )
    return lax.ppermute(ahead, "chip", forward), lax.ppermute(behind, "chip", backward)


def within_block_part(query_heads, key_heads, value_heads):
    row_count = query_heads.shape[0]
    block_rows = min(512, row_count)
    parts_list = []
    for first_row in range(0, row_count, block_rows):
        last_row = min(first_row + block_rows, row_count)
        scores = jnp.einsum(
            "thd,shd->hts",
            query_heads[first_row:last_row],
            key_heads[:last_row],
            preferred_element_type=jnp.float32,
        )
        row_index = first_row + lax.broadcasted_iota(jnp.int32, (last_row - first_row, last_row), 0)
        col_index = lax.broadcasted_iota(jnp.int32, (last_row - first_row, last_row), 1)
        scores = jnp.where((col_index <= row_index)[None], scores, jnp.zeros_like(scores)).astype(
            jnp.bfloat16
        )
        parts_list.append(
            jnp.einsum(
                "hts,she->the", scores, value_heads[:last_row], preferred_element_type=jnp.float32
            )
        )
    return jnp.concatenate(parts_list, axis=0)


def normalize(query_heads, prefix, within_block, norm_gain):
    heads_dev = query_heads.shape[1]
    carried = jnp.einsum(
        "thd,hde->the", query_heads, prefix.astype(jnp.bfloat16), preferred_element_type=jnp.float32
    )
    attended = carried + within_block
    mean_square = jnp.mean(attended * attended, axis=2, keepdims=True)
    gain_heads = norm_gain.reshape(heads_dev, HEAD_DIM)
    normed = (attended * lax.rsqrt(mean_square + 1e-06) * gain_heads[None]).astype(jnp.bfloat16)
    return normed.reshape(query_heads.shape[0], heads_dev * HEAD_DIM)


def gather_head(normed, n_head, place):
    if n_head == 2:
        other = lax.ppermute(normed, "head", SWAP)
        return pair_order(normed, other, place, 1)
    return lax.all_gather(normed, "head", axis=1, tiled=True)


def chip_scan(kv_state, core, n_chip):
    partner_state = lax.ppermute(kv_state, "core", SWAP)
    chip_state = kv_state + partner_state
    half = kv_state.shape[0] // 2
    chip_half = lax.dynamic_slice_in_dim(chip_state, core * half, half, 0)
    return partner_state, chip_half


def chip_finish(chip_prefix_half, partner_state, core):
    other_half = lax.ppermute(chip_prefix_half, "core", SWAP)
    chip_prefix = pair_order(chip_prefix_half, other_half, core, 0)
    return chip_prefix + jnp.where(core == 1, partner_state, jnp.zeros_like(partner_state))


def split_heads(block, heads_dev):
    return block.reshape(block.shape[0], heads_dev, HEAD_DIM)


def local_gather(queries, keys, values, out_weight, norm_gain, n_chip, n_head):
    heads_dev = norm_gain.shape[0] // HEAD_DIM
    core = lax.axis_index("core")
    place = lax.axis_index("head") if n_head == 2 else 0
    weight_own = lax.all_gather(out_weight, "chip", axis=0, tiled=True)
    query_block, key_block, value_block = head_blocks([queries, keys, values], n_head, place)
    query_heads, key_heads, value_heads = (
        split_heads(b, heads_dev) for b in (query_block, key_block, value_block)
    )
    kv_state = jnp.einsum(
        "thd,the->hde", key_heads, value_heads, preferred_element_type=jnp.float32
    )
    partner_state, chip_half = chip_scan(kv_state, core, n_chip)
    prefix = chip_finish(exclusive_prefix(chip_half, "chip", n_chip), partner_state, core)
    within_block = within_block_part(query_heads, key_heads, value_heads)
    normed = normalize(query_heads, prefix, within_block, norm_gain)
    gathered = gather_head(normed, n_head, place)
    row_count = gathered.shape[0]
    split = gathered.reshape(row_count, n_chip, 2, out_weight.shape[0])
    weight_own, split = lax.optimization_barrier((weight_own, split))
    weight_other = lax.ppermute(weight_own, "core", SWAP)
    normed_own = lax.dynamic_index_in_dim(split, core, 2, False).reshape(row_count, -1)
    normed_other = lax.dynamic_index_in_dim(split, 1 - core, 2, False).reshape(row_count, -1)
    outcome = jnp.dot(normed_own, weight_own, preferred_element_type=jnp.float32)
    outcome = outcome + jnp.dot(normed_other, weight_other, preferred_element_type=jnp.float32)
    return outcome.astype(jnp.bfloat16)


def local_ring(queries, keys, values, out_weight, norm_gain, n_chip, n_head, order):
    heads_dev = norm_gain.shape[0] // HEAD_DIM
    core = lax.axis_index("core")
    place = lax.axis_index("head")
    n_steps = n_chip // 2
    barrier = lax.optimization_barrier
    key_block, value_block = head_blocks([keys, values], n_head, place)
    ahead, behind = ring_step(out_weight, out_weight, order)
    ahead, behind, key_block, value_block = barrier((ahead, behind, key_block, value_block))
    got = [out_weight, ahead, behind]
    offsets = [0, 1, -1]
    (query_block,) = head_blocks([queries], n_head, place)
    ahead, behind = ring_step(ahead, behind, order, last=n_steps == 2)
    swapped = [lax.ppermute(w, "core", SWAP) for w in got]
    key_heads, value_heads = split_heads(key_block, heads_dev), split_heads(value_block, heads_dev)
    kv_state = jnp.einsum(
        "thd,the->hde", key_heads, value_heads, preferred_element_type=jnp.float32
    )
    partner_state, chip_half = chip_scan(kv_state, core, n_chip)
    ahead, behind, swapped, partner_state, chip_half = barrier(
        (ahead, behind, swapped, partner_state, chip_half)
    )
    if n_steps == 2:
        got.append(jnp.concatenate([ahead, behind], 0))
        offsets.append(2)
    else:
        got += [ahead, behind]
        offsets += [2, -2]
    chip_prefix_half = exclusive_prefix(chip_half, "chip", n_chip)
    query_heads = split_heads(query_block, heads_dev)
    within_block = within_block_part(query_heads, key_heads, value_heads)
    swapped += [lax.ppermute(w, "core", SWAP) for w in got[len(swapped):]]
    chip_prefix_half, within_block, swapped = barrier((chip_prefix_half, within_block, swapped))
    for step in range(3, n_steps + 1):
        ahead, behind = ring_step(ahead, behind, order, last=step == n_steps)
        if step == n_steps:
            got.append(jnp.concatenate([ahead, behind], 0))
            offsets.append(step)
        else:
            got += [ahead, behind]
            offsets += [step, -step]
    swapped += [lax.ppermute(w, "core", SWAP) for w in got[len(swapped):]]
    prefix = chip_finish(chip_prefix_half, partner_state, core)
    normed = normalize(query_heads, prefix, within_block, norm_gain)
    gathered = gather_head(normed, n_head, place)
    row_count = gathered.shape[0]
    split = gathered.reshape(row_count, n_chip, 2, out_weight.shape[0])
    ring_place = jnp.asarray([order.index(j) for j in range(n_chip)], jnp.int32)[lax.axis_index("chip")]
    sources = jnp.asarray(order, jnp.int32)[(ring_place - jnp.asarray(offsets, jnp.int32)) % n_chip]
    by_offset = jnp.take(split, sources, axis=1)
    normed_own = lax.dynamic_index_in_dim(by_offset, core, 2, False)
    normed_other = lax.dynamic_index_in_dim(by_offset, 1 - core, 2, False)
    outcome = None
    for i in range(len(offsets)):
        part = jnp.dot(normed_own[:, i], got[i], preferred_element_type=jnp.float32)
        part = part + jnp.dot(normed_other[:, i], swapped[i], preferred_element_type=jnp.float32)
        outcome = part if outcome is None else outcome + part
    return outcome.astype(jnp.bfloat16)


def solution(mesh):
    n_seq = mesh.shape["seq"]
    n_head = mesh.shape["head"]
    fine = Mesh(mesh.devices.reshape(n_seq // 2, 2, n_head), ("chip", "core", "head"))
    rows = ("chip", "core", "head")
    order = chip_cycle(fine.devices) if n_head == 2 else None
    if order is None:
        body = functools.partial(local_gather, n_chip=n_seq // 2, n_head=n_head)
    else:
        body = functools.partial(local_ring, n_chip=n_seq // 2, n_head=n_head, order=order)
    return jax.shard_map(
        body,
        mesh=fine,
        in_specs=(
            P(rows, None),
            P(rows, None),
            P(rows, None),
            P(("chip", "core"), "head"),
            P("head"),
        ),
        out_specs=P(("chip", "core"), "head"),
        check_vma=False,
    )
```

```python
import functools

import jax
import jax.numpy as jnp
from jax import lax
from jax.experimental import pallas as pl
from jax.experimental.pallas import tpu as pltpu
from jax.sharding import Mesh
from jax.sharding import PartitionSpec as P

HEAD_DIM = 128
SWAP = [(0, 1), (1, 0)]


def exclusive_prefix(state, axis, size):
    total = state
    shift = 1
    while shift < size:
        pairs = [(i, i + shift) for i in range(size - shift)]
        total = total + lax.ppermute(total, axis, pairs)
        shift *= 2
    return total - state


def pair_order(own, other, place, axis):
    first = jnp.where(place == 0, own, other)
    second = jnp.where(place == 0, other, own)
    return jnp.concatenate([first, second], axis=axis)


def head_blocks(arrays, n_head, place):
    if n_head == 2:
        rows = arrays[0].shape[0]
        width = arrays[0].shape[1] // 2
        stacked = jnp.stack(arrays).reshape(len(arrays), rows, 2, width)
        own = lax.dynamic_index_in_dim(stacked, place, 2, False)
        sent = lax.dynamic_index_in_dim(stacked, 1 - place, 2, False)
        other = lax.ppermute(sent, "head", SWAP)
        block = pair_order(own, other, place, 1)
        return [block[i] for i in range(len(arrays))]
    return [
        lax.all_to_all(a, "head", split_axis=1, concat_axis=0, tiled=True) for a in arrays
    ]


def chip_cycle(devices):
    n = devices.shape[0]
    coords = [getattr(devices[j, 0, 0], "coords", None) for j in range(n)]
    if n < 4 or n > 16 or any(c is None for c in coords):
        return None

    def adjacent(a, b):
        return sum(abs(int(u) - int(v)) for u, v in zip(coords[a], coords[b])) == 1

    path = [0]

    def search():
        if len(path) == n:
            return adjacent(path[-1], path[0])
        for k in range(n):
            if k not in path and adjacent(path[-1], k):
                path.append(k)
                if search():
                    return True
                path.pop()
        return False

    return list(path) if search() else None


def ring_links(order):
    n = len(order)
    forward = [(order[i], order[(i + 1) % n]) for i in range(n)]
    backward = [(order[(i + 1) % n], order[i]) for i in range(n)]
    return forward, backward


def ring_step(ahead, behind, order, last=False):
    forward, backward = ring_links(order)
    if last:
        half_rows = ahead.shape[0] // 2
        return lax.ppermute(ahead[:half_rows], "chip", forward), lax.ppermute(
            behind[half_rows:], "chip", backward
        )
    return lax.ppermute(ahead, "chip", forward), lax.ppermute(behind, "chip", backward)


def within_block_part(query_heads, key_heads, value_heads):
    row_count = query_heads.shape[0]
    block_rows = min(512, row_count)
    parts_list = []
    for first_row in range(0, row_count, block_rows):
        last_row = min(first_row + block_rows, row_count)
        scores = jnp.einsum(
            "thd,shd->hts",
            query_heads[first_row:last_row],
            key_heads[:last_row],
            preferred_element_type=jnp.float32,
        )
        row_index = first_row + lax.broadcasted_iota(jnp.int32, (last_row - first_row, last_row), 0)
        col_index = lax.broadcasted_iota(jnp.int32, (last_row - first_row, last_row), 1)
        scores = jnp.where((col_index <= row_index)[None], scores, jnp.zeros_like(scores)).astype(
            jnp.bfloat16
        )
        parts_list.append(
            jnp.einsum(
                "hts,she->the", scores, value_heads[:last_row], preferred_element_type=jnp.float32
            )
        )
    return jnp.concatenate(parts_list, axis=0)


def normalize(query_heads, prefix, within_block, norm_gain):
    heads_dev = query_heads.shape[1]
    carried = jnp.einsum(
        "thd,hde->the", query_heads, prefix.astype(jnp.bfloat16), preferred_element_type=jnp.float32
    )
    attended = carried + within_block
    mean_square = jnp.mean(attended * attended, axis=2, keepdims=True)
    gain_heads = norm_gain.reshape(heads_dev, HEAD_DIM)
    normed = (attended * lax.rsqrt(mean_square + 1e-06) * gain_heads[None]).astype(jnp.bfloat16)
    return normed.reshape(query_heads.shape[0], heads_dev * HEAD_DIM)


def gather_head(normed, n_head, place):
    if n_head == 2:
        other = lax.ppermute(normed, "head", SWAP)
        return pair_order(normed, other, place, 1)
    return lax.all_gather(normed, "head", axis=1, tiled=True)


def chip_scan(kv_state, core, n_chip):
    partner_state = lax.ppermute(kv_state, "core", SWAP)
    chip_state = kv_state + partner_state
    half = kv_state.shape[0] // 2
    chip_half = lax.dynamic_slice_in_dim(chip_state, core * half, half, 0)
    return partner_state, chip_half


def chip_finish(chip_prefix_half, partner_state, core):
    other_half = lax.ppermute(chip_prefix_half, "core", SWAP)
    chip_prefix = pair_order(chip_prefix_half, other_half, core, 0)
    return chip_prefix + jnp.where(core == 1, partner_state, jnp.zeros_like(partner_state))


def split_heads(block, heads_dev):
    return block.reshape(block.shape[0], heads_dev, HEAD_DIM)


def project_blocks(normed, blocks, group=4):
    n = len(blocks)
    rows, cols = blocks[0].shape
    tokens = normed.shape[0]
    def kernel(normed_ref, *refs):
        block_refs = refs[:n]
        out_ref, weights, sems, acc = refs[n:]
        copies = [
            pltpu.make_async_copy(block_refs[i], weights.at[pl.ds(i * rows, rows), :], sems.at[i])
            for i in range(n)
        ]
        for c in copies:
            c.start()
        for g in range(0, n, group):
            last = min(g + group, n)
            for i in range(g, last):
                copies[i].wait()
            part = jnp.dot(
                normed_ref[:, g * rows:last * rows],
                weights[g * rows:last * rows, :],
                preferred_element_type=jnp.float32,
            )
            if g == 0:
                acc[...] = part
            else:
                acc[...] += part
        out_ref[...] = acc[...].astype(out_ref.dtype)
    return pl.pallas_call(
        kernel,
        out_shape=jax.ShapeDtypeStruct((tokens, cols), jnp.bfloat16),
        in_specs=[pl.BlockSpec(memory_space=pltpu.VMEM)] + [pl.BlockSpec(memory_space=pl.ANY)] * n,
        out_specs=pl.BlockSpec(memory_space=pltpu.VMEM),
        scratch_shapes=[
            pltpu.VMEM((n * rows, cols), blocks[0].dtype),
            pltpu.SemaphoreType.DMA((n,)),
            pltpu.VMEM((tokens, cols), jnp.float32),
        ],
    )(normed, *blocks)


def local_gather(queries, keys, values, out_weight, norm_gain, n_chip, n_head):
    heads_dev = norm_gain.shape[0] // HEAD_DIM
    core = lax.axis_index("core")
    place = lax.axis_index("head") if n_head == 2 else 0
    weight_own = lax.all_gather(out_weight, "chip", axis=0, tiled=True)
    query_block, key_block, value_block = head_blocks([queries, keys, values], n_head, place)
    query_heads, key_heads, value_heads = (
        split_heads(b, heads_dev) for b in (query_block, key_block, value_block)
    )
    kv_state = jnp.einsum(
        "thd,the->hde", key_heads, value_heads, preferred_element_type=jnp.float32
    )
    partner_state, chip_half = chip_scan(kv_state, core, n_chip)
    prefix = chip_finish(exclusive_prefix(chip_half, "chip", n_chip), partner_state, core)
    within_block = within_block_part(query_heads, key_heads, value_heads)
    normed = normalize(query_heads, prefix, within_block, norm_gain)
    gathered = gather_head(normed, n_head, place)
    row_count = gathered.shape[0]
    split = gathered.reshape(row_count, n_chip, 2, out_weight.shape[0])
    weight_own, split = lax.optimization_barrier((weight_own, split))
    weight_other = lax.ppermute(weight_own, "core", SWAP)
    normed_own = lax.dynamic_index_in_dim(split, core, 2, False).reshape(row_count, -1)
    normed_other = lax.dynamic_index_in_dim(split, 1 - core, 2, False).reshape(row_count, -1)
    outcome = jnp.dot(normed_own, weight_own, preferred_element_type=jnp.float32)
    outcome = outcome + jnp.dot(normed_other, weight_other, preferred_element_type=jnp.float32)
    return outcome.astype(jnp.bfloat16)


def local_ring(queries, keys, values, out_weight, norm_gain, n_chip, n_head, order):
    heads_dev = norm_gain.shape[0] // HEAD_DIM
    core = lax.axis_index("core")
    place = lax.axis_index("head")
    n_steps = n_chip // 2
    barrier = lax.optimization_barrier
    key_block, value_block = head_blocks([keys, values], n_head, place)
    ahead, behind = ring_step(out_weight, out_weight, order)
    ahead, behind, key_block, value_block = barrier((ahead, behind, key_block, value_block))
    got = [out_weight, ahead, behind]
    offsets = [0, 1, -1]
    (query_block,) = head_blocks([queries], n_head, place)
    ahead, behind = ring_step(ahead, behind, order, last=n_steps == 2)
    swapped = [lax.ppermute(w, "core", SWAP) for w in got]
    key_heads, value_heads = split_heads(key_block, heads_dev), split_heads(value_block, heads_dev)
    kv_state = jnp.einsum(
        "thd,the->hde", key_heads, value_heads, preferred_element_type=jnp.float32
    )
    partner_state, chip_half = chip_scan(kv_state, core, n_chip)
    ahead, behind, swapped, partner_state, chip_half = barrier(
        (ahead, behind, swapped, partner_state, chip_half)
    )
    if n_steps == 2:
        got.append(jnp.concatenate([ahead, behind], 0))
        offsets.append(2)
    else:
        got += [ahead, behind]
        offsets += [2, -2]
    chip_prefix_half = exclusive_prefix(chip_half, "chip", n_chip)
    query_heads = split_heads(query_block, heads_dev)
    within_block = within_block_part(query_heads, key_heads, value_heads)
    swapped += [lax.ppermute(w, "core", SWAP) for w in got[len(swapped):]]
    chip_prefix_half, within_block, swapped = barrier((chip_prefix_half, within_block, swapped))
    for step in range(3, n_steps + 1):
        ahead, behind = ring_step(ahead, behind, order, last=step == n_steps)
        if step == n_steps:
            got.append(jnp.concatenate([ahead, behind], 0))
            offsets.append(step)
        else:
            got += [ahead, behind]
            offsets += [step, -step]
    swapped += [lax.ppermute(w, "core", SWAP) for w in got[len(swapped):]]
    prefix = chip_finish(chip_prefix_half, partner_state, core)
    normed = normalize(query_heads, prefix, within_block, norm_gain)
    gathered = gather_head(normed, n_head, place)
    row_count = gathered.shape[0]
    split = gathered.reshape(row_count, n_chip, 2, out_weight.shape[0])
    ring_place = jnp.asarray([order.index(j) for j in range(n_chip)], jnp.int32)[lax.axis_index("chip")]
    sources = jnp.asarray(order, jnp.int32)[(ring_place - jnp.asarray(offsets, jnp.int32)) % n_chip]
    by_offset = jnp.take(split, sources, axis=1)
    by_offset = jnp.where(core == 0, by_offset, by_offset[:, :, ::-1]).reshape(row_count, -1)
    return project_blocks(by_offset, [w for pair in zip(got, swapped) for w in pair])


def solution(mesh):
    n_seq = mesh.shape["seq"]
    n_head = mesh.shape["head"]
    fine = Mesh(mesh.devices.reshape(n_seq // 2, 2, n_head), ("chip", "core", "head"))
    rows = ("chip", "core", "head")
    order = chip_cycle(fine.devices) if n_head == 2 else None
    if order is None:
        body = functools.partial(local_gather, n_chip=n_seq // 2, n_head=n_head)
    else:
        body = functools.partial(local_ring, n_chip=n_seq // 2, n_head=n_head, order=order)
    return jax.shard_map(
        body,
        mesh=fine,
        in_specs=(
            P(rows, None),
            P(rows, None),
            P(rows, None),
            P(("chip", "core"), "head"),
            P("head"),
        ),
        out_specs=P(("chip", "core"), "head"),
        check_vma=False,
    )
```

```python
import functools

import jax
import jax.numpy as jnp
from jax import lax
from jax.experimental import pallas as pl
from jax.experimental.pallas import tpu as pltpu
from jax.sharding import Mesh
from jax.sharding import PartitionSpec as P

HEAD_DIM = 128
SWAP = [(0, 1), (1, 0)]


def exclusive_prefix(state, axis, size):
    total = state
    shift = 1
    while shift < size:
        pairs = [(i, i + shift) for i in range(size - shift)]
        total = total + lax.ppermute(total, axis, pairs)
        shift *= 2
    return total - state


def pair_order(own, other, place, axis):
    first = jnp.where(place == 0, own, other)
    second = jnp.where(place == 0, other, own)
    return jnp.concatenate([first, second], axis=axis)


def head_blocks(arrays, n_head, place):
    if n_head == 2:
        rows = arrays[0].shape[0]
        width = arrays[0].shape[1] // 2
        stacked = jnp.stack(arrays).reshape(len(arrays), rows, 2, width)
        own = lax.dynamic_index_in_dim(stacked, place, 2, False)
        sent = lax.dynamic_index_in_dim(stacked, 1 - place, 2, False)
        other = lax.ppermute(sent, "head", SWAP)
        block = pair_order(own, other, place, 1)
        return [block[i] for i in range(len(arrays))]
    return [
        lax.all_to_all(a, "head", split_axis=1, concat_axis=0, tiled=True) for a in arrays
    ]


def chip_cycle(devices):
    n = devices.shape[0]
    coords = [getattr(devices[j, 0, 0], "coords", None) for j in range(n)]
    if n < 4 or n > 16 or any(c is None for c in coords):
        return None

    def adjacent(a, b):
        return sum(abs(int(u) - int(v)) for u, v in zip(coords[a], coords[b])) == 1

    path = [0]

    def search():
        if len(path) == n:
            return adjacent(path[-1], path[0])
        for k in range(n):
            if k not in path and adjacent(path[-1], k):
                path.append(k)
                if search():
                    return True
                path.pop()
        return False

    return list(path) if search() else None


def ring_links(order):
    n = len(order)
    forward = [(order[i], order[(i + 1) % n]) for i in range(n)]
    backward = [(order[(i + 1) % n], order[i]) for i in range(n)]
    return forward, backward


def ring_step(ahead, behind, order, last=False):
    forward, backward = ring_links(order)
    if last:
        half_rows = ahead.shape[0] // 2
        return lax.ppermute(ahead[:half_rows], "chip", forward), lax.ppermute(
            behind[half_rows:], "chip", backward
        )
    return lax.ppermute(ahead, "chip", forward), lax.ppermute(behind, "chip", backward)


def within_block_part(query_heads, key_heads, value_heads):
    row_count = query_heads.shape[0]
    block_rows = min(512, row_count)
    parts_list = []
    for first_row in range(0, row_count, block_rows):
        last_row = min(first_row + block_rows, row_count)
        scores = jnp.einsum(
            "thd,shd->hts",
            query_heads[first_row:last_row],
            key_heads[:last_row],
            preferred_element_type=jnp.float32,
        )
        row_index = first_row + lax.broadcasted_iota(jnp.int32, (last_row - first_row, last_row), 0)
        col_index = lax.broadcasted_iota(jnp.int32, (last_row - first_row, last_row), 1)
        scores = jnp.where((col_index <= row_index)[None], scores, jnp.zeros_like(scores)).astype(
            jnp.bfloat16
        )
        parts_list.append(
            jnp.einsum(
                "hts,she->the", scores, value_heads[:last_row], preferred_element_type=jnp.float32
            )
        )
    return jnp.concatenate(parts_list, axis=0)


def normalize(query_heads, prefix, within_block, norm_gain):
    heads_dev = query_heads.shape[1]
    carried = jnp.einsum(
        "thd,hde->the", query_heads, prefix.astype(jnp.bfloat16), preferred_element_type=jnp.float32
    )
    attended = carried + within_block
    mean_square = jnp.mean(attended * attended, axis=2, keepdims=True)
    gain_heads = norm_gain.reshape(heads_dev, HEAD_DIM)
    normed = (attended * lax.rsqrt(mean_square + 1e-06) * gain_heads[None]).astype(jnp.bfloat16)
    return normed.reshape(query_heads.shape[0], heads_dev * HEAD_DIM)


def gather_head(normed, n_head, place):
    if n_head == 2:
        other = lax.ppermute(normed, "head", SWAP)
        return pair_order(normed, other, place, 1)
    return lax.all_gather(normed, "head", axis=1, tiled=True)


def chip_scan(kv_state, core, n_chip):
    partner_state = lax.ppermute(kv_state, "core", SWAP)
    chip_state = kv_state + partner_state
    half = kv_state.shape[0] // 2
    chip_half = lax.dynamic_slice_in_dim(chip_state, core * half, half, 0)
    return partner_state, chip_half


def chip_finish(chip_prefix_half, partner_state, core):
    other_half = lax.ppermute(chip_prefix_half, "core", SWAP)
    chip_prefix = pair_order(chip_prefix_half, other_half, core, 0)
    return chip_prefix + jnp.where(core == 1, partner_state, jnp.zeros_like(partner_state))


def split_heads(block, heads_dev):
    return block.reshape(block.shape[0], heads_dev, HEAD_DIM)


def project_blocks(normed, blocks, group=4):
    n = len(blocks)
    rows, cols = blocks[0].shape
    tokens = normed.shape[0]
    def kernel(normed_ref, *refs):
        block_refs = refs[:n]
        out_ref, weights, sems, acc = refs[n:]
        copies = [
            pltpu.make_async_copy(block_refs[i], weights.at[pl.ds(i * rows, rows), :], sems.at[i])
            for i in range(n)
        ]
        for c in copies:
            c.start()
        for g in range(0, n, group):
            last = min(g + group, n)
            for i in range(g, last):
                copies[i].wait()
            part = jnp.dot(
                normed_ref[:, g * rows:last * rows],
                weights[g * rows:last * rows, :],
                preferred_element_type=jnp.float32,
            )
            if g == 0:
                acc[...] = part
            else:
                acc[...] += part
        out_ref[...] = acc[...].astype(out_ref.dtype)
    return pl.pallas_call(
        kernel,
        out_shape=jax.ShapeDtypeStruct((tokens, cols), jnp.bfloat16),
        in_specs=[pl.BlockSpec(memory_space=pltpu.VMEM)] + [pl.BlockSpec(memory_space=pl.ANY)] * n,
        out_specs=pl.BlockSpec(memory_space=pltpu.VMEM),
        scratch_shapes=[
            pltpu.VMEM((n * rows, cols), blocks[0].dtype),
            pltpu.SemaphoreType.DMA((n,)),
            pltpu.VMEM((tokens, cols), jnp.float32),
        ],
    )(normed, *blocks)


def local_gather(queries, keys, values, out_weight, norm_gain, n_chip, n_head):
    heads_dev = norm_gain.shape[0] // HEAD_DIM
    core = lax.axis_index("core")
    place = lax.axis_index("head") if n_head == 2 else 0
    weight_own = lax.all_gather(out_weight, "chip", axis=0, tiled=True)
    query_block, key_block, value_block = head_blocks([queries, keys, values], n_head, place)
    query_heads, key_heads, value_heads = (
        split_heads(b, heads_dev) for b in (query_block, key_block, value_block)
    )
    kv_state = jnp.einsum(
        "thd,the->hde", key_heads, value_heads, preferred_element_type=jnp.float32
    )
    partner_state, chip_half = chip_scan(kv_state, core, n_chip)
    prefix = chip_finish(exclusive_prefix(chip_half, "chip", n_chip), partner_state, core)
    within_block = within_block_part(query_heads, key_heads, value_heads)
    normed = normalize(query_heads, prefix, within_block, norm_gain)
    gathered = gather_head(normed, n_head, place)
    row_count = gathered.shape[0]
    split = gathered.reshape(row_count, n_chip, 2, out_weight.shape[0])
    weight_own, split = lax.optimization_barrier((weight_own, split))
    weight_other = lax.ppermute(weight_own, "core", SWAP)
    normed_own = lax.dynamic_index_in_dim(split, core, 2, False).reshape(row_count, -1)
    normed_other = lax.dynamic_index_in_dim(split, 1 - core, 2, False).reshape(row_count, -1)
    outcome = jnp.dot(normed_own, weight_own, preferred_element_type=jnp.float32)
    outcome = outcome + jnp.dot(normed_other, weight_other, preferred_element_type=jnp.float32)
    return outcome.astype(jnp.bfloat16)


def local_ring(queries, keys, values, out_weight, norm_gain, n_chip, n_head, order):
    heads_dev = norm_gain.shape[0] // HEAD_DIM
    core = lax.axis_index("core")
    place = lax.axis_index("head")
    n_steps = n_chip // 2
    barrier = lax.optimization_barrier
    key_block, value_block = head_blocks([keys, values], n_head, place)
    ahead, behind = ring_step(out_weight, out_weight, order)
    ahead, behind, key_block, value_block = barrier((ahead, behind, key_block, value_block))
    got = [out_weight, ahead, behind]
    offsets = [0, 1, -1]
    (query_block,) = head_blocks([queries], n_head, place)
    swapped = [lax.ppermute(w, "core", SWAP) for w in got]
    key_heads, value_heads = split_heads(key_block, heads_dev), split_heads(value_block, heads_dev)
    kv_state = jnp.einsum(
        "thd,the->hde", key_heads, value_heads, preferred_element_type=jnp.float32
    )
    partner_state, chip_half = chip_scan(kv_state, core, n_chip)
    chip_prefix_half = exclusive_prefix(chip_half, "chip", n_chip)
    query_heads = split_heads(query_block, heads_dev)
    within_block = within_block_part(query_heads, key_heads, value_heads)
    swapped += [lax.ppermute(w, "core", SWAP) for w in got[len(swapped):]]
    chip_prefix_half, within_block, swapped = barrier((chip_prefix_half, within_block, swapped))
    for step in range(2, n_steps + 1):
        ahead, behind = ring_step(ahead, behind, order, last=step == n_steps)
        if step == n_steps:
            got.append(jnp.concatenate([ahead, behind], 0))
            offsets.append(step)
        else:
            got += [ahead, behind]
            offsets += [step, -step]
    swapped += [lax.ppermute(w, "core", SWAP) for w in got[len(swapped):]]
    prefix = chip_finish(chip_prefix_half, partner_state, core)
    normed = normalize(query_heads, prefix, within_block, norm_gain)
    gathered = gather_head(normed, n_head, place)
    row_count = gathered.shape[0]
    split = gathered.reshape(row_count, n_chip, 2, out_weight.shape[0])
    ring_place = jnp.asarray([order.index(j) for j in range(n_chip)], jnp.int32)[lax.axis_index("chip")]
    sources = jnp.asarray(order, jnp.int32)[(ring_place - jnp.asarray(offsets, jnp.int32)) % n_chip]
    by_offset = jnp.take(split, sources, axis=1)
    by_offset = jnp.where(core == 0, by_offset, by_offset[:, :, ::-1]).reshape(row_count, -1)
    return project_blocks(by_offset, [w for pair in zip(got, swapped) for w in pair])


def solution(mesh):
    n_seq = mesh.shape["seq"]
    n_head = mesh.shape["head"]
    fine = Mesh(mesh.devices.reshape(n_seq // 2, 2, n_head), ("chip", "core", "head"))
    rows = ("chip", "core", "head")
    order = chip_cycle(fine.devices) if n_head == 2 else None
    if order is None:
        body = functools.partial(local_gather, n_chip=n_seq // 2, n_head=n_head)
    else:
        body = functools.partial(local_ring, n_chip=n_seq // 2, n_head=n_head, order=order)
    return jax.shard_map(
        body,
        mesh=fine,
        in_specs=(
            P(rows, None),
            P(rows, None),
            P(rows, None),
            P(("chip", "core"), "head"),
            P("head"),
        ),
        out_specs=P(("chip", "core"), "head"),
        check_vma=False,
    )
```

```python
import functools

import jax
import jax.numpy as jnp
from jax import lax
from jax.experimental import pallas as pl
from jax.experimental.pallas import tpu as pltpu
from jax.sharding import Mesh
from jax.sharding import PartitionSpec as P

HEAD_DIM = 128
SWAP = [(0, 1), (1, 0)]


def exclusive_prefix(state, axis, size):
    total = state
    shift = 1
    while shift < size:
        pairs = [(i, i + shift) for i in range(size - shift)]
        total = total + lax.ppermute(total, axis, pairs)
        shift *= 2
    return total - state


def pair_order(own, other, place, axis):
    first = jnp.where(place == 0, own, other)
    second = jnp.where(place == 0, other, own)
    return jnp.concatenate([first, second], axis=axis)


def head_blocks(arrays, n_head, place):
    if n_head == 2:
        rows = arrays[0].shape[0]
        width = arrays[0].shape[1] // 2
        stacked = jnp.stack(arrays).reshape(len(arrays), rows, 2, width)
        own = lax.dynamic_index_in_dim(stacked, place, 2, False)
        sent = lax.dynamic_index_in_dim(stacked, 1 - place, 2, False)
        other = lax.ppermute(sent, "head", SWAP)
        block = pair_order(own, other, place, 1)
        return [block[i] for i in range(len(arrays))]
    return [
        lax.all_to_all(a, "head", split_axis=1, concat_axis=0, tiled=True) for a in arrays
    ]


def chip_cycle(devices):
    n = devices.shape[0]
    coords = [getattr(devices[j, 0, 0], "coords", None) for j in range(n)]
    if n < 4 or n > 16 or any(c is None for c in coords):
        return None

    def adjacent(a, b):
        return sum(abs(int(u) - int(v)) for u, v in zip(coords[a], coords[b])) == 1

    path = [0]

    def search():
        if len(path) == n:
            return adjacent(path[-1], path[0])
        for k in range(n):
            if k not in path and adjacent(path[-1], k):
                path.append(k)
                if search():
                    return True
                path.pop()
        return False

    return list(path) if search() else None


def ring_links(order):
    n = len(order)
    forward = [(order[i], order[(i + 1) % n]) for i in range(n)]
    backward = [(order[(i + 1) % n], order[i]) for i in range(n)]
    return forward, backward


def ring_step(ahead, behind, order, last=False):
    forward, backward = ring_links(order)
    if last:
        half_rows = ahead.shape[0] // 2
        return lax.ppermute(ahead[:half_rows], "chip", forward), lax.ppermute(
            behind[half_rows:], "chip", backward
        )
    return lax.ppermute(ahead, "chip", forward), lax.ppermute(behind, "chip", backward)


def within_block_part(query_heads, key_heads, value_heads):
    row_count = query_heads.shape[0]
    block_rows = min(512, row_count)
    parts_list = []
    for first_row in range(0, row_count, block_rows):
        last_row = min(first_row + block_rows, row_count)
        scores = jnp.einsum(
            "thd,shd->hts",
            query_heads[first_row:last_row],
            key_heads[:last_row],
            preferred_element_type=jnp.float32,
        )
        row_index = first_row + lax.broadcasted_iota(jnp.int32, (last_row - first_row, last_row), 0)
        col_index = lax.broadcasted_iota(jnp.int32, (last_row - first_row, last_row), 1)
        scores = jnp.where((col_index <= row_index)[None], scores, jnp.zeros_like(scores)).astype(
            jnp.bfloat16
        )
        parts_list.append(
            jnp.einsum(
                "hts,she->the", scores, value_heads[:last_row], preferred_element_type=jnp.float32
            )
        )
    return jnp.concatenate(parts_list, axis=0)


def normalize(query_heads, prefix, within_block, norm_gain):
    heads_dev = query_heads.shape[1]
    carried = jnp.einsum(
        "thd,hde->the", query_heads, prefix.astype(jnp.bfloat16), preferred_element_type=jnp.float32
    )
    attended = carried + within_block
    mean_square = jnp.mean(attended * attended, axis=2, keepdims=True)
    gain_heads = norm_gain.reshape(heads_dev, HEAD_DIM)
    normed = (attended * lax.rsqrt(mean_square + 1e-06) * gain_heads[None]).astype(jnp.bfloat16)
    return normed.reshape(query_heads.shape[0], heads_dev * HEAD_DIM)


def gather_head(normed, n_head, place):
    if n_head == 2:
        other = lax.ppermute(normed, "head", SWAP)
        return pair_order(normed, other, place, 1)
    return lax.all_gather(normed, "head", axis=1, tiled=True)


def chip_scan(kv_state, core, n_chip):
    partner_state = lax.ppermute(kv_state, "core", SWAP)
    chip_state = kv_state + partner_state
    half = kv_state.shape[0] // 2
    chip_half = lax.dynamic_slice_in_dim(chip_state, core * half, half, 0)
    return partner_state, chip_half


def chip_finish(chip_prefix_half, partner_state, core):
    other_half = lax.ppermute(chip_prefix_half, "core", SWAP)
    chip_prefix = pair_order(chip_prefix_half, other_half, core, 0)
    return chip_prefix + jnp.where(core == 1, partner_state, jnp.zeros_like(partner_state))


def split_heads(block, heads_dev):
    return block.reshape(block.shape[0], heads_dev, HEAD_DIM)


def project_blocks(normed, blocks, group=4):
    n = len(blocks)
    rows, cols = blocks[0].shape
    tokens = normed.shape[0]
    def kernel(normed_ref, *refs):
        block_refs = refs[:n]
        out_ref, weights, sems, acc = refs[n:]
        copies = [
            pltpu.make_async_copy(block_refs[i], weights.at[pl.ds(i * rows, rows), :], sems.at[i])
            for i in range(n)
        ]
        for c in copies:
            c.start()
        for g in range(0, n, group):
            last = min(g + group, n)
            for i in range(g, last):
                copies[i].wait()
            part = jnp.dot(
                normed_ref[:, g * rows:last * rows],
                weights[g * rows:last * rows, :],
                preferred_element_type=jnp.float32,
            )
            if g == 0:
                acc[...] = part
            else:
                acc[...] += part
        out_ref[...] = acc[...].astype(out_ref.dtype)
    return pl.pallas_call(
        kernel,
        out_shape=jax.ShapeDtypeStruct((tokens, cols), jnp.bfloat16),
        in_specs=[pl.BlockSpec(memory_space=pltpu.VMEM)] + [pl.BlockSpec(memory_space=pl.ANY)] * n,
        out_specs=pl.BlockSpec(memory_space=pltpu.VMEM),
        scratch_shapes=[
            pltpu.VMEM((n * rows, cols), blocks[0].dtype),
            pltpu.SemaphoreType.DMA((n,)),
            pltpu.VMEM((tokens, cols), jnp.float32),
        ],
    )(normed, *blocks)


def local_gather(queries, keys, values, out_weight, norm_gain, n_chip, n_head):
    heads_dev = norm_gain.shape[0] // HEAD_DIM
    core = lax.axis_index("core")
    place = lax.axis_index("head") if n_head == 2 else 0
    weight_own = lax.all_gather(out_weight, "chip", axis=0, tiled=True)
    query_block, key_block, value_block = head_blocks([queries, keys, values], n_head, place)
    query_heads, key_heads, value_heads = (
        split_heads(b, heads_dev) for b in (query_block, key_block, value_block)
    )
    kv_state = jnp.einsum(
        "thd,the->hde", key_heads, value_heads, preferred_element_type=jnp.float32
    )
    partner_state, chip_half = chip_scan(kv_state, core, n_chip)
    prefix = chip_finish(exclusive_prefix(chip_half, "chip", n_chip), partner_state, core)
    within_block = within_block_part(query_heads, key_heads, value_heads)
    normed = normalize(query_heads, prefix, within_block, norm_gain)
    gathered = gather_head(normed, n_head, place)
    row_count = gathered.shape[0]
    split = gathered.reshape(row_count, n_chip, 2, out_weight.shape[0])
    weight_own, split = lax.optimization_barrier((weight_own, split))
    weight_other = lax.ppermute(weight_own, "core", SWAP)
    normed_own = lax.dynamic_index_in_dim(split, core, 2, False).reshape(row_count, -1)
    normed_other = lax.dynamic_index_in_dim(split, 1 - core, 2, False).reshape(row_count, -1)
    outcome = jnp.dot(normed_own, weight_own, preferred_element_type=jnp.float32)
    outcome = outcome + jnp.dot(normed_other, weight_other, preferred_element_type=jnp.float32)
    return outcome.astype(jnp.bfloat16)


def local_ring(queries, keys, values, out_weight, norm_gain, n_chip, n_head, order):
    heads_dev = norm_gain.shape[0] // HEAD_DIM
    core = lax.axis_index("core")
    place = lax.axis_index("head")
    n_steps = n_chip // 2
    barrier = lax.optimization_barrier
    key_block, value_block = head_blocks([keys, values], n_head, place)
    ahead, behind = ring_step(out_weight, out_weight, order)
    ahead, behind, key_block, value_block = barrier((ahead, behind, key_block, value_block))
    got = [out_weight, ahead, behind]
    offsets = [0, 1, -1]
    (query_block,) = head_blocks([queries], n_head, place)
    swapped = [lax.ppermute(w, "core", SWAP) for w in got]
    key_heads, value_heads = split_heads(key_block, heads_dev), split_heads(value_block, heads_dev)
    kv_state = jnp.einsum(
        "thd,the->hde", key_heads, value_heads, preferred_element_type=jnp.float32
    )
    partner_state, chip_half = chip_scan(kv_state, core, n_chip)
    chip_prefix_half = exclusive_prefix(chip_half, "chip", n_chip)
    query_heads = split_heads(query_block, heads_dev)
    within_block = within_block_part(query_heads, key_heads, value_heads)
    ahead, behind = ring_step(ahead, behind, order, last=n_steps == 2)
    chip_prefix_half, within_block, swapped, ahead, behind = barrier(
        (chip_prefix_half, within_block, swapped, ahead, behind)
    )
    if n_steps == 2:
        got.append(jnp.concatenate([ahead, behind], 0))
        offsets.append(2)
    else:
        got += [ahead, behind]
        offsets += [2, -2]
    for step in range(3, n_steps + 1):
        ahead, behind = ring_step(ahead, behind, order, last=step == n_steps)
        if step == n_steps:
            got.append(jnp.concatenate([ahead, behind], 0))
            offsets.append(step)
        else:
            got += [ahead, behind]
            offsets += [step, -step]
    swapped += [lax.ppermute(w, "core", SWAP) for w in got[len(swapped):]]
    prefix = chip_finish(chip_prefix_half, partner_state, core)
    normed = normalize(query_heads, prefix, within_block, norm_gain)
    gathered = gather_head(normed, n_head, place)
    row_count = gathered.shape[0]
    split = gathered.reshape(row_count, n_chip, 2, out_weight.shape[0])
    ring_place = jnp.asarray([order.index(j) for j in range(n_chip)], jnp.int32)[lax.axis_index("chip")]
    sources = jnp.asarray(order, jnp.int32)[(ring_place - jnp.asarray(offsets, jnp.int32)) % n_chip]
    by_offset = jnp.take(split, sources, axis=1)
    by_offset = jnp.where(core == 0, by_offset, by_offset[:, :, ::-1]).reshape(row_count, -1)
    return project_blocks(by_offset, [w for pair in zip(got, swapped) for w in pair])


def solution(mesh):
    n_seq = mesh.shape["seq"]
    n_head = mesh.shape["head"]
    fine = Mesh(mesh.devices.reshape(n_seq // 2, 2, n_head), ("chip", "core", "head"))
    rows = ("chip", "core", "head")
    order = chip_cycle(fine.devices) if n_head == 2 else None
    if order is None:
        body = functools.partial(local_gather, n_chip=n_seq // 2, n_head=n_head)
    else:
        body = functools.partial(local_ring, n_chip=n_seq // 2, n_head=n_head, order=order)
    return jax.shard_map(
        body,
        mesh=fine,
        in_specs=(
            P(rows, None),
            P(rows, None),
            P(rows, None),
            P(("chip", "core"), "head"),
            P("head"),
        ),
        out_specs=P(("chip", "core"), "head"),
        check_vma=False,
    )
```

```python
import functools

import jax
import jax.numpy as jnp
from jax import lax
from jax.experimental import pallas as pl
from jax.experimental.pallas import tpu as pltpu
from jax.sharding import Mesh
from jax.sharding import PartitionSpec as P

HEAD_DIM = 128
SWAP = [(0, 1), (1, 0)]


def exclusive_prefix(state, axis, size):
    total = state
    shift = 1
    while shift < size:
        pairs = [(i, i + shift) for i in range(size - shift)]
        total = total + lax.ppermute(total, axis, pairs)
        shift *= 2
    return total - state


def pair_order(own, other, place, axis):
    first = jnp.where(place == 0, own, other)
    second = jnp.where(place == 0, other, own)
    return jnp.concatenate([first, second], axis=axis)


def head_blocks(arrays, n_head, place):
    if n_head == 2:
        rows = arrays[0].shape[0]
        width = arrays[0].shape[1] // 2
        stacked = jnp.stack(arrays).reshape(len(arrays), rows, 2, width)
        own = lax.dynamic_index_in_dim(stacked, place, 2, False)
        sent = lax.dynamic_index_in_dim(stacked, 1 - place, 2, False)
        other = lax.ppermute(sent, "head", SWAP)
        block = pair_order(own, other, place, 1)
        return [block[i] for i in range(len(arrays))]
    return [
        lax.all_to_all(a, "head", split_axis=1, concat_axis=0, tiled=True) for a in arrays
    ]


def chip_cycle(devices):
    n = devices.shape[0]
    coords = [getattr(devices[j, 0, 0], "coords", None) for j in range(n)]
    if n < 4 or n > 16 or any(c is None for c in coords):
        return None

    def adjacent(a, b):
        return sum(abs(int(u) - int(v)) for u, v in zip(coords[a], coords[b])) == 1

    path = [0]

    def search():
        if len(path) == n:
            return adjacent(path[-1], path[0])
        for k in range(n):
            if k not in path and adjacent(path[-1], k):
                path.append(k)
                if search():
                    return True
                path.pop()
        return False

    return list(path) if search() else None


def ring_links(order):
    n = len(order)
    forward = [(order[i], order[(i + 1) % n]) for i in range(n)]
    backward = [(order[(i + 1) % n], order[i]) for i in range(n)]
    return forward, backward


def ring_step(ahead, behind, order, last=False):
    forward, backward = ring_links(order)
    if last:
        half_rows = ahead.shape[0] // 2
        return lax.ppermute(ahead[:half_rows], "chip", forward), lax.ppermute(
            behind[half_rows:], "chip", backward
        )
    return lax.ppermute(ahead, "chip", forward), lax.ppermute(behind, "chip", backward)


def within_block_part(query_heads, key_heads, value_heads):
    row_count = query_heads.shape[0]
    block_rows = min(512, row_count)
    parts_list = []
    for first_row in range(0, row_count, block_rows):
        last_row = min(first_row + block_rows, row_count)
        scores = jnp.einsum(
            "thd,shd->hts",
            query_heads[first_row:last_row],
            key_heads[:last_row],
            preferred_element_type=jnp.float32,
        )
        row_index = first_row + lax.broadcasted_iota(jnp.int32, (last_row - first_row, last_row), 0)
        col_index = lax.broadcasted_iota(jnp.int32, (last_row - first_row, last_row), 1)
        scores = jnp.where((col_index <= row_index)[None], scores, jnp.zeros_like(scores)).astype(
            jnp.bfloat16
        )
        parts_list.append(
            jnp.einsum(
                "hts,she->the", scores, value_heads[:last_row], preferred_element_type=jnp.float32
            )
        )
    return jnp.concatenate(parts_list, axis=0)


def normalize(query_heads, prefix, within_block, norm_gain):
    heads_dev = query_heads.shape[1]
    carried = jnp.einsum(
        "thd,hde->the", query_heads, prefix.astype(jnp.bfloat16), preferred_element_type=jnp.float32
    )
    attended = carried + within_block
    mean_square = jnp.mean(attended * attended, axis=2, keepdims=True)
    gain_heads = norm_gain.reshape(heads_dev, HEAD_DIM)
    normed = (attended * lax.rsqrt(mean_square + 1e-06) * gain_heads[None]).astype(jnp.bfloat16)
    return normed.reshape(query_heads.shape[0], heads_dev * HEAD_DIM)


def gather_head(normed, n_head, place):
    if n_head == 2:
        other = lax.ppermute(normed, "head", SWAP)
        return pair_order(normed, other, place, 1)
    return lax.all_gather(normed, "head", axis=1, tiled=True)


def chip_scan(kv_state, core, n_chip):
    partner_state = lax.ppermute(kv_state, "core", SWAP)
    chip_state = kv_state + partner_state
    half = kv_state.shape[0] // 2
    chip_half = lax.dynamic_slice_in_dim(chip_state, core * half, half, 0)
    return partner_state, chip_half


def chip_finish(chip_prefix_half, partner_state, core):
    other_half = lax.ppermute(chip_prefix_half, "core", SWAP)
    chip_prefix = pair_order(chip_prefix_half, other_half, core, 0)
    return chip_prefix + jnp.where(core == 1, partner_state, jnp.zeros_like(partner_state))


def split_heads(block, heads_dev):
    return block.reshape(block.shape[0], heads_dev, HEAD_DIM)


def project_blocks(normed, starts, blocks, group=4):
    n = len(blocks)
    rows, cols = blocks[0].shape
    tokens = normed.shape[0]

    def kernel(starts_ref, normed_ref, *refs):
        block_refs = refs[:n]
        out_ref, features, weights, sems, acc = refs[n:]
        copies = []
        for i in range(n):
            start = pl.multiple_of(starts_ref[i], rows)
            copies.append(
                (
                    pltpu.make_async_copy(
                        normed_ref.at[:, pl.ds(start, rows)],
                        features.at[:, pl.ds(i * rows, rows)],
                        sems.at[0, i],
                    ),
                    pltpu.make_async_copy(
                        block_refs[i], weights.at[pl.ds(i * rows, rows), :], sems.at[1, i]
                    ),
                )
            )
        for pair in copies:
            for c in pair:
                c.start()
        for g in range(0, n, group):
            last = min(g + group, n)
            for i in range(g, last):
                for c in copies[i]:
                    c.wait()
            part = jnp.dot(
                features[:, g * rows:last * rows],
                weights[g * rows:last * rows, :],
                preferred_element_type=jnp.float32,
            )
            if g == 0:
                acc[...] = part
            else:
                acc[...] += part
        out_ref[...] = acc[...].astype(out_ref.dtype)

    return pl.pallas_call(
        kernel,
        out_shape=jax.ShapeDtypeStruct((tokens, cols), jnp.bfloat16),
        in_specs=[pl.BlockSpec(memory_space=pltpu.SMEM), pl.BlockSpec(memory_space=pl.ANY)]
        + [pl.BlockSpec(memory_space=pl.ANY)] * n,
        out_specs=pl.BlockSpec(memory_space=pltpu.VMEM),
        scratch_shapes=[
            pltpu.VMEM((tokens, n * rows), normed.dtype),
            pltpu.VMEM((n * rows, cols), blocks[0].dtype),
            pltpu.SemaphoreType.DMA((2, n)),
            pltpu.VMEM((tokens, cols), jnp.float32),
        ],
    )(starts, normed, *blocks)


def local_gather(queries, keys, values, out_weight, norm_gain, n_chip, n_head):
    heads_dev = norm_gain.shape[0] // HEAD_DIM
    core = lax.axis_index("core")
    place = lax.axis_index("head") if n_head == 2 else 0
    weight_own = lax.all_gather(out_weight, "chip", axis=0, tiled=True)
    query_block, key_block, value_block = head_blocks([queries, keys, values], n_head, place)
    query_heads, key_heads, value_heads = (
        split_heads(b, heads_dev) for b in (query_block, key_block, value_block)
    )
    kv_state = jnp.einsum(
        "thd,the->hde", key_heads, value_heads, preferred_element_type=jnp.float32
    )
    partner_state, chip_half = chip_scan(kv_state, core, n_chip)
    prefix = chip_finish(exclusive_prefix(chip_half, "chip", n_chip), partner_state, core)
    within_block = within_block_part(query_heads, key_heads, value_heads)
    normed = normalize(query_heads, prefix, within_block, norm_gain)
    gathered = gather_head(normed, n_head, place)
    row_count = gathered.shape[0]
    split = gathered.reshape(row_count, n_chip, 2, out_weight.shape[0])
    weight_own, split = lax.optimization_barrier((weight_own, split))
    weight_other = lax.ppermute(weight_own, "core", SWAP)
    normed_own = lax.dynamic_index_in_dim(split, core, 2, False).reshape(row_count, -1)
    normed_other = lax.dynamic_index_in_dim(split, 1 - core, 2, False).reshape(row_count, -1)
    outcome = jnp.dot(normed_own, weight_own, preferred_element_type=jnp.float32)
    outcome = outcome + jnp.dot(normed_other, weight_other, preferred_element_type=jnp.float32)
    return outcome.astype(jnp.bfloat16)


def local_ring(queries, keys, values, out_weight, norm_gain, n_chip, n_head, order):
    heads_dev = norm_gain.shape[0] // HEAD_DIM
    core = lax.axis_index("core")
    place = lax.axis_index("head")
    n_steps = n_chip // 2
    barrier = lax.optimization_barrier
    key_block, value_block = head_blocks([keys, values], n_head, place)
    ahead, behind = ring_step(out_weight, out_weight, order)
    ahead, behind, key_block, value_block = barrier((ahead, behind, key_block, value_block))
    got = [out_weight, ahead, behind]
    offsets = [0, 1, -1]
    (query_block,) = head_blocks([queries], n_head, place)
    swapped = [lax.ppermute(w, "core", SWAP) for w in got]
    key_heads, value_heads = split_heads(key_block, heads_dev), split_heads(value_block, heads_dev)
    kv_state = jnp.einsum(
        "thd,the->hde", key_heads, value_heads, preferred_element_type=jnp.float32
    )
    partner_state, chip_half = chip_scan(kv_state, core, n_chip)
    chip_prefix_half = exclusive_prefix(chip_half, "chip", n_chip)
    query_heads = split_heads(query_block, heads_dev)
    within_block = within_block_part(query_heads, key_heads, value_heads)
    swapped += [lax.ppermute(w, "core", SWAP) for w in got[len(swapped):]]
    chip_prefix_half, within_block, swapped = barrier((chip_prefix_half, within_block, swapped))
    for step in range(2, n_steps + 1):
        ahead, behind = ring_step(ahead, behind, order, last=step == n_steps)
        if step == n_steps:
            got.append(jnp.concatenate([ahead, behind], 0))
            offsets.append(step)
        else:
            got += [ahead, behind]
            offsets += [step, -step]
    swapped += [lax.ppermute(w, "core", SWAP) for w in got[len(swapped):]]
    prefix = chip_finish(chip_prefix_half, partner_state, core)
    normed = normalize(query_heads, prefix, within_block, norm_gain)
    gathered = gather_head(normed, n_head, place)
    row_count = gathered.shape[0]
    ring_place = jnp.asarray([order.index(j) for j in range(n_chip)], jnp.int32)[lax.axis_index("chip")]
    sources = jnp.asarray(order, jnp.int32)[(ring_place - jnp.asarray(offsets, jnp.int32)) % n_chip]
    cores = jnp.stack([core, 1 - core]).astype(jnp.int32)
    starts = ((sources[:, None] * 2 + cores[None, :]) * out_weight.shape[0]).reshape(-1)
    return project_blocks(gathered, starts, [w for pair in zip(got, swapped) for w in pair])


def solution(mesh):
    n_seq = mesh.shape["seq"]
    n_head = mesh.shape["head"]
    fine = Mesh(mesh.devices.reshape(n_seq // 2, 2, n_head), ("chip", "core", "head"))
    rows = ("chip", "core", "head")
    order = chip_cycle(fine.devices) if n_head == 2 else None
    if order is None:
        body = functools.partial(local_gather, n_chip=n_seq // 2, n_head=n_head)
    else:
        body = functools.partial(local_ring, n_chip=n_seq // 2, n_head=n_head, order=order)
    return jax.shard_map(
        body,
        mesh=fine,
        in_specs=(
            P(rows, None),
            P(rows, None),
            P(rows, None),
            P(("chip", "core"), "head"),
            P("head"),
        ),
        out_specs=P(("chip", "core"), "head"),
        check_vma=False,
    )
```

```python
import functools

import jax
import jax.numpy as jnp
from jax import lax
from jax.experimental import pallas as pl
from jax.experimental.pallas import tpu as pltpu
from jax.sharding import Mesh
from jax.sharding import PartitionSpec as P

HEAD_DIM = 128
SWAP = [(0, 1), (1, 0)]


def exclusive_prefix(state, axis, size):
    total = state
    shift = 1
    while shift < size:
        pairs = [(i, i + shift) for i in range(size - shift)]
        total = total + lax.ppermute(total, axis, pairs)
        shift *= 2
    return total - state


def pair_order(own, other, place, axis):
    first = jnp.where(place == 0, own, other)
    second = jnp.where(place == 0, other, own)
    return jnp.concatenate([first, second], axis=axis)


def head_blocks(arrays, n_head, place):
    if n_head == 2:
        rows = arrays[0].shape[0]
        width = arrays[0].shape[1] // 2
        stacked = jnp.stack(arrays).reshape(len(arrays), rows, 2, width)
        own = lax.dynamic_index_in_dim(stacked, place, 2, False)
        sent = lax.dynamic_index_in_dim(stacked, 1 - place, 2, False)
        other = lax.ppermute(sent, "head", SWAP)
        block = pair_order(own, other, place, 1)
        return [block[i] for i in range(len(arrays))]
    return [
        lax.all_to_all(a, "head", split_axis=1, concat_axis=0, tiled=True) for a in arrays
    ]


def chip_cycle(devices):
    n = devices.shape[0]
    coords = [getattr(devices[j, 0, 0], "coords", None) for j in range(n)]
    if n < 4 or n > 16 or any(c is None for c in coords):
        return None

    def adjacent(a, b):
        return sum(abs(int(u) - int(v)) for u, v in zip(coords[a], coords[b])) == 1

    path = [0]

    def search():
        if len(path) == n:
            return adjacent(path[-1], path[0])
        for k in range(n):
            if k not in path and adjacent(path[-1], k):
                path.append(k)
                if search():
                    return True
                path.pop()
        return False

    return list(path) if search() else None


def ring_links(order):
    n = len(order)
    forward = [(order[i], order[(i + 1) % n]) for i in range(n)]
    backward = [(order[(i + 1) % n], order[i]) for i in range(n)]
    return forward, backward


def ring_step(ahead, behind, order, last=False):
    forward, backward = ring_links(order)
    if last:
        half_rows = ahead.shape[0] // 2
        return lax.ppermute(ahead[:half_rows], "chip", forward), lax.ppermute(
            behind[half_rows:], "chip", backward
        )
    return lax.ppermute(ahead, "chip", forward), lax.ppermute(behind, "chip", backward)


def within_block_part(query_heads, key_heads, value_heads):
    row_count = query_heads.shape[0]
    block_rows = min(512, row_count)
    parts_list = []
    for first_row in range(0, row_count, block_rows):
        last_row = min(first_row + block_rows, row_count)
        scores = jnp.einsum(
            "thd,shd->hts",
            query_heads[first_row:last_row],
            key_heads[:last_row],
            preferred_element_type=jnp.float32,
        )
        row_index = first_row + lax.broadcasted_iota(jnp.int32, (last_row - first_row, last_row), 0)
        col_index = lax.broadcasted_iota(jnp.int32, (last_row - first_row, last_row), 1)
        scores = jnp.where((col_index <= row_index)[None], scores, jnp.zeros_like(scores)).astype(
            jnp.bfloat16
        )
        parts_list.append(
            jnp.einsum(
                "hts,she->the", scores, value_heads[:last_row], preferred_element_type=jnp.float32
            )
        )
    return jnp.concatenate(parts_list, axis=0)


def normalize(query_heads, prefix, within_block, norm_gain):
    heads_dev = query_heads.shape[1]
    carried = jnp.einsum(
        "thd,hde->the", query_heads, prefix.astype(jnp.bfloat16), preferred_element_type=jnp.float32
    )
    attended = carried + within_block
    mean_square = jnp.mean(attended * attended, axis=2, keepdims=True)
    gain_heads = norm_gain.reshape(heads_dev, HEAD_DIM)
    normed = (attended * lax.rsqrt(mean_square + 1e-06) * gain_heads[None]).astype(jnp.bfloat16)
    return normed.reshape(query_heads.shape[0], heads_dev * HEAD_DIM)


def gather_head(normed, n_head, place):
    if n_head == 2:
        other = lax.ppermute(normed, "head", SWAP)
        return pair_order(normed, other, place, 1)
    return lax.all_gather(normed, "head", axis=1, tiled=True)


def chip_scan(kv_state, core, n_chip):
    partner_state = lax.ppermute(kv_state, "core", SWAP)
    chip_state = kv_state + partner_state
    half = kv_state.shape[0] // 2
    chip_half = lax.dynamic_slice_in_dim(chip_state, core * half, half, 0)
    return partner_state, chip_half


def chip_finish(chip_prefix_half, partner_state, core):
    other_half = lax.ppermute(chip_prefix_half, "core", SWAP)
    chip_prefix = pair_order(chip_prefix_half, other_half, core, 0)
    return chip_prefix + jnp.where(core == 1, partner_state, jnp.zeros_like(partner_state))


def split_heads(block, heads_dev):
    return block.reshape(block.shape[0], heads_dev, HEAD_DIM)


def project_blocks(normed, starts, blocks, partial=None, group=4):
    n = len(blocks)
    rows, cols = blocks[0].shape
    tokens = normed.shape[0]
    extra = [] if partial is None else [partial]

    def kernel(starts_ref, normed_ref, *refs):
        block_refs = refs[:n]
        refs = refs[n:]
        if partial is not None:
            partial_ref, refs = refs[0], refs[1:]
        out_ref, features, weights, sems, acc = refs
        copies = []
        for i in range(n):
            start = pl.multiple_of(starts_ref[i], rows)
            copies.append(
                (
                    pltpu.make_async_copy(
                        normed_ref.at[:, pl.ds(start, rows)],
                        features.at[:, pl.ds(i * rows, rows)],
                        sems.at[0, i],
                    ),
                    pltpu.make_async_copy(
                        block_refs[i], weights.at[pl.ds(i * rows, rows), :], sems.at[1, i]
                    ),
                )
            )
        for pair in copies:
            for c in pair:
                c.start()
        for g in range(0, n, group):
            last = min(g + group, n)
            for i in range(g, last):
                for c in copies[i]:
                    c.wait()
            part = jnp.dot(
                features[:, g * rows:last * rows],
                weights[g * rows:last * rows, :],
                preferred_element_type=jnp.float32,
            )
            if g == 0:
                acc[...] = part if partial is None else partial_ref[...] + part
            else:
                acc[...] += part
        out_ref[...] = acc[...].astype(out_ref.dtype)

    return pl.pallas_call(
        kernel,
        out_shape=jax.ShapeDtypeStruct(
            (tokens, cols), jnp.float32 if partial is None else jnp.bfloat16
        ),
        in_specs=[pl.BlockSpec(memory_space=pltpu.SMEM), pl.BlockSpec(memory_space=pl.ANY)]
        + [pl.BlockSpec(memory_space=pl.ANY)] * n
        + [pl.BlockSpec(memory_space=pltpu.VMEM)] * len(extra),
        out_specs=pl.BlockSpec(memory_space=pltpu.VMEM),
        scratch_shapes=[
            pltpu.VMEM((tokens, n * rows), normed.dtype),
            pltpu.VMEM((n * rows, cols), blocks[0].dtype),
            pltpu.SemaphoreType.DMA((2, n)),
            pltpu.VMEM((tokens, cols), jnp.float32),
        ],
    )(starts, normed, *blocks, *extra)


def local_gather(queries, keys, values, out_weight, norm_gain, n_chip, n_head):
    heads_dev = norm_gain.shape[0] // HEAD_DIM
    core = lax.axis_index("core")
    place = lax.axis_index("head") if n_head == 2 else 0
    weight_own = lax.all_gather(out_weight, "chip", axis=0, tiled=True)
    query_block, key_block, value_block = head_blocks([queries, keys, values], n_head, place)
    query_heads, key_heads, value_heads = (
        split_heads(b, heads_dev) for b in (query_block, key_block, value_block)
    )
    kv_state = jnp.einsum(
        "thd,the->hde", key_heads, value_heads, preferred_element_type=jnp.float32
    )
    partner_state, chip_half = chip_scan(kv_state, core, n_chip)
    prefix = chip_finish(exclusive_prefix(chip_half, "chip", n_chip), partner_state, core)
    within_block = within_block_part(query_heads, key_heads, value_heads)
    normed = normalize(query_heads, prefix, within_block, norm_gain)
    gathered = gather_head(normed, n_head, place)
    row_count = gathered.shape[0]
    split = gathered.reshape(row_count, n_chip, 2, out_weight.shape[0])
    weight_own, split = lax.optimization_barrier((weight_own, split))
    weight_other = lax.ppermute(weight_own, "core", SWAP)
    normed_own = lax.dynamic_index_in_dim(split, core, 2, False).reshape(row_count, -1)
    normed_other = lax.dynamic_index_in_dim(split, 1 - core, 2, False).reshape(row_count, -1)
    outcome = jnp.dot(normed_own, weight_own, preferred_element_type=jnp.float32)
    outcome = outcome + jnp.dot(normed_other, weight_other, preferred_element_type=jnp.float32)
    return outcome.astype(jnp.bfloat16)


def local_ring(queries, keys, values, out_weight, norm_gain, n_chip, n_head, order):
    heads_dev = norm_gain.shape[0] // HEAD_DIM
    core = lax.axis_index("core")
    place = lax.axis_index("head")
    n_steps = n_chip // 2
    barrier = lax.optimization_barrier
    key_block, value_block = head_blocks([keys, values], n_head, place)
    ahead, behind = ring_step(out_weight, out_weight, order)
    ahead, behind, key_block, value_block = barrier((ahead, behind, key_block, value_block))
    got = [out_weight, ahead, behind]
    offsets = [0, 1, -1]
    (query_block,) = head_blocks([queries], n_head, place)
    swapped = [lax.ppermute(w, "core", SWAP) for w in got]
    key_heads, value_heads = split_heads(key_block, heads_dev), split_heads(value_block, heads_dev)
    kv_state = jnp.einsum(
        "thd,the->hde", key_heads, value_heads, preferred_element_type=jnp.float32
    )
    partner_state, chip_half = chip_scan(kv_state, core, n_chip)
    chip_prefix_half = exclusive_prefix(chip_half, "chip", n_chip)
    query_heads = split_heads(query_block, heads_dev)
    within_block = within_block_part(query_heads, key_heads, value_heads)
    swapped += [lax.ppermute(w, "core", SWAP) for w in got[len(swapped):]]
    chip_prefix_half, within_block, swapped = barrier((chip_prefix_half, within_block, swapped))
    for step in range(2, n_steps + 1):
        ahead, behind = ring_step(ahead, behind, order, last=step == n_steps)
        if step == n_steps:
            got.append(jnp.concatenate([ahead, behind], 0))
            offsets.append(step)
        else:
            got += [ahead, behind]
            offsets += [step, -step]
    swapped += [lax.ppermute(w, "core", SWAP) for w in got[len(swapped):]]
    prefix = chip_finish(chip_prefix_half, partner_state, core)
    normed = normalize(query_heads, prefix, within_block, norm_gain)
    gathered = gather_head(normed, n_head, place)
    row_count = gathered.shape[0]
    ring_place = jnp.asarray([order.index(j) for j in range(n_chip)], jnp.int32)[lax.axis_index("chip")]
    sources = jnp.asarray(order, jnp.int32)[(ring_place - jnp.asarray(offsets, jnp.int32)) % n_chip]
    cores = jnp.stack([core, 1 - core]).astype(jnp.int32)
    starts = ((sources[:, None] * 2 + cores[None, :]) * out_weight.shape[0]).reshape(-1)
    blocks = [w for pair in zip(got, swapped) for w in pair]
    early = project_blocks(gathered, starts[:-2], blocks[:-2])
    return project_blocks(gathered, starts[-2:], blocks[-2:], partial=early)


def solution(mesh):
    n_seq = mesh.shape["seq"]
    n_head = mesh.shape["head"]
    fine = Mesh(mesh.devices.reshape(n_seq // 2, 2, n_head), ("chip", "core", "head"))
    rows = ("chip", "core", "head")
    order = chip_cycle(fine.devices) if n_head == 2 else None
    if order is None:
        body = functools.partial(local_gather, n_chip=n_seq // 2, n_head=n_head)
    else:
        body = functools.partial(local_ring, n_chip=n_seq // 2, n_head=n_head, order=order)
    return jax.shard_map(
        body,
        mesh=fine,
        in_specs=(
            P(rows, None),
            P(rows, None),
            P(rows, None),
            P(("chip", "core"), "head"),
            P("head"),
        ),
        out_specs=P(("chip", "core"), "head"),
        check_vma=False,
    )
```

```python
import functools

import jax
import jax.numpy as jnp
from jax import lax
from jax.experimental import pallas as pl
from jax.experimental.pallas import tpu as pltpu
from jax.sharding import Mesh
from jax.sharding import PartitionSpec as P

HEAD_DIM = 128
SWAP = [(0, 1), (1, 0)]


def exclusive_prefix(state, axis, size):
    total = state
    shift = 1
    while shift < size:
        pairs = [(i, i + shift) for i in range(size - shift)]
        total = total + lax.ppermute(total, axis, pairs)
        shift *= 2
    return total - state


def pair_order(own, other, place, axis):
    first = jnp.where(place == 0, own, other)
    second = jnp.where(place == 0, other, own)
    return jnp.concatenate([first, second], axis=axis)


def head_blocks(arrays, n_head, place):
    if n_head == 2:
        rows = arrays[0].shape[0]
        width = arrays[0].shape[1] // 2
        stacked = jnp.stack(arrays).reshape(len(arrays), rows, 2, width)
        own = lax.dynamic_index_in_dim(stacked, place, 2, False)
        sent = lax.dynamic_index_in_dim(stacked, 1 - place, 2, False)
        other = lax.ppermute(sent, "head", SWAP)
        block = pair_order(own, other, place, 1)
        return [block[i] for i in range(len(arrays))]
    return [
        lax.all_to_all(a, "head", split_axis=1, concat_axis=0, tiled=True) for a in arrays
    ]


def chip_cycle(devices):
    n = devices.shape[0]
    coords = [getattr(devices[j, 0, 0], "coords", None) for j in range(n)]
    if n < 4 or n > 16 or any(c is None for c in coords):
        return None

    def adjacent(a, b):
        return sum(abs(int(u) - int(v)) for u, v in zip(coords[a], coords[b])) == 1

    path = [0]

    def search():
        if len(path) == n:
            return adjacent(path[-1], path[0])
        for k in range(n):
            if k not in path and adjacent(path[-1], k):
                path.append(k)
                if search():
                    return True
                path.pop()
        return False

    return list(path) if search() else None


def ring_links(order):
    n = len(order)
    forward = [(order[i], order[(i + 1) % n]) for i in range(n)]
    backward = [(order[(i + 1) % n], order[i]) for i in range(n)]
    return forward, backward


def ring_step(ahead, behind, order, last=False):
    forward, backward = ring_links(order)
    if last:
        half_rows = ahead.shape[0] // 2
        return lax.ppermute(ahead[:half_rows], "chip", forward), lax.ppermute(
            behind[half_rows:], "chip", backward
        )
    return lax.ppermute(ahead, "chip", forward), lax.ppermute(behind, "chip", backward)


def within_block_part(query_heads, key_heads, value_heads):
    row_count = query_heads.shape[0]
    block_rows = min(512, row_count)
    parts_list = []
    for first_row in range(0, row_count, block_rows):
        last_row = min(first_row + block_rows, row_count)
        scores = jnp.einsum(
            "thd,shd->hts",
            query_heads[first_row:last_row],
            key_heads[:last_row],
            preferred_element_type=jnp.float32,
        )
        row_index = first_row + lax.broadcasted_iota(jnp.int32, (last_row - first_row, last_row), 0)
        col_index = lax.broadcasted_iota(jnp.int32, (last_row - first_row, last_row), 1)
        scores = jnp.where((col_index <= row_index)[None], scores, jnp.zeros_like(scores)).astype(
            jnp.bfloat16
        )
        parts_list.append(
            jnp.einsum(
                "hts,she->the", scores, value_heads[:last_row], preferred_element_type=jnp.float32
            )
        )
    return jnp.concatenate(parts_list, axis=0)


def normalize(query_heads, prefix, within_block, norm_gain):
    heads_dev = query_heads.shape[1]
    carried = jnp.einsum(
        "thd,hde->the", query_heads, prefix.astype(jnp.bfloat16), preferred_element_type=jnp.float32
    )
    attended = carried + within_block
    mean_square = jnp.mean(attended * attended, axis=2, keepdims=True)
    gain_heads = norm_gain.reshape(heads_dev, HEAD_DIM)
    normed = (attended * lax.rsqrt(mean_square + 1e-06) * gain_heads[None]).astype(jnp.bfloat16)
    return normed.reshape(query_heads.shape[0], heads_dev * HEAD_DIM)


def gather_head(normed, n_head, place):
    if n_head == 2:
        other = lax.ppermute(normed, "head", SWAP)
        return pair_order(normed, other, place, 1)
    return lax.all_gather(normed, "head", axis=1, tiled=True)


def chip_scan(kv_state, core, n_chip):
    partner_state = lax.ppermute(kv_state, "core", SWAP)
    chip_state = kv_state + partner_state
    half = kv_state.shape[0] // 2
    chip_half = lax.dynamic_slice_in_dim(chip_state, core * half, half, 0)
    return partner_state, chip_half


def chip_finish(chip_prefix_half, partner_state, core):
    other_half = lax.ppermute(chip_prefix_half, "core", SWAP)
    chip_prefix = pair_order(chip_prefix_half, other_half, core, 0)
    return chip_prefix + jnp.where(core == 1, partner_state, jnp.zeros_like(partner_state))


def split_heads(block, heads_dev):
    return block.reshape(block.shape[0], heads_dev, HEAD_DIM)


def project_blocks(normed, starts, blocks, group=4):
    n = len(blocks)
    rows, cols = blocks[0].shape
    tokens = normed.shape[0]

    def kernel(starts_ref, normed_ref, *refs):
        block_refs = refs[:n]
        out_ref, features, weights, sems, acc = refs[n:]
        copies = []
        for i in range(n):
            start = pl.multiple_of(starts_ref[i], rows)
            copies.append(
                (
                    pltpu.make_async_copy(
                        normed_ref.at[:, pl.ds(start, rows)],
                        features.at[:, pl.ds(i * rows, rows)],
                        sems.at[0, i],
                    ),
                    pltpu.make_async_copy(
                        block_refs[i], weights.at[pl.ds(i * rows, rows), :], sems.at[1, i]
                    ),
                )
            )
        for pair in copies:
            for c in pair:
                c.start()
        for g in range(0, n, group):
            last = min(g + group, n)
            for i in range(g, last):
                for c in copies[i]:
                    c.wait()
            part = jnp.dot(
                features[:, g * rows:last * rows],
                weights[g * rows:last * rows, :],
                preferred_element_type=jnp.float32,
            )
            if g == 0:
                acc[...] = part
            else:
                acc[...] += part
        out_ref[...] = acc[...].astype(out_ref.dtype)

    return pl.pallas_call(
        kernel,
        out_shape=jax.ShapeDtypeStruct((tokens, cols), jnp.bfloat16),
        in_specs=[pl.BlockSpec(memory_space=pltpu.SMEM), pl.BlockSpec(memory_space=pl.ANY)]
        + [pl.BlockSpec(memory_space=pl.ANY)] * n,
        out_specs=pl.BlockSpec(memory_space=pltpu.VMEM),
        scratch_shapes=[
            pltpu.VMEM((tokens, n * rows), normed.dtype),
            pltpu.VMEM((n * rows, cols), blocks[0].dtype),
            pltpu.SemaphoreType.DMA((2, n)),
            pltpu.VMEM((tokens, cols), jnp.float32),
        ],
    )(starts, normed, *blocks)


def local_gather(queries, keys, values, out_weight, norm_gain, n_chip, n_head):
    heads_dev = norm_gain.shape[0] // HEAD_DIM
    core = lax.axis_index("core")
    place = lax.axis_index("head") if n_head == 2 else 0
    weight_own = lax.all_gather(out_weight, "chip", axis=0, tiled=True)
    query_block, key_block, value_block = head_blocks([queries, keys, values], n_head, place)
    query_heads, key_heads, value_heads = (
        split_heads(b, heads_dev) for b in (query_block, key_block, value_block)
    )
    kv_state = jnp.einsum(
        "thd,the->hde", key_heads, value_heads, preferred_element_type=jnp.float32
    )
    partner_state, chip_half = chip_scan(kv_state, core, n_chip)
    prefix = chip_finish(exclusive_prefix(chip_half, "chip", n_chip), partner_state, core)
    within_block = within_block_part(query_heads, key_heads, value_heads)
    normed = normalize(query_heads, prefix, within_block, norm_gain)
    gathered = gather_head(normed, n_head, place)
    row_count = gathered.shape[0]
    split = gathered.reshape(row_count, n_chip, 2, out_weight.shape[0])
    weight_own, split = lax.optimization_barrier((weight_own, split))
    weight_other = lax.ppermute(weight_own, "core", SWAP)
    normed_own = lax.dynamic_index_in_dim(split, core, 2, False).reshape(row_count, -1)
    normed_other = lax.dynamic_index_in_dim(split, 1 - core, 2, False).reshape(row_count, -1)
    outcome = jnp.dot(normed_own, weight_own, preferred_element_type=jnp.float32)
    outcome = outcome + jnp.dot(normed_other, weight_other, preferred_element_type=jnp.float32)
    return outcome.astype(jnp.bfloat16)


def local_ring(queries, keys, values, out_weight, norm_gain, n_chip, n_head, order):
    heads_dev = norm_gain.shape[0] // HEAD_DIM
    core = lax.axis_index("core")
    place = lax.axis_index("head")
    n_steps = n_chip // 2
    barrier = lax.optimization_barrier
    key_block, value_block = head_blocks([keys, values], n_head, place)
    ahead, behind = ring_step(out_weight, out_weight, order)
    ahead, behind, key_block, value_block = barrier((ahead, behind, key_block, value_block))
    got = [out_weight, ahead, behind]
    offsets = [0, 1, -1]
    (query_block,) = head_blocks([queries], n_head, place)
    swapped = [lax.ppermute(w, "core", SWAP) for w in got]
    key_heads, value_heads = split_heads(key_block, heads_dev), split_heads(value_block, heads_dev)
    kv_state = jnp.einsum(
        "thd,the->hde", key_heads, value_heads, preferred_element_type=jnp.float32
    )
    partner_state, chip_half = chip_scan(kv_state, core, n_chip)
    query_heads = split_heads(query_block, heads_dev)
    within_block = within_block_part(query_heads, key_heads, value_heads)
    total = chip_half
    shift, step = 1, 2
    while shift < n_chip:
        pairs = [(i, i + shift) for i in range(n_chip - shift)]
        total = total + lax.ppermute(total, "chip", pairs)
        if step <= n_steps:
            ahead, behind = ring_step(ahead, behind, order, last=step == n_steps)
            fresh = [jnp.concatenate([ahead, behind], 0)] if step == n_steps else [ahead, behind]
            ahead, behind, total, swapped = barrier((ahead, behind, total, swapped))
            if step < n_steps:
                fresh = [ahead, behind]
            got += fresh
            offsets += [step] if step == n_steps else [step, -step]
            swapped = swapped + [lax.ppermute(w, "core", SWAP) for w in fresh]
            step += 1
        shift *= 2
    chip_prefix_half = total - chip_half
    while step <= n_steps:
        ahead, behind = ring_step(ahead, behind, order, last=step == n_steps)
        if step == n_steps:
            got.append(jnp.concatenate([ahead, behind], 0))
            offsets.append(step)
        else:
            got += [ahead, behind]
            offsets += [step, -step]
        step += 1
    swapped += [lax.ppermute(w, "core", SWAP) for w in got[len(swapped):]]
    prefix = chip_finish(chip_prefix_half, partner_state, core)
    normed = normalize(query_heads, prefix, within_block, norm_gain)
    gathered = gather_head(normed, n_head, place)
    row_count = gathered.shape[0]
    ring_place = jnp.asarray([order.index(j) for j in range(n_chip)], jnp.int32)[lax.axis_index("chip")]
    sources = jnp.asarray(order, jnp.int32)[(ring_place - jnp.asarray(offsets, jnp.int32)) % n_chip]
    cores = jnp.stack([core, 1 - core]).astype(jnp.int32)
    starts = ((sources[:, None] * 2 + cores[None, :]) * out_weight.shape[0]).reshape(-1)
    return project_blocks(gathered, starts, [w for pair in zip(got, swapped) for w in pair])


def solution(mesh):
    n_seq = mesh.shape["seq"]
    n_head = mesh.shape["head"]
    fine = Mesh(mesh.devices.reshape(n_seq // 2, 2, n_head), ("chip", "core", "head"))
    rows = ("chip", "core", "head")
    order = chip_cycle(fine.devices) if n_head == 2 else None
    if order is None:
        body = functools.partial(local_gather, n_chip=n_seq // 2, n_head=n_head)
    else:
        body = functools.partial(local_ring, n_chip=n_seq // 2, n_head=n_head, order=order)
    return jax.shard_map(
        body,
        mesh=fine,
        in_specs=(
            P(rows, None),
            P(rows, None),
            P(rows, None),
            P(("chip", "core"), "head"),
            P("head"),
        ),
        out_specs=P(("chip", "core"), "head"),
        check_vma=False,
    )
```

```python
import functools

import jax
import jax.numpy as jnp
from jax import lax
from jax.experimental import pallas as pl
from jax.experimental.pallas import tpu as pltpu
from jax.sharding import Mesh
from jax.sharding import PartitionSpec as P

HEAD_DIM = 128
SWAP = [(0, 1), (1, 0)]


def exclusive_prefix(state, axis, size):
    total = state
    shift = 1
    while shift < size:
        pairs = [(i, i + shift) for i in range(size - shift)]
        total = total + lax.ppermute(total, axis, pairs)
        shift *= 2
    return total - state


def pair_order(own, other, place, axis):
    first = jnp.where(place == 0, own, other)
    second = jnp.where(place == 0, other, own)
    return jnp.concatenate([first, second], axis=axis)


def head_blocks(arrays, n_head, place):
    if n_head == 2:
        width = arrays[0].shape[1] // 2
        own = [lax.dynamic_slice_in_dim(a, place * width, width, 1) for a in arrays]
        sent = [lax.dynamic_slice_in_dim(a, (1 - place) * width, width, 1) for a in arrays]
        other = lax.ppermute(tuple(sent), "head", SWAP)
        return [pair_order(o, r, place, 0) for o, r in zip(own, other)]
    return [
        lax.all_to_all(a, "head", split_axis=1, concat_axis=0, tiled=True) for a in arrays
    ]


def chip_cycle(devices):
    n = devices.shape[0]
    coords = [getattr(devices[j, 0, 0], "coords", None) for j in range(n)]
    if n < 4 or n > 16 or any(c is None for c in coords):
        return None

    def adjacent(a, b):
        return sum(abs(int(u) - int(v)) for u, v in zip(coords[a], coords[b])) == 1

    path = [0]

    def search():
        if len(path) == n:
            return adjacent(path[-1], path[0])
        for k in range(n):
            if k not in path and adjacent(path[-1], k):
                path.append(k)
                if search():
                    return True
                path.pop()
        return False

    return list(path) if search() else None


def ring_links(order):
    n = len(order)
    forward = [(order[i], order[(i + 1) % n]) for i in range(n)]
    backward = [(order[(i + 1) % n], order[i]) for i in range(n)]
    return forward, backward


def ring_step(ahead, behind, order, last=False):
    forward, backward = ring_links(order)
    if last:
        half_rows = ahead.shape[0] // 2
        return lax.ppermute(ahead[:half_rows], "chip", forward), lax.ppermute(
            behind[half_rows:], "chip", backward
        )
    return lax.ppermute(ahead, "chip", forward), lax.ppermute(behind, "chip", backward)


def within_block_part(query_heads, key_heads, value_heads):
    row_count = query_heads.shape[0]
    block_rows = min(512, row_count)
    parts_list = []
    for first_row in range(0, row_count, block_rows):
        last_row = min(first_row + block_rows, row_count)
        scores = jnp.einsum(
            "thd,shd->hts",
            query_heads[first_row:last_row],
            key_heads[:last_row],
            preferred_element_type=jnp.float32,
        )
        row_index = first_row + lax.broadcasted_iota(jnp.int32, (last_row - first_row, last_row), 0)
        col_index = lax.broadcasted_iota(jnp.int32, (last_row - first_row, last_row), 1)
        scores = jnp.where((col_index <= row_index)[None], scores, jnp.zeros_like(scores)).astype(
            jnp.bfloat16
        )
        parts_list.append(
            jnp.einsum(
                "hts,she->the", scores, value_heads[:last_row], preferred_element_type=jnp.float32
            )
        )
    return jnp.concatenate(parts_list, axis=0)


def normalize(query_heads, prefix, within_block, norm_gain):
    heads_dev = query_heads.shape[1]
    carried = jnp.einsum(
        "thd,hde->the", query_heads, prefix.astype(jnp.bfloat16), preferred_element_type=jnp.float32
    )
    attended = carried + within_block
    mean_square = jnp.mean(attended * attended, axis=2, keepdims=True)
    gain_heads = norm_gain.reshape(heads_dev, HEAD_DIM)
    normed = (attended * lax.rsqrt(mean_square + 1e-06) * gain_heads[None]).astype(jnp.bfloat16)
    return normed.reshape(query_heads.shape[0], heads_dev * HEAD_DIM)


def gather_head(normed, n_head, place):
    if n_head == 2:
        other = lax.ppermute(normed, "head", SWAP)
        return pair_order(normed, other, place, 1)
    return lax.all_gather(normed, "head", axis=1, tiled=True)


def chip_scan(kv_state, core, n_chip):
    partner_state = lax.ppermute(kv_state, "core", SWAP)
    chip_state = kv_state + partner_state
    half = kv_state.shape[0] // 2
    chip_half = lax.dynamic_slice_in_dim(chip_state, core * half, half, 0)
    return partner_state, chip_half


def chip_finish(chip_prefix_half, partner_state, core):
    other_half = lax.ppermute(chip_prefix_half, "core", SWAP)
    chip_prefix = pair_order(chip_prefix_half, other_half, core, 0)
    return chip_prefix + jnp.where(core == 1, partner_state, jnp.zeros_like(partner_state))


def split_heads(block, heads_dev):
    return block.reshape(block.shape[0], heads_dev, HEAD_DIM)


def project_blocks(normed, starts, blocks, group=4):
    n = len(blocks)
    rows, cols = blocks[0].shape
    tokens = normed.shape[0]

    def kernel(starts_ref, normed_ref, *refs):
        block_refs = refs[:n]
        out_ref, features, weights, sems, acc = refs[n:]
        copies = []
        for i in range(n):
            start = pl.multiple_of(starts_ref[i], rows)
            copies.append(
                (
                    pltpu.make_async_copy(
                        normed_ref.at[:, pl.ds(start, rows)],
                        features.at[:, pl.ds(i * rows, rows)],
                        sems.at[0, i],
                    ),
                    pltpu.make_async_copy(
                        block_refs[i], weights.at[pl.ds(i * rows, rows), :], sems.at[1, i]
                    ),
                )
            )
        for pair in copies:
            for c in pair:
                c.start()
        for g in range(0, n, group):
            last = min(g + group, n)
            for i in range(g, last):
                for c in copies[i]:
                    c.wait()
            part = jnp.dot(
                features[:, g * rows:last * rows],
                weights[g * rows:last * rows, :],
                preferred_element_type=jnp.float32,
            )
            if g == 0:
                acc[...] = part
            else:
                acc[...] += part
        out_ref[...] = acc[...].astype(out_ref.dtype)

    return pl.pallas_call(
        kernel,
        out_shape=jax.ShapeDtypeStruct((tokens, cols), jnp.bfloat16),
        in_specs=[pl.BlockSpec(memory_space=pltpu.SMEM), pl.BlockSpec(memory_space=pl.ANY)]
        + [pl.BlockSpec(memory_space=pl.ANY)] * n,
        out_specs=pl.BlockSpec(memory_space=pltpu.VMEM),
        scratch_shapes=[
            pltpu.VMEM((tokens, n * rows), normed.dtype),
            pltpu.VMEM((n * rows, cols), blocks[0].dtype),
            pltpu.SemaphoreType.DMA((2, n)),
            pltpu.VMEM((tokens, cols), jnp.float32),
        ],
    )(starts, normed, *blocks)


def local_gather(queries, keys, values, out_weight, norm_gain, n_chip, n_head):
    heads_dev = norm_gain.shape[0] // HEAD_DIM
    core = lax.axis_index("core")
    place = lax.axis_index("head") if n_head == 2 else 0
    weight_own = lax.all_gather(out_weight, "chip", axis=0, tiled=True)
    query_block, key_block, value_block = head_blocks([queries, keys, values], n_head, place)
    query_heads, key_heads, value_heads = (
        split_heads(b, heads_dev) for b in (query_block, key_block, value_block)
    )
    kv_state = jnp.einsum(
        "thd,the->hde", key_heads, value_heads, preferred_element_type=jnp.float32
    )
    partner_state, chip_half = chip_scan(kv_state, core, n_chip)
    prefix = chip_finish(exclusive_prefix(chip_half, "chip", n_chip), partner_state, core)
    within_block = within_block_part(query_heads, key_heads, value_heads)
    normed = normalize(query_heads, prefix, within_block, norm_gain)
    gathered = gather_head(normed, n_head, place)
    row_count = gathered.shape[0]
    split = gathered.reshape(row_count, n_chip, 2, out_weight.shape[0])
    weight_own, split = lax.optimization_barrier((weight_own, split))
    weight_other = lax.ppermute(weight_own, "core", SWAP)
    normed_own = lax.dynamic_index_in_dim(split, core, 2, False).reshape(row_count, -1)
    normed_other = lax.dynamic_index_in_dim(split, 1 - core, 2, False).reshape(row_count, -1)
    outcome = jnp.dot(normed_own, weight_own, preferred_element_type=jnp.float32)
    outcome = outcome + jnp.dot(normed_other, weight_other, preferred_element_type=jnp.float32)
    return outcome.astype(jnp.bfloat16)


def local_ring(queries, keys, values, out_weight, norm_gain, n_chip, n_head, order):
    heads_dev = norm_gain.shape[0] // HEAD_DIM
    core = lax.axis_index("core")
    place = lax.axis_index("head")
    n_steps = n_chip // 2
    barrier = lax.optimization_barrier
    key_block, value_block = head_blocks([keys, values], n_head, place)
    ahead, behind = ring_step(out_weight, out_weight, order)
    ahead, behind, key_block, value_block = barrier((ahead, behind, key_block, value_block))
    got = [out_weight, ahead, behind]
    offsets = [0, 1, -1]
    (query_block,) = head_blocks([queries], n_head, place)
    swapped = [lax.ppermute(w, "core", SWAP) for w in got]
    key_heads, value_heads = split_heads(key_block, heads_dev), split_heads(value_block, heads_dev)
    kv_state = jnp.einsum(
        "thd,the->hde", key_heads, value_heads, preferred_element_type=jnp.float32
    )
    partner_state, chip_half = chip_scan(kv_state, core, n_chip)
    chip_prefix_half = exclusive_prefix(chip_half, "chip", n_chip)
    query_heads = split_heads(query_block, heads_dev)
    within_block = within_block_part(query_heads, key_heads, value_heads)
    swapped += [lax.ppermute(w, "core", SWAP) for w in got[len(swapped):]]
    chip_prefix_half, within_block, swapped = barrier((chip_prefix_half, within_block, swapped))
    for step in range(2, n_steps + 1):
        if step >= 4:
            early = len(got) - 2
            swapped += [lax.ppermute(w, "core", SWAP) for w in got[len(swapped):early]]
            ahead, behind, swapped = barrier((ahead, behind, swapped))
        ahead, behind = ring_step(ahead, behind, order, last=step == n_steps)
        if step == n_steps:
            got.append(jnp.concatenate([ahead, behind], 0))
            offsets.append(step)
        else:
            got += [ahead, behind]
            offsets += [step, -step]
    swapped += [lax.ppermute(w, "core", SWAP) for w in got[len(swapped):]]
    prefix = chip_finish(chip_prefix_half, partner_state, core)
    normed = normalize(query_heads, prefix, within_block, norm_gain)
    gathered = gather_head(normed, n_head, place)
    row_count = gathered.shape[0]
    ring_place = jnp.asarray([order.index(j) for j in range(n_chip)], jnp.int32)[lax.axis_index("chip")]
    sources = jnp.asarray(order, jnp.int32)[(ring_place - jnp.asarray(offsets, jnp.int32)) % n_chip]
    cores = jnp.stack([core, 1 - core]).astype(jnp.int32)
    starts = ((sources[:, None] * 2 + cores[None, :]) * out_weight.shape[0]).reshape(-1)
    return project_blocks(gathered, starts, [w for pair in zip(got, swapped) for w in pair])


def solution(mesh):
    n_seq = mesh.shape["seq"]
    n_head = mesh.shape["head"]
    fine = Mesh(mesh.devices.reshape(n_seq // 2, 2, n_head), ("chip", "core", "head"))
    rows = ("chip", "core", "head")
    order = chip_cycle(fine.devices) if n_head == 2 else None
    if order is None:
        body = functools.partial(local_gather, n_chip=n_seq // 2, n_head=n_head)
    else:
        body = functools.partial(local_ring, n_chip=n_seq // 2, n_head=n_head, order=order)
    return jax.shard_map(
        body,
        mesh=fine,
        in_specs=(
            P(rows, None),
            P(rows, None),
            P(rows, None),
            P(("chip", "core"), "head"),
            P("head"),
        ),
        out_specs=P(("chip", "core"), "head"),
        check_vma=False,
    )
```

```python
import functools

import jax
import jax.numpy as jnp
from jax import lax
from jax.experimental import pallas as pl
from jax.experimental.pallas import tpu as pltpu
from jax.sharding import Mesh
from jax.sharding import PartitionSpec as P

HEAD_DIM = 128
SWAP = [(0, 1), (1, 0)]


def exclusive_prefix(state, axis, size):
    total = state
    shift = 1
    while shift < size:
        pairs = [(i, i + shift) for i in range(size - shift)]
        total = total + lax.ppermute(total, axis, pairs)
        shift *= 2
    return total - state


def pair_order(own, other, place, axis):
    first = jnp.where(place == 0, own, other)
    second = jnp.where(place == 0, other, own)
    return jnp.concatenate([first, second], axis=axis)


def head_blocks(arrays, n_head, place):
    if n_head == 2:
        width = arrays[0].shape[1] // 2
        own = [lax.dynamic_slice_in_dim(a, place * width, width, 1) for a in arrays]
        sent = [lax.dynamic_slice_in_dim(a, (1 - place) * width, width, 1) for a in arrays]
        other = lax.ppermute(tuple(sent), "head", SWAP)
        return [pair_order(o, r, place, 0) for o, r in zip(own, other)]
    return [
        lax.all_to_all(a, "head", split_axis=1, concat_axis=0, tiled=True) for a in arrays
    ]


def chip_cycle(devices):
    n = devices.shape[0]
    coords = [getattr(devices[j, 0, 0], "coords", None) for j in range(n)]
    if n < 4 or n > 16 or any(c is None for c in coords):
        return None

    def adjacent(a, b):
        return sum(abs(int(u) - int(v)) for u, v in zip(coords[a], coords[b])) == 1

    path = [0]

    def search():
        if len(path) == n:
            return adjacent(path[-1], path[0])
        for k in range(n):
            if k not in path and adjacent(path[-1], k):
                path.append(k)
                if search():
                    return True
                path.pop()
        return False

    return list(path) if search() else None


def ring_links(order):
    n = len(order)
    forward = [(order[i], order[(i + 1) % n]) for i in range(n)]
    backward = [(order[(i + 1) % n], order[i]) for i in range(n)]
    return forward, backward


def ring_step(ahead, behind, order, last=False):
    forward, backward = ring_links(order)
    if last:
        half_rows = ahead.shape[0] // 2
        return lax.ppermute(ahead[:half_rows], "chip", forward), lax.ppermute(
            behind[half_rows:], "chip", backward
        )
    return lax.ppermute(ahead, "chip", forward), lax.ppermute(behind, "chip", backward)


def within_block_part(query_heads, key_heads, value_heads):
    row_count = query_heads.shape[0]
    block_rows = min(512, row_count)
    parts_list = []
    for first_row in range(0, row_count, block_rows):
        last_row = min(first_row + block_rows, row_count)
        scores = jnp.einsum(
            "thd,shd->hts",
            query_heads[first_row:last_row],
            key_heads[:last_row],
            preferred_element_type=jnp.float32,
        )
        row_index = first_row + lax.broadcasted_iota(jnp.int32, (last_row - first_row, last_row), 0)
        col_index = lax.broadcasted_iota(jnp.int32, (last_row - first_row, last_row), 1)
        scores = jnp.where((col_index <= row_index)[None], scores, jnp.zeros_like(scores)).astype(
            jnp.bfloat16
        )
        parts_list.append(
            jnp.einsum(
                "hts,she->the", scores, value_heads[:last_row], preferred_element_type=jnp.float32
            )
        )
    return jnp.concatenate(parts_list, axis=0)


def normalize(query_heads, prefix, within_block, norm_gain):
    heads_dev = query_heads.shape[1]
    carried = jnp.einsum(
        "thd,hde->the", query_heads, prefix.astype(jnp.bfloat16), preferred_element_type=jnp.float32
    )
    attended = carried + within_block
    mean_square = jnp.mean(attended * attended, axis=2, keepdims=True)
    gain_heads = norm_gain.reshape(heads_dev, HEAD_DIM)
    normed = (attended * lax.rsqrt(mean_square + 1e-06) * gain_heads[None]).astype(jnp.bfloat16)
    return normed.reshape(query_heads.shape[0], heads_dev * HEAD_DIM)


def gather_head(normed, n_head, place):
    if n_head == 2:
        other = lax.ppermute(normed, "head", SWAP)
        return pair_order(normed, other, place, 1)
    return lax.all_gather(normed, "head", axis=1, tiled=True)


def chip_scan(kv_state, core, n_chip):
    partner_state = lax.ppermute(kv_state, "core", SWAP)
    chip_state = kv_state + partner_state
    half = kv_state.shape[0] // 2
    chip_half = lax.dynamic_slice_in_dim(chip_state, core * half, half, 0)
    return partner_state, chip_half


def chip_finish(chip_prefix_half, partner_state, core):
    other_half = lax.ppermute(chip_prefix_half, "core", SWAP)
    chip_prefix = pair_order(chip_prefix_half, other_half, core, 0)
    return chip_prefix + jnp.where(core == 1, partner_state, jnp.zeros_like(partner_state))


def split_heads(block, heads_dev):
    return block.reshape(block.shape[0], heads_dev, HEAD_DIM)


def project_blocks(normed, starts, blocks, chunk, group=4):
    row_counts = [b.shape[0] for b in blocks]
    total = sum(row_counts)
    n = total // chunk
    cols = blocks[0].shape[1]
    tokens = normed.shape[0]
    firsts = [sum(row_counts[:i]) for i in range(len(blocks))]

    def kernel(starts_ref, normed_ref, *refs):
        block_refs = refs[: len(blocks)]
        out_ref, features, weights, sems, acc = refs[len(blocks):]
        feature_copies = []
        for i in range(n):
            start = pl.multiple_of(starts_ref[i], chunk)
            feature_copies.append(
                pltpu.make_async_copy(
                    normed_ref.at[:, pl.ds(start, chunk)],
                    features.at[:, pl.ds(i * chunk, chunk)],
                    sems.at[0, i],
                )
            )
        weight_copies = [
            pltpu.make_async_copy(
                block_refs[b], weights.at[pl.ds(firsts[b], row_counts[b]), :], sems.at[1, b]
            )
            for b in range(len(blocks))
        ]
        for c in feature_copies + weight_copies:
            c.start()
        waited = set()
        for g in range(0, n, group):
            last = min(g + group, n)
            for i in range(g, last):
                feature_copies[i].wait()
                b = max(k for k in range(len(blocks)) if firsts[k] <= i * chunk)
                if b not in waited:
                    weight_copies[b].wait()
                    waited.add(b)
            part = jnp.dot(
                features[:, g * chunk:last * chunk],
                weights[g * chunk:last * chunk, :],
                preferred_element_type=jnp.float32,
            )
            if g == 0:
                acc[...] = part
            else:
                acc[...] += part
        out_ref[...] = acc[...].astype(out_ref.dtype)

    return pl.pallas_call(
        kernel,
        out_shape=jax.ShapeDtypeStruct((tokens, cols), jnp.bfloat16),
        in_specs=[pl.BlockSpec(memory_space=pltpu.SMEM), pl.BlockSpec(memory_space=pl.ANY)]
        + [pl.BlockSpec(memory_space=pl.ANY)] * len(blocks),
        out_specs=pl.BlockSpec(memory_space=pltpu.VMEM),
        scratch_shapes=[
            pltpu.VMEM((tokens, total), normed.dtype),
            pltpu.VMEM((total, cols), blocks[0].dtype),
            pltpu.SemaphoreType.DMA((2, max(n, len(blocks)))),
            pltpu.VMEM((tokens, cols), jnp.float32),
        ],
    )(starts, normed, *blocks)


def local_gather(queries, keys, values, out_weight, norm_gain, n_chip, n_head):
    heads_dev = norm_gain.shape[0] // HEAD_DIM
    core = lax.axis_index("core")
    place = lax.axis_index("head") if n_head == 2 else 0
    weight_own = lax.all_gather(out_weight, "chip", axis=0, tiled=True)
    query_block, key_block, value_block = head_blocks([queries, keys, values], n_head, place)
    query_heads, key_heads, value_heads = (
        split_heads(b, heads_dev) for b in (query_block, key_block, value_block)
    )
    kv_state = jnp.einsum(
        "thd,the->hde", key_heads, value_heads, preferred_element_type=jnp.float32
    )
    partner_state, chip_half = chip_scan(kv_state, core, n_chip)
    prefix = chip_finish(exclusive_prefix(chip_half, "chip", n_chip), partner_state, core)
    within_block = within_block_part(query_heads, key_heads, value_heads)
    normed = normalize(query_heads, prefix, within_block, norm_gain)
    gathered = gather_head(normed, n_head, place)
    row_count = gathered.shape[0]
    split = gathered.reshape(row_count, n_chip, 2, out_weight.shape[0])
    weight_own, split = lax.optimization_barrier((weight_own, split))
    weight_other = lax.ppermute(weight_own, "core", SWAP)
    normed_own = lax.dynamic_index_in_dim(split, core, 2, False).reshape(row_count, -1)
    normed_other = lax.dynamic_index_in_dim(split, 1 - core, 2, False).reshape(row_count, -1)
    outcome = jnp.dot(normed_own, weight_own, preferred_element_type=jnp.float32)
    outcome = outcome + jnp.dot(normed_other, weight_other, preferred_element_type=jnp.float32)
    return outcome.astype(jnp.bfloat16)


def local_ring(queries, keys, values, out_weight, norm_gain, n_chip, n_head, order):
    heads_dev = norm_gain.shape[0] // HEAD_DIM
    core = lax.axis_index("core")
    place = lax.axis_index("head")
    n_steps = n_chip // 2
    barrier = lax.optimization_barrier
    weight_rows, weight_cols = out_weight.shape
    gathered_half = lax.all_gather(out_weight[:, : weight_cols // 2], "chip", axis=0, tiled=True)
    out_weight = out_weight[:, weight_cols // 2:]
    key_block, value_block = head_blocks([keys, values], n_head, place)
    ahead, behind = ring_step(out_weight, out_weight, order)
    ahead, behind, key_block, value_block = barrier((ahead, behind, key_block, value_block))
    got = [out_weight, ahead, behind]
    offsets = [0, 1, -1]
    (query_block,) = head_blocks([queries], n_head, place)
    swapped = [lax.ppermute(w, "core", SWAP) for w in got]
    key_heads, value_heads = split_heads(key_block, heads_dev), split_heads(value_block, heads_dev)
    kv_state = jnp.einsum(
        "thd,the->hde", key_heads, value_heads, preferred_element_type=jnp.float32
    )
    partner_state, chip_half = chip_scan(kv_state, core, n_chip)
    chip_prefix_half = exclusive_prefix(chip_half, "chip", n_chip)
    query_heads = split_heads(query_block, heads_dev)
    within_block = within_block_part(query_heads, key_heads, value_heads)
    swapped += [lax.ppermute(w, "core", SWAP) for w in got[len(swapped):]]
    chip_prefix_half, within_block, swapped = barrier((chip_prefix_half, within_block, swapped))
    for step in range(2, n_steps + 1):
        if step >= 4:
            early = len(got) - 2
            swapped += [lax.ppermute(w, "core", SWAP) for w in got[len(swapped):early]]
            ahead, behind, swapped = barrier((ahead, behind, swapped))
        ahead, behind = ring_step(ahead, behind, order, last=step == n_steps)
        if step == n_steps:
            got.append(jnp.concatenate([ahead, behind], 0))
            offsets.append(step)
        else:
            got += [ahead, behind]
            offsets += [step, -step]
    swapped += [lax.ppermute(w, "core", SWAP) for w in got[len(swapped):]]
    prefix = chip_finish(chip_prefix_half, partner_state, core)
    normed = normalize(query_heads, prefix, within_block, norm_gain)
    gathered = gather_head(normed, n_head, place)
    row_count = gathered.shape[0]
    ring_place = jnp.asarray([order.index(j) for j in range(n_chip)], jnp.int32)[lax.axis_index("chip")]
    sources = jnp.asarray(order, jnp.int32)[(ring_place - jnp.asarray(offsets, jnp.int32)) % n_chip]
    cores = jnp.stack([core, 1 - core]).astype(jnp.int32)
    starts = ((sources[:, None] * 2 + cores[None, :]) * weight_rows).reshape(-1)
    ring_part = project_blocks(
        gathered, starts, [w for pair in zip(got, swapped) for w in pair], weight_rows
    )
    gathered_half, gathered = barrier((gathered_half, gathered))
    partner_half = lax.ppermute(gathered_half, "core", SWAP)
    chips = jnp.arange(n_chip, dtype=jnp.int32)
    half_starts = jnp.concatenate([(chips * 2 + core) * weight_rows, (chips * 2 + 1 - core) * weight_rows])
    gather_part = project_blocks(gathered, half_starts, [gathered_half, partner_half], weight_rows)
    return jnp.concatenate([gather_part, ring_part], axis=1)


def solution(mesh):
    n_seq = mesh.shape["seq"]
    n_head = mesh.shape["head"]
    fine = Mesh(mesh.devices.reshape(n_seq // 2, 2, n_head), ("chip", "core", "head"))
    rows = ("chip", "core", "head")
    order = chip_cycle(fine.devices) if n_head == 2 else None
    if order is None:
        body = functools.partial(local_gather, n_chip=n_seq // 2, n_head=n_head)
    else:
        body = functools.partial(local_ring, n_chip=n_seq // 2, n_head=n_head, order=order)
    return jax.shard_map(
        body,
        mesh=fine,
        in_specs=(
            P(rows, None),
            P(rows, None),
            P(rows, None),
            P(("chip", "core"), "head"),
            P("head"),
        ),
        out_specs=P(("chip", "core"), "head"),
        check_vma=False,
    )
```

```python
import functools

import jax
import jax.numpy as jnp
from jax import lax
from jax.experimental import pallas as pl
from jax.experimental.pallas import tpu as pltpu
from jax.sharding import Mesh
from jax.sharding import PartitionSpec as P

HEAD_DIM = 128
SWAP = [(0, 1), (1, 0)]


def exclusive_prefix(state, axis, size):
    total = state
    shift = 1
    while shift < size:
        pairs = [(i, i + shift) for i in range(size - shift)]
        total = total + lax.ppermute(total, axis, pairs)
        shift *= 2
    return total - state


def pair_order(own, other, place, axis):
    first = jnp.where(place == 0, own, other)
    second = jnp.where(place == 0, other, own)
    return jnp.concatenate([first, second], axis=axis)


def head_blocks(arrays, n_head, place):
    if n_head == 2:
        width = arrays[0].shape[1] // 2
        own = [lax.dynamic_slice_in_dim(a, place * width, width, 1) for a in arrays]
        sent = [lax.dynamic_slice_in_dim(a, (1 - place) * width, width, 1) for a in arrays]
        other = lax.ppermute(tuple(sent), "head", SWAP)
        return [pair_order(o, r, place, 0) for o, r in zip(own, other)]
    return [
        lax.all_to_all(a, "head", split_axis=1, concat_axis=0, tiled=True) for a in arrays
    ]


def chip_cycle(devices):
    n = devices.shape[0]
    coords = [getattr(devices[j, 0, 0], "coords", None) for j in range(n)]
    if n < 4 or n > 16 or any(c is None for c in coords):
        return None

    def adjacent(a, b):
        return sum(abs(int(u) - int(v)) for u, v in zip(coords[a], coords[b])) == 1

    path = [0]

    def search():
        if len(path) == n:
            return adjacent(path[-1], path[0])
        for k in range(n):
            if k not in path and adjacent(path[-1], k):
                path.append(k)
                if search():
                    return True
                path.pop()
        return False

    return list(path) if search() else None


def ring_links(order):
    n = len(order)
    forward = [(order[i], order[(i + 1) % n]) for i in range(n)]
    backward = [(order[(i + 1) % n], order[i]) for i in range(n)]
    return forward, backward


def ring_step(ahead, behind, order, last=False):
    forward, backward = ring_links(order)
    if last:
        half_rows = ahead.shape[0] // 2
        return lax.ppermute(ahead[:half_rows], "chip", forward), lax.ppermute(
            behind[half_rows:], "chip", backward
        )
    return lax.ppermute(ahead, "chip", forward), lax.ppermute(behind, "chip", backward)


def within_block_part(query_heads, key_heads, value_heads):
    row_count = query_heads.shape[0]
    block_rows = min(512, row_count)
    parts_list = []
    for first_row in range(0, row_count, block_rows):
        last_row = min(first_row + block_rows, row_count)
        scores = jnp.einsum(
            "thd,shd->hts",
            query_heads[first_row:last_row],
            key_heads[:last_row],
            preferred_element_type=jnp.float32,
        )
        row_index = first_row + lax.broadcasted_iota(jnp.int32, (last_row - first_row, last_row), 0)
        col_index = lax.broadcasted_iota(jnp.int32, (last_row - first_row, last_row), 1)
        scores = jnp.where((col_index <= row_index)[None], scores, jnp.zeros_like(scores)).astype(
            jnp.bfloat16
        )
        parts_list.append(
            jnp.einsum(
                "hts,she->the", scores, value_heads[:last_row], preferred_element_type=jnp.float32
            )
        )
    return jnp.concatenate(parts_list, axis=0)


def normalize(query_heads, prefix, within_block, norm_gain):
    heads_dev = query_heads.shape[1]
    carried = jnp.einsum(
        "thd,hde->the", query_heads, prefix.astype(jnp.bfloat16), preferred_element_type=jnp.float32
    )
    attended = carried + within_block
    mean_square = jnp.mean(attended * attended, axis=2, keepdims=True)
    gain_heads = norm_gain.reshape(heads_dev, HEAD_DIM)
    normed = (attended * lax.rsqrt(mean_square + 1e-06) * gain_heads[None]).astype(jnp.bfloat16)
    return normed.reshape(query_heads.shape[0], heads_dev * HEAD_DIM)


def gather_head(normed, n_head, place):
    if n_head == 2:
        other = lax.ppermute(normed, "head", SWAP)
        return pair_order(normed, other, place, 1)
    return lax.all_gather(normed, "head", axis=1, tiled=True)


def chip_scan(kv_state, core, n_chip):
    partner_state = lax.ppermute(kv_state, "core", SWAP)
    chip_state = kv_state + partner_state
    half = kv_state.shape[0] // 2
    chip_half = lax.dynamic_slice_in_dim(chip_state, core * half, half, 0)
    return partner_state, chip_half


def chip_finish(chip_prefix_half, partner_state, core):
    other_half = lax.ppermute(chip_prefix_half, "core", SWAP)
    chip_prefix = pair_order(chip_prefix_half, other_half, core, 0)
    return chip_prefix + jnp.where(core == 1, partner_state, jnp.zeros_like(partner_state))


def split_heads(block, heads_dev):
    return block.reshape(block.shape[0], heads_dev, HEAD_DIM)


def project_blocks(normed, starts, blocks, group=4):
    n = len(blocks)
    rows, cols = blocks[0].shape
    tokens = normed.shape[0]

    def kernel(starts_ref, normed_ref, *refs):
        block_refs = refs[:n]
        out_ref, features, weights, sems, acc = refs[n:]
        copies = []
        for i in range(n):
            start = pl.multiple_of(starts_ref[i], rows)
            copies.append(
                (
                    pltpu.make_async_copy(
                        normed_ref.at[:, pl.ds(start, rows)],
                        features.at[:, pl.ds(i * rows, rows)],
                        sems.at[0, i],
                    ),
                    pltpu.make_async_copy(
                        block_refs[i], weights.at[pl.ds(i * rows, rows), :], sems.at[1, i]
                    ),
                )
            )
        for pair in copies:
            for c in pair:
                c.start()
        for g in range(0, n, group):
            last = min(g + group, n)
            for i in range(g, last):
                for c in copies[i]:
                    c.wait()
            part = jnp.dot(
                features[:, g * rows:last * rows],
                weights[g * rows:last * rows, :],
                preferred_element_type=jnp.float32,
            )
            if g == 0:
                acc[...] = part
            else:
                acc[...] += part
        out_ref[...] = acc[...].astype(out_ref.dtype)

    return pl.pallas_call(
        kernel,
        out_shape=jax.ShapeDtypeStruct((tokens, cols), jnp.bfloat16),
        in_specs=[pl.BlockSpec(memory_space=pltpu.SMEM), pl.BlockSpec(memory_space=pl.ANY)]
        + [pl.BlockSpec(memory_space=pl.ANY)] * n,
        out_specs=pl.BlockSpec(memory_space=pltpu.VMEM),
        scratch_shapes=[
            pltpu.VMEM((tokens, n * rows), normed.dtype),
            pltpu.VMEM((n * rows, cols), blocks[0].dtype),
            pltpu.SemaphoreType.DMA((2, n)),
            pltpu.VMEM((tokens, cols), jnp.float32),
        ],
    )(starts, normed, *blocks)


def local_gather(queries, keys, values, out_weight, norm_gain, n_chip, n_head):
    heads_dev = norm_gain.shape[0] // HEAD_DIM
    core = lax.axis_index("core")
    place = lax.axis_index("head") if n_head == 2 else 0
    weight_own = lax.all_gather(out_weight, "chip", axis=0, tiled=True)
    query_block, key_block, value_block = head_blocks([queries, keys, values], n_head, place)
    query_heads, key_heads, value_heads = (
        split_heads(b, heads_dev) for b in (query_block, key_block, value_block)
    )
    kv_state = jnp.einsum(
        "thd,the->hde", key_heads, value_heads, preferred_element_type=jnp.float32
    )
    partner_state, chip_half = chip_scan(kv_state, core, n_chip)
    prefix = chip_finish(exclusive_prefix(chip_half, "chip", n_chip), partner_state, core)
    within_block = within_block_part(query_heads, key_heads, value_heads)
    normed = normalize(query_heads, prefix, within_block, norm_gain)
    gathered = gather_head(normed, n_head, place)
    row_count = gathered.shape[0]
    split = gathered.reshape(row_count, n_chip, 2, out_weight.shape[0])
    weight_own, split = lax.optimization_barrier((weight_own, split))
    weight_other = lax.ppermute(weight_own, "core", SWAP)
    normed_own = lax.dynamic_index_in_dim(split, core, 2, False).reshape(row_count, -1)
    normed_other = lax.dynamic_index_in_dim(split, 1 - core, 2, False).reshape(row_count, -1)
    outcome = jnp.dot(normed_own, weight_own, preferred_element_type=jnp.float32)
    outcome = outcome + jnp.dot(normed_other, weight_other, preferred_element_type=jnp.float32)
    return outcome.astype(jnp.bfloat16)


def local_ring(queries, keys, values, out_weight, norm_gain, n_chip, n_head, order):
    heads_dev = norm_gain.shape[0] // HEAD_DIM
    core = lax.axis_index("core")
    place = lax.axis_index("head")
    n_steps = n_chip // 2
    barrier = lax.optimization_barrier
    key_block, value_block = head_blocks([keys, values], n_head, place)
    ahead, behind = ring_step(out_weight, out_weight, order)
    ahead, behind, key_block, value_block = barrier((ahead, behind, key_block, value_block))
    got = [out_weight, ahead, behind]
    offsets = [0, 1, -1]
    (query_block,) = head_blocks([queries], n_head, place)
    swapped = [lax.ppermute(w, "core", SWAP) for w in got]
    key_heads, value_heads = split_heads(key_block, heads_dev), split_heads(value_block, heads_dev)
    kv_state = jnp.einsum(
        "thd,the->hde", key_heads, value_heads, preferred_element_type=jnp.float32
    )
    partner_state, chip_half = chip_scan(kv_state, core, n_chip)
    chip_prefix_half = exclusive_prefix(chip_half, "chip", n_chip)
    query_heads = split_heads(query_block, heads_dev)
    within_block = within_block_part(query_heads, key_heads, value_heads)
    swapped += [lax.ppermute(w, "core", SWAP) for w in got[len(swapped):]]
    chip_prefix_half, within_block, swapped = barrier((chip_prefix_half, within_block, swapped))
    for step in range(2, n_steps + 1):
        if step >= 4:
            early = len(got) - 2
            swapped += [lax.ppermute(w, "core", SWAP) for w in got[len(swapped):early]]
            ahead, behind, swapped = barrier((ahead, behind, swapped))
        ahead, behind = ring_step(ahead, behind, order, last=step == n_steps)
        if step == n_steps:
            got.append(jnp.concatenate([ahead, behind], 0))
            offsets.append(step)
        else:
            got += [ahead, behind]
            offsets += [step, -step]
    swapped += [lax.ppermute(w, "core", SWAP) for w in got[len(swapped):]]
    prefix = chip_finish(chip_prefix_half, partner_state, core)
    normed = normalize(query_heads, prefix, within_block, norm_gain)
    normed, held = barrier((normed, got[-1] if n_steps < 4 else got[-3]))
    gathered = gather_head(normed, n_head, place)
    row_count = gathered.shape[0]
    ring_place = jnp.asarray([order.index(j) for j in range(n_chip)], jnp.int32)[lax.axis_index("chip")]
    sources = jnp.asarray(order, jnp.int32)[(ring_place - jnp.asarray(offsets, jnp.int32)) % n_chip]
    cores = jnp.stack([core, 1 - core]).astype(jnp.int32)
    starts = ((sources[:, None] * 2 + cores[None, :]) * out_weight.shape[0]).reshape(-1)
    return project_blocks(gathered, starts, [w for pair in zip(got, swapped) for w in pair])


def solution(mesh):
    n_seq = mesh.shape["seq"]
    n_head = mesh.shape["head"]
    fine = Mesh(mesh.devices.reshape(n_seq // 2, 2, n_head), ("chip", "core", "head"))
    rows = ("chip", "core", "head")
    order = chip_cycle(fine.devices) if n_head == 2 else None
    if order is None:
        body = functools.partial(local_gather, n_chip=n_seq // 2, n_head=n_head)
    else:
        body = functools.partial(local_ring, n_chip=n_seq // 2, n_head=n_head, order=order)
    return jax.shard_map(
        body,
        mesh=fine,
        in_specs=(
            P(rows, None),
            P(rows, None),
            P(rows, None),
            P(("chip", "core"), "head"),
            P("head"),
        ),
        out_specs=P(("chip", "core"), "head"),
        check_vma=False,
    )
```

```python
import functools

import jax
import jax.numpy as jnp
from jax import lax
from jax.experimental import pallas as pl
from jax.experimental.pallas import tpu as pltpu
from jax.sharding import Mesh
from jax.sharding import PartitionSpec as P

HEAD_DIM = 128
SWAP = [(0, 1), (1, 0)]


def exclusive_prefix(state, axis, size):
    total = state
    shift = 1
    while shift < size:
        pairs = [(i, i + shift) for i in range(size - shift)]
        total = total + lax.ppermute(total, axis, pairs)
        shift *= 2
    return total - state


def pair_order(own, other, place, axis):
    first = jnp.where(place == 0, own, other)
    second = jnp.where(place == 0, other, own)
    return jnp.concatenate([first, second], axis=axis)


def head_blocks(arrays, n_head, place):
    if n_head == 2:
        width = arrays[0].shape[1] // 2
        own = [lax.dynamic_slice_in_dim(a, place * width, width, 1) for a in arrays]
        sent = [lax.dynamic_slice_in_dim(a, (1 - place) * width, width, 1) for a in arrays]
        other = lax.ppermute(tuple(sent), "head", SWAP)
        return [pair_order(o, r, place, 0) for o, r in zip(own, other)]
    return [
        lax.all_to_all(a, "head", split_axis=1, concat_axis=0, tiled=True) for a in arrays
    ]


def chip_cycle(devices):
    n = devices.shape[0]
    coords = [getattr(devices[j, 0, 0], "coords", None) for j in range(n)]
    if n < 4 or n > 16 or any(c is None for c in coords):
        return None

    def adjacent(a, b):
        return sum(abs(int(u) - int(v)) for u, v in zip(coords[a], coords[b])) == 1

    path = [0]

    def search():
        if len(path) == n:
            return adjacent(path[-1], path[0])
        for k in range(n):
            if k not in path and adjacent(path[-1], k):
                path.append(k)
                if search():
                    return True
                path.pop()
        return False

    return list(path) if search() else None


def ring_links(order):
    n = len(order)
    forward = [(order[i], order[(i + 1) % n]) for i in range(n)]
    backward = [(order[(i + 1) % n], order[i]) for i in range(n)]
    return forward, backward


def ring_step(ahead, behind, order, last=False):
    forward, backward = ring_links(order)
    if last:
        half_rows = ahead.shape[0] // 2
        return lax.ppermute(ahead[:half_rows], "chip", forward), lax.ppermute(
            behind[half_rows:], "chip", backward
        )
    return lax.ppermute(ahead, "chip", forward), lax.ppermute(behind, "chip", backward)


def within_block_part(query_heads, key_heads, value_heads):
    row_count = query_heads.shape[0]
    block_rows = min(512, row_count)
    parts_list = []
    for first_row in range(0, row_count, block_rows):
        last_row = min(first_row + block_rows, row_count)
        scores = jnp.einsum(
            "thd,shd->hts",
            query_heads[first_row:last_row],
            key_heads[:last_row],
            preferred_element_type=jnp.float32,
        )
        row_index = first_row + lax.broadcasted_iota(jnp.int32, (last_row - first_row, last_row), 0)
        col_index = lax.broadcasted_iota(jnp.int32, (last_row - first_row, last_row), 1)
        scores = jnp.where((col_index <= row_index)[None], scores, jnp.zeros_like(scores)).astype(
            jnp.bfloat16
        )
        parts_list.append(
            jnp.einsum(
                "hts,she->the", scores, value_heads[:last_row], preferred_element_type=jnp.float32
            )
        )
    return jnp.concatenate(parts_list, axis=0)


def normalize(query_heads, prefix, within_block, norm_gain):
    heads_dev = query_heads.shape[1]
    carried = jnp.einsum(
        "thd,hde->the", query_heads, prefix.astype(jnp.bfloat16), preferred_element_type=jnp.float32
    )
    attended = carried + within_block
    mean_square = jnp.mean(attended * attended, axis=2, keepdims=True)
    gain_heads = norm_gain.reshape(heads_dev, HEAD_DIM)
    normed = (attended * lax.rsqrt(mean_square + 1e-06) * gain_heads[None]).astype(jnp.bfloat16)
    return normed.reshape(query_heads.shape[0], heads_dev * HEAD_DIM)


def gather_head(normed, n_head, place):
    if n_head == 2:
        other = lax.ppermute(normed, "head", SWAP)
        return pair_order(normed, other, place, 1)
    return lax.all_gather(normed, "head", axis=1, tiled=True)


def chip_scan(kv_state, core, n_chip):
    partner_state = lax.ppermute(kv_state, "core", SWAP)
    chip_state = kv_state + partner_state
    half = kv_state.shape[0] // 2
    chip_half = lax.dynamic_slice_in_dim(chip_state, core * half, half, 0)
    return partner_state, chip_half


def chip_finish(chip_prefix_half, partner_state, core):
    other_half = lax.ppermute(chip_prefix_half, "core", SWAP)
    chip_prefix = pair_order(chip_prefix_half, other_half, core, 0)
    return chip_prefix + jnp.where(core == 1, partner_state, jnp.zeros_like(partner_state))


def split_heads(block, heads_dev):
    return block.reshape(block.shape[0], heads_dev, HEAD_DIM)


def project_blocks(normed, starts, blocks, group=4, out_dtype=jnp.bfloat16):
    n = len(blocks)
    rows, cols = blocks[0].shape
    tokens = normed.shape[0]

    def kernel(starts_ref, normed_ref, *refs):
        block_refs = refs[:n]
        out_ref, features, weights, sems, acc = refs[n:]
        copies = []
        for i in range(n):
            start = pl.multiple_of(starts_ref[i], rows)
            copies.append(
                (
                    pltpu.make_async_copy(
                        normed_ref.at[:, pl.ds(start, rows)],
                        features.at[:, pl.ds(i * rows, rows)],
                        sems.at[0, i],
                    ),
                    pltpu.make_async_copy(
                        block_refs[i], weights.at[pl.ds(i * rows, rows), :], sems.at[1, i]
                    ),
                )
            )
        for pair in copies:
            for c in pair:
                c.start()
        for g in range(0, n, group):
            last = min(g + group, n)
            for i in range(g, last):
                for c in copies[i]:
                    c.wait()
            part = jnp.dot(
                features[:, g * rows:last * rows],
                weights[g * rows:last * rows, :],
                preferred_element_type=jnp.float32,
            )
            if g == 0:
                acc[...] = part
            else:
                acc[...] += part
        out_ref[...] = acc[...].astype(out_ref.dtype)

    return pl.pallas_call(
        kernel,
        out_shape=jax.ShapeDtypeStruct((tokens, cols), out_dtype),
        in_specs=[pl.BlockSpec(memory_space=pltpu.SMEM), pl.BlockSpec(memory_space=pl.ANY)]
        + [pl.BlockSpec(memory_space=pl.ANY)] * n,
        out_specs=pl.BlockSpec(memory_space=pltpu.VMEM),
        scratch_shapes=[
            pltpu.VMEM((tokens, n * rows), normed.dtype),
            pltpu.VMEM((n * rows, cols), blocks[0].dtype),
            pltpu.SemaphoreType.DMA((2, n)),
            pltpu.VMEM((tokens, cols), jnp.float32),
        ],
    )(starts, normed, *blocks)


def local_gather(queries, keys, values, out_weight, norm_gain, n_chip, n_head):
    heads_dev = norm_gain.shape[0] // HEAD_DIM
    core = lax.axis_index("core")
    place = lax.axis_index("head") if n_head == 2 else 0
    weight_own = lax.all_gather(out_weight, "chip", axis=0, tiled=True)
    query_block, key_block, value_block = head_blocks([queries, keys, values], n_head, place)
    query_heads, key_heads, value_heads = (
        split_heads(b, heads_dev) for b in (query_block, key_block, value_block)
    )
    kv_state = jnp.einsum(
        "thd,the->hde", key_heads, value_heads, preferred_element_type=jnp.float32
    )
    partner_state, chip_half = chip_scan(kv_state, core, n_chip)
    prefix = chip_finish(exclusive_prefix(chip_half, "chip", n_chip), partner_state, core)
    within_block = within_block_part(query_heads, key_heads, value_heads)
    normed = normalize(query_heads, prefix, within_block, norm_gain)
    gathered = gather_head(normed, n_head, place)
    row_count = gathered.shape[0]
    split = gathered.reshape(row_count, n_chip, 2, out_weight.shape[0])
    weight_own, split = lax.optimization_barrier((weight_own, split))
    weight_other = lax.ppermute(weight_own, "core", SWAP)
    normed_own = lax.dynamic_index_in_dim(split, core, 2, False).reshape(row_count, -1)
    normed_other = lax.dynamic_index_in_dim(split, 1 - core, 2, False).reshape(row_count, -1)
    outcome = jnp.dot(normed_own, weight_own, preferred_element_type=jnp.float32)
    outcome = outcome + jnp.dot(normed_other, weight_other, preferred_element_type=jnp.float32)
    return outcome.astype(jnp.bfloat16)


def local_ring(queries, keys, values, out_weight, norm_gain, n_chip, n_head, order):
    heads_dev = norm_gain.shape[0] // HEAD_DIM
    core = lax.axis_index("core")
    place = lax.axis_index("head")
    n_steps = n_chip // 2
    barrier = lax.optimization_barrier
    key_block, value_block = head_blocks([keys, values], n_head, place)
    ahead, behind = ring_step(out_weight, out_weight, order)
    ahead, behind, key_block, value_block = barrier((ahead, behind, key_block, value_block))
    got = [out_weight, ahead, behind]
    offsets = [0, 1, -1]
    (query_block,) = head_blocks([queries], n_head, place)
    swapped = [lax.ppermute(w, "core", SWAP) for w in got]
    key_heads, value_heads = split_heads(key_block, heads_dev), split_heads(value_block, heads_dev)
    kv_state = jnp.einsum(
        "thd,the->hde", key_heads, value_heads, preferred_element_type=jnp.float32
    )
    partner_state, chip_half = chip_scan(kv_state, core, n_chip)
    chip_prefix_half = exclusive_prefix(chip_half, "chip", n_chip)
    query_heads = split_heads(query_block, heads_dev)
    within_block = within_block_part(query_heads, key_heads, value_heads)
    swapped += [lax.ppermute(w, "core", SWAP) for w in got[len(swapped):]]
    chip_prefix_half, within_block, swapped = barrier((chip_prefix_half, within_block, swapped))
    for step in range(2, n_steps):
        if step >= 4:
            early = len(got) - 2
            swapped += [lax.ppermute(w, "core", SWAP) for w in got[len(swapped):early]]
            ahead, behind, swapped = barrier((ahead, behind, swapped))
        ahead, behind = ring_step(ahead, behind, order)
        got += [ahead, behind]
        offsets += [step, -step]
    swapped += [lax.ppermute(w, "core", SWAP) for w in got[len(swapped):]]
    last_ahead, last_behind = ring_step(ahead, behind, order, last=True)
    offsets.append(n_steps)
    prefix = chip_finish(chip_prefix_half, partner_state, core)
    normed = normalize(query_heads, prefix, within_block, norm_gain)
    gathered = gather_head(normed, n_head, place)
    row_count = gathered.shape[0]
    ring_place = jnp.asarray([order.index(j) for j in range(n_chip)], jnp.int32)[lax.axis_index("chip")]
    sources = jnp.asarray(order, jnp.int32)[(ring_place - jnp.asarray(offsets, jnp.int32)) % n_chip]
    cores = jnp.stack([core, 1 - core]).astype(jnp.int32)
    weight_rows = out_weight.shape[0]
    starts = ((sources[:, None] * 2 + cores[None, :]) * weight_rows).reshape(-1)
    partial = project_blocks(
        gathered,
        starts[:-2],
        [w for pair in zip(got, swapped) for w in pair],
        out_dtype=jnp.float32,
    )
    partial, last_ahead, last_behind = barrier((partial, last_ahead, last_behind))
    last_own = jnp.concatenate([last_ahead, last_behind], 0)
    last_other = lax.ppermute(last_own, "core", SWAP)
    features = [lax.dynamic_slice_in_dim(gathered, starts[-2 + k], weight_rows, 1) for k in range(2)]
    outcome = partial + jnp.dot(features[0], last_own, preferred_element_type=jnp.float32)
    outcome = outcome + jnp.dot(features[1], last_other, preferred_element_type=jnp.float32)
    return outcome.astype(jnp.bfloat16)


def solution(mesh):
    n_seq = mesh.shape["seq"]
    n_head = mesh.shape["head"]
    fine = Mesh(mesh.devices.reshape(n_seq // 2, 2, n_head), ("chip", "core", "head"))
    rows = ("chip", "core", "head")
    order = chip_cycle(fine.devices) if n_head == 2 else None
    if order is None:
        body = functools.partial(local_gather, n_chip=n_seq // 2, n_head=n_head)
    else:
        body = functools.partial(local_ring, n_chip=n_seq // 2, n_head=n_head, order=order)
    return jax.shard_map(
        body,
        mesh=fine,
        in_specs=(
            P(rows, None),
            P(rows, None),
            P(rows, None),
            P(("chip", "core"), "head"),
            P("head"),
        ),
        out_specs=P(("chip", "core"), "head"),
        check_vma=False,
    )
```

```python
import functools

import jax
import jax.numpy as jnp
from jax import lax
from jax.experimental import pallas as pl
from jax.experimental.pallas import tpu as pltpu
from jax.sharding import Mesh
from jax.sharding import PartitionSpec as P

HEAD_DIM = 128
SWAP = [(0, 1), (1, 0)]


def exclusive_prefix(state, axis, size):
    total = state
    shift = 1
    while shift < size:
        pairs = [(i, i + shift) for i in range(size - shift)]
        total = total + lax.ppermute(total, axis, pairs)
        shift *= 2
    return total - state


def pair_order(own, other, place, axis):
    first = jnp.where(place == 0, own, other)
    second = jnp.where(place == 0, other, own)
    return jnp.concatenate([first, second], axis=axis)


def head_blocks(arrays, n_head, place):
    if n_head == 2:
        rows = arrays[0].shape[0]
        width = arrays[0].shape[1] // 2
        stacked = jnp.stack(arrays).reshape(len(arrays), rows, 2, width)
        own = lax.dynamic_index_in_dim(stacked, place, 2, False)
        sent = lax.dynamic_index_in_dim(stacked, 1 - place, 2, False)
        other = lax.ppermute(sent, "head", SWAP)
        block = pair_order(own, other, place, 1)
        return [block[i] for i in range(len(arrays))]
    return [
        lax.all_to_all(a, "head", split_axis=1, concat_axis=0, tiled=True) for a in arrays
    ]


def chip_cycle(devices):
    n = devices.shape[0]
    coords = [getattr(devices[j, 0, 0], "coords", None) for j in range(n)]
    if n < 4 or n > 16 or any(c is None for c in coords):
        return None

    def adjacent(a, b):
        return sum(abs(int(u) - int(v)) for u, v in zip(coords[a], coords[b])) == 1

    path = [0]

    def search():
        if len(path) == n:
            return adjacent(path[-1], path[0])
        for k in range(n):
            if k not in path and adjacent(path[-1], k):
                path.append(k)
                if search():
                    return True
                path.pop()
        return False

    return list(path) if search() else None


def ring_links(order):
    n = len(order)
    forward = [(order[i], order[(i + 1) % n]) for i in range(n)]
    backward = [(order[(i + 1) % n], order[i]) for i in range(n)]
    return forward, backward


def ring_step(ahead, behind, order, last=False):
    forward, backward = ring_links(order)
    if last:
        half_rows = ahead.shape[0] // 2
        return lax.ppermute(ahead[:half_rows], "chip", forward), lax.ppermute(
            behind[half_rows:], "chip", backward
        )
    return lax.ppermute(ahead, "chip", forward), lax.ppermute(behind, "chip", backward)


def within_block_part(query_heads, key_heads, value_heads):
    row_count = query_heads.shape[0]
    block_rows = min(512, row_count)
    parts_list = []
    for first_row in range(0, row_count, block_rows):
        last_row = min(first_row + block_rows, row_count)
        scores = jnp.einsum(
            "thd,shd->hts",
            query_heads[first_row:last_row],
            key_heads[:last_row],
            preferred_element_type=jnp.float32,
        )
        row_index = first_row + lax.broadcasted_iota(jnp.int32, (last_row - first_row, last_row), 0)
        col_index = lax.broadcasted_iota(jnp.int32, (last_row - first_row, last_row), 1)
        scores = jnp.where((col_index <= row_index)[None], scores, jnp.zeros_like(scores)).astype(
            jnp.bfloat16
        )
        parts_list.append(
            jnp.einsum(
                "hts,she->the", scores, value_heads[:last_row], preferred_element_type=jnp.float32
            )
        )
    return jnp.concatenate(parts_list, axis=0)


def normalize(query_heads, prefix, within_block, norm_gain):
    heads_dev = query_heads.shape[1]
    carried = jnp.einsum(
        "thd,hde->the", query_heads, prefix.astype(jnp.bfloat16), preferred_element_type=jnp.float32
    )
    attended = carried + within_block
    mean_square = jnp.mean(attended * attended, axis=2, keepdims=True)
    gain_heads = norm_gain.reshape(heads_dev, HEAD_DIM)
    normed = (attended * lax.rsqrt(mean_square + 1e-06) * gain_heads[None]).astype(jnp.bfloat16)
    return normed.reshape(query_heads.shape[0], heads_dev * HEAD_DIM)


def gather_head(normed, n_head, place):
    if n_head == 2:
        other = lax.ppermute(normed, "head", SWAP)
        return pair_order(normed, other, place, 1)
    return lax.all_gather(normed, "head", axis=1, tiled=True)


def chip_scan(kv_state, core, n_chip):
    partner_state = lax.ppermute(kv_state, "core", SWAP)
    chip_state = kv_state + partner_state
    half = kv_state.shape[0] // 2
    chip_half = lax.dynamic_slice_in_dim(chip_state, core * half, half, 0)
    return partner_state, chip_half


def chip_finish(chip_prefix_half, partner_state, core):
    other_half = lax.ppermute(chip_prefix_half, "core", SWAP)
    chip_prefix = pair_order(chip_prefix_half, other_half, core, 0)
    return chip_prefix + jnp.where(core == 1, partner_state, jnp.zeros_like(partner_state))


def split_heads(block, heads_dev):
    return block.reshape(block.shape[0], heads_dev, HEAD_DIM)


def project_blocks(normed, starts, blocks, group=4):
    n = len(blocks)
    rows, cols = blocks[0].shape
    tokens = normed.shape[0]

    def kernel(starts_ref, normed_ref, *refs):
        block_refs = refs[:n]
        out_ref, features, weights, sems, acc = refs[n:]
        copies = []
        for i in range(n):
            start = pl.multiple_of(starts_ref[i], rows)
            copies.append(
                (
                    pltpu.make_async_copy(
                        normed_ref.at[:, pl.ds(start, rows)],
                        features.at[:, pl.ds(i * rows, rows)],
                        sems.at[0, i],
                    ),
                    pltpu.make_async_copy(
                        block_refs[i], weights.at[pl.ds(i * rows, rows), :], sems.at[1, i]
                    ),
                )
            )
        for pair in copies:
            for c in pair:
                c.start()
        for g in range(0, n, group):
            last = min(g + group, n)
            for i in range(g, last):
                for c in copies[i]:
                    c.wait()
            part = jnp.dot(
                features[:, g * rows:last * rows],
                weights[g * rows:last * rows, :],
                preferred_element_type=jnp.float32,
            )
            if g == 0:
                acc[...] = part
            else:
                acc[...] += part
        out_ref[...] = acc[...].astype(out_ref.dtype)

    return pl.pallas_call(
        kernel,
        out_shape=jax.ShapeDtypeStruct((tokens, cols), jnp.bfloat16),
        in_specs=[pl.BlockSpec(memory_space=pltpu.SMEM), pl.BlockSpec(memory_space=pl.ANY)]
        + [pl.BlockSpec(memory_space=pl.ANY)] * n,
        out_specs=pl.BlockSpec(memory_space=pltpu.VMEM),
        scratch_shapes=[
            pltpu.VMEM((tokens, n * rows), normed.dtype),
            pltpu.VMEM((n * rows, cols), blocks[0].dtype),
            pltpu.SemaphoreType.DMA((2, n)),
            pltpu.VMEM((tokens, cols), jnp.float32),
        ],
    )(starts, normed, *blocks)


def local_gather(queries, keys, values, out_weight, norm_gain, n_chip, n_head):
    heads_dev = norm_gain.shape[0] // HEAD_DIM
    core = lax.axis_index("core")
    place = lax.axis_index("head") if n_head == 2 else 0
    weight_own = lax.all_gather(out_weight, "chip", axis=0, tiled=True)
    query_block, key_block, value_block = head_blocks([queries, keys, values], n_head, place)
    query_heads, key_heads, value_heads = (
        split_heads(b, heads_dev) for b in (query_block, key_block, value_block)
    )
    kv_state = jnp.einsum(
        "thd,the->hde", key_heads, value_heads, preferred_element_type=jnp.float32
    )
    partner_state, chip_half = chip_scan(kv_state, core, n_chip)
    prefix = chip_finish(exclusive_prefix(chip_half, "chip", n_chip), partner_state, core)
    within_block = within_block_part(query_heads, key_heads, value_heads)
    normed = normalize(query_heads, prefix, within_block, norm_gain)
    gathered = gather_head(normed, n_head, place)
    row_count = gathered.shape[0]
    split = gathered.reshape(row_count, n_chip, 2, out_weight.shape[0])
    weight_own, split = lax.optimization_barrier((weight_own, split))
    weight_other = lax.ppermute(weight_own, "core", SWAP)
    normed_own = lax.dynamic_index_in_dim(split, core, 2, False).reshape(row_count, -1)
    normed_other = lax.dynamic_index_in_dim(split, 1 - core, 2, False).reshape(row_count, -1)
    outcome = jnp.dot(normed_own, weight_own, preferred_element_type=jnp.float32)
    outcome = outcome + jnp.dot(normed_other, weight_other, preferred_element_type=jnp.float32)
    return outcome.astype(jnp.bfloat16)


def ring_halves(ahead, behind, order, last=False):
    forward, backward = ring_links(order)
    if last:
        return (lax.ppermute(ahead[0], "chip", forward), lax.ppermute(behind[1], "chip", backward))
    return lax.ppermute(ahead, "chip", forward), lax.ppermute(behind, "chip", backward)


def local_ring(queries, keys, values, out_weight, norm_gain, n_chip, n_head, order):
    heads_dev = norm_gain.shape[0] // HEAD_DIM
    core = lax.axis_index("core")
    place = lax.axis_index("head")
    n_steps = n_chip // 2
    barrier = lax.optimization_barrier
    weight_rows = out_weight.shape[0]
    half_rows = weight_rows // 2
    halves = (out_weight[:half_rows], out_weight[half_rows:])
    key_block, value_block = head_blocks([keys, values], n_head, place)
    ahead, behind = ring_halves(halves, halves, order)
    ahead, behind, key_block, value_block = barrier((ahead, behind, key_block, value_block))
    got = [halves, ahead, behind]
    offsets = [0, 1, -1]
    (query_block,) = head_blocks([queries], n_head, place)
    swapped = [lax.ppermute(w, "core", SWAP) for w in got]
    key_heads, value_heads = split_heads(key_block, heads_dev), split_heads(value_block, heads_dev)
    kv_state = jnp.einsum(
        "thd,the->hde", key_heads, value_heads, preferred_element_type=jnp.float32
    )
    partner_state, chip_half = chip_scan(kv_state, core, n_chip)
    chip_prefix_half = exclusive_prefix(chip_half, "chip", n_chip)
    query_heads = split_heads(query_block, heads_dev)
    within_block = within_block_part(query_heads, key_heads, value_heads)
    chip_prefix_half, within_block, swapped = barrier((chip_prefix_half, within_block, swapped))
    for step in range(2, n_steps + 1):
        ahead, behind = ring_halves(ahead, behind, order, last=step == n_steps)
        if step == n_steps:
            got.append((ahead, behind))
            offsets.append(step)
        else:
            got += [ahead, behind]
            offsets += [step, -step]
    swapped += [lax.ppermute(w, "core", SWAP) for w in got[len(swapped):]]
    prefix = chip_finish(chip_prefix_half, partner_state, core)
    normed = normalize(query_heads, prefix, within_block, norm_gain)
    gathered = gather_head(normed, n_head, place)
    ring_place = jnp.asarray([order.index(j) for j in range(n_chip)], jnp.int32)[lax.axis_index("chip")]
    sources = jnp.asarray(order, jnp.int32)[(ring_place - jnp.asarray(offsets, jnp.int32)) % n_chip]
    cores = jnp.stack([core, 1 - core]).astype(jnp.int32)
    parts = jnp.asarray([0, half_rows], jnp.int32)
    starts = (
        (sources[:, None, None] * 2 + cores[None, :, None]) * weight_rows + parts[None, None, :]
    ).reshape(-1)
    blocks = [h for own, other in zip(got, swapped) for pair in (own, other) for h in pair]
    return project_blocks(gathered, starts, blocks, group=8)


def solution(mesh):
    n_seq = mesh.shape["seq"]
    n_head = mesh.shape["head"]
    fine = Mesh(mesh.devices.reshape(n_seq // 2, 2, n_head), ("chip", "core", "head"))
    rows = ("chip", "core", "head")
    order = chip_cycle(fine.devices) if n_head == 2 else None
    if order is None:
        body = functools.partial(local_gather, n_chip=n_seq // 2, n_head=n_head)
    else:
        body = functools.partial(local_ring, n_chip=n_seq // 2, n_head=n_head, order=order)
    return jax.shard_map(
        body,
        mesh=fine,
        in_specs=(
            P(rows, None),
            P(rows, None),
            P(rows, None),
            P(("chip", "core"), "head"),
            P("head"),
        ),
        out_specs=P(("chip", "core"), "head"),
        check_vma=False,
    )
```

```python
import functools

import jax
import jax.numpy as jnp
from jax import lax
from jax.experimental import pallas as pl
from jax.experimental.pallas import tpu as pltpu
from jax.sharding import Mesh
from jax.sharding import PartitionSpec as P

HEAD_DIM = 128
SWAP = [(0, 1), (1, 0)]


def exclusive_prefix(state, axis, size):
    total = state
    shift = 1
    while shift < size:
        pairs = [(i, i + shift) for i in range(size - shift)]
        total = total + lax.ppermute(total, axis, pairs)
        shift *= 2
    return total - state


def pair_order(own, other, place, axis):
    first = jnp.where(place == 0, own, other)
    second = jnp.where(place == 0, other, own)
    return jnp.concatenate([first, second], axis=axis)


def head_blocks(arrays, n_head, place):
    if n_head == 2:
        rows = arrays[0].shape[0]
        width = arrays[0].shape[1] // 2
        stacked = jnp.stack(arrays).reshape(len(arrays), rows, 2, width)
        own = lax.dynamic_index_in_dim(stacked, place, 2, False)
        sent = lax.dynamic_index_in_dim(stacked, 1 - place, 2, False)
        other = lax.ppermute(sent, "head", SWAP)
        block = pair_order(own, other, place, 1)
        return [block[i] for i in range(len(arrays))]
    return [
        lax.all_to_all(a, "head", split_axis=1, concat_axis=0, tiled=True) for a in arrays
    ]


def chip_cycle(devices):
    n = devices.shape[0]
    coords = [getattr(devices[j, 0, 0], "coords", None) for j in range(n)]
    if n < 4 or n > 16 or any(c is None for c in coords):
        return None

    def adjacent(a, b):
        return sum(abs(int(u) - int(v)) for u, v in zip(coords[a], coords[b])) == 1

    path = [0]

    def search():
        if len(path) == n:
            return adjacent(path[-1], path[0])
        for k in range(n):
            if k not in path and adjacent(path[-1], k):
                path.append(k)
                if search():
                    return True
                path.pop()
        return False

    return list(path) if search() else None


def ring_links(order):
    n = len(order)
    forward = [(order[i], order[(i + 1) % n]) for i in range(n)]
    backward = [(order[(i + 1) % n], order[i]) for i in range(n)]
    return forward, backward


def ring_step(ahead, behind, order, last=False):
    forward, backward = ring_links(order)
    if last:
        half_rows = ahead.shape[0] // 2
        return lax.ppermute(ahead[:half_rows], "chip", forward), lax.ppermute(
            behind[half_rows:], "chip", backward
        )
    return lax.ppermute(ahead, "chip", forward), lax.ppermute(behind, "chip", backward)


def within_block_part(query_heads, key_heads, value_heads):
    row_count = query_heads.shape[0]
    block_rows = min(512, row_count)
    parts_list = []
    for first_row in range(0, row_count, block_rows):
        last_row = min(first_row + block_rows, row_count)
        scores = jnp.einsum(
            "thd,shd->hts",
            query_heads[first_row:last_row],
            key_heads[:last_row],
            preferred_element_type=jnp.float32,
        )
        row_index = first_row + lax.broadcasted_iota(jnp.int32, (last_row - first_row, last_row), 0)
        col_index = lax.broadcasted_iota(jnp.int32, (last_row - first_row, last_row), 1)
        scores = jnp.where((col_index <= row_index)[None], scores, jnp.zeros_like(scores)).astype(
            jnp.bfloat16
        )
        parts_list.append(
            jnp.einsum(
                "hts,she->the", scores, value_heads[:last_row], preferred_element_type=jnp.float32
            )
        )
    return jnp.concatenate(parts_list, axis=0)


def normalize(query_heads, prefix, within_block, norm_gain):
    heads_dev = query_heads.shape[1]
    carried = jnp.einsum(
        "thd,hde->the", query_heads, prefix.astype(jnp.bfloat16), preferred_element_type=jnp.float32
    )
    attended = carried + within_block
    mean_square = jnp.mean(attended * attended, axis=2, keepdims=True)
    gain_heads = norm_gain.reshape(heads_dev, HEAD_DIM)
    normed = (attended * lax.rsqrt(mean_square + 1e-06) * gain_heads[None]).astype(jnp.bfloat16)
    return normed.reshape(query_heads.shape[0], heads_dev * HEAD_DIM)


def gather_head(normed, n_head, place):
    if n_head == 2:
        other = lax.ppermute(normed, "head", SWAP)
        return pair_order(normed, other, place, 1)
    return lax.all_gather(normed, "head", axis=1, tiled=True)


def chip_scan(kv_state, core, n_chip):
    partner_state = lax.ppermute(kv_state, "core", SWAP)
    chip_state = kv_state + partner_state
    half = kv_state.shape[0] // 2
    chip_half = lax.dynamic_slice_in_dim(chip_state, core * half, half, 0)
    return partner_state, chip_half


def chip_finish(chip_prefix_half, partner_state, core):
    other_half = lax.ppermute(chip_prefix_half, "core", SWAP)
    chip_prefix = pair_order(chip_prefix_half, other_half, core, 0)
    return chip_prefix + jnp.where(core == 1, partner_state, jnp.zeros_like(partner_state))


def split_heads(block, heads_dev):
    return block.reshape(block.shape[0], heads_dev, HEAD_DIM)


def project_blocks(normed, starts, blocks, group=4):
    n = len(blocks)
    rows, cols = blocks[0].shape
    tokens = normed.shape[0]

    def kernel(starts_ref, normed_ref, *refs):
        block_refs = refs[:n]
        out_ref, features, weights, sems, acc = refs[n:]
        copies = []
        for i in range(n):
            start = pl.multiple_of(starts_ref[i], rows)
            copies.append(
                (
                    pltpu.make_async_copy(
                        normed_ref.at[:, pl.ds(start, rows)],
                        features.at[:, pl.ds(i * rows, rows)],
                        sems.at[0, i],
                    ),
                    pltpu.make_async_copy(
                        block_refs[i], weights.at[pl.ds(i * rows, rows), :], sems.at[1, i]
                    ),
                )
            )
        def start_group(g):
            for i in range(g, min(g + group, n)):
                for c in copies[i]:
                    c.start()

        start_group(0)
        start_group(group)
        for g in range(0, n, group):
            last = min(g + group, n)
            for i in range(g, last):
                for c in copies[i]:
                    c.wait()
            start_group(g + 2 * group)
            part = jnp.dot(
                features[:, g * rows:last * rows],
                weights[g * rows:last * rows, :],
                preferred_element_type=jnp.float32,
            )
            if g == 0:
                acc[...] = part
            else:
                acc[...] += part
        out_ref[...] = acc[...].astype(out_ref.dtype)

    return pl.pallas_call(
        kernel,
        out_shape=jax.ShapeDtypeStruct((tokens, cols), jnp.bfloat16),
        in_specs=[pl.BlockSpec(memory_space=pltpu.SMEM), pl.BlockSpec(memory_space=pl.ANY)]
        + [pl.BlockSpec(memory_space=pl.ANY)] * n,
        out_specs=pl.BlockSpec(memory_space=pltpu.VMEM),
        scratch_shapes=[
            pltpu.VMEM((tokens, n * rows), normed.dtype),
            pltpu.VMEM((n * rows, cols), blocks[0].dtype),
            pltpu.SemaphoreType.DMA((2, n)),
            pltpu.VMEM((tokens, cols), jnp.float32),
        ],
    )(starts, normed, *blocks)


def local_gather(queries, keys, values, out_weight, norm_gain, n_chip, n_head):
    heads_dev = norm_gain.shape[0] // HEAD_DIM
    core = lax.axis_index("core")
    place = lax.axis_index("head") if n_head == 2 else 0
    weight_own = lax.all_gather(out_weight, "chip", axis=0, tiled=True)
    query_block, key_block, value_block = head_blocks([queries, keys, values], n_head, place)
    query_heads, key_heads, value_heads = (
        split_heads(b, heads_dev) for b in (query_block, key_block, value_block)
    )
    kv_state = jnp.einsum(
        "thd,the->hde", key_heads, value_heads, preferred_element_type=jnp.float32
    )
    partner_state, chip_half = chip_scan(kv_state, core, n_chip)
    prefix = chip_finish(exclusive_prefix(chip_half, "chip", n_chip), partner_state, core)
    within_block = within_block_part(query_heads, key_heads, value_heads)
    normed = normalize(query_heads, prefix, within_block, norm_gain)
    gathered = gather_head(normed, n_head, place)
    row_count = gathered.shape[0]
    split = gathered.reshape(row_count, n_chip, 2, out_weight.shape[0])
    weight_own, split = lax.optimization_barrier((weight_own, split))
    weight_other = lax.ppermute(weight_own, "core", SWAP)
    normed_own = lax.dynamic_index_in_dim(split, core, 2, False).reshape(row_count, -1)
    normed_other = lax.dynamic_index_in_dim(split, 1 - core, 2, False).reshape(row_count, -1)
    outcome = jnp.dot(normed_own, weight_own, preferred_element_type=jnp.float32)
    outcome = outcome + jnp.dot(normed_other, weight_other, preferred_element_type=jnp.float32)
    return outcome.astype(jnp.bfloat16)


def local_ring(queries, keys, values, out_weight, norm_gain, n_chip, n_head, order):
    heads_dev = norm_gain.shape[0] // HEAD_DIM
    core = lax.axis_index("core")
    place = lax.axis_index("head")
    n_steps = n_chip // 2
    barrier = lax.optimization_barrier
    key_block, value_block = head_blocks([keys, values], n_head, place)
    ahead, behind = ring_step(out_weight, out_weight, order)
    ahead, behind, key_block, value_block = barrier((ahead, behind, key_block, value_block))
    got = [out_weight, ahead, behind]
    offsets = [0, 1, -1]
    (query_block,) = head_blocks([queries], n_head, place)
    swapped = [lax.ppermute(w, "core", SWAP) for w in got]
    key_heads, value_heads = split_heads(key_block, heads_dev), split_heads(value_block, heads_dev)
    kv_state = jnp.einsum(
        "thd,the->hde", key_heads, value_heads, preferred_element_type=jnp.float32
    )
    partner_state, chip_half = chip_scan(kv_state, core, n_chip)
    chip_prefix_half = exclusive_prefix(chip_half, "chip", n_chip)
    query_heads = split_heads(query_block, heads_dev)
    within_block = within_block_part(query_heads, key_heads, value_heads)
    swapped += [lax.ppermute(w, "core", SWAP) for w in got[len(swapped):]]
    chip_prefix_half, within_block, swapped = barrier((chip_prefix_half, within_block, swapped))
    for step in range(2, n_steps + 1):
        ahead, behind = ring_step(ahead, behind, order, last=step == n_steps)
        if step == n_steps:
            got.append(jnp.concatenate([ahead, behind], 0))
            offsets.append(step)
        else:
            got += [ahead, behind]
            offsets += [step, -step]
    swapped += [lax.ppermute(w, "core", SWAP) for w in got[len(swapped):]]
    prefix = chip_finish(chip_prefix_half, partner_state, core)
    normed = normalize(query_heads, prefix, within_block, norm_gain)
    gathered = gather_head(normed, n_head, place)
    row_count = gathered.shape[0]
    ring_place = jnp.asarray([order.index(j) for j in range(n_chip)], jnp.int32)[lax.axis_index("chip")]
    sources = jnp.asarray(order, jnp.int32)[(ring_place - jnp.asarray(offsets, jnp.int32)) % n_chip]
    cores = jnp.stack([core, 1 - core]).astype(jnp.int32)
    starts = ((sources[:, None] * 2 + cores[None, :]) * out_weight.shape[0]).reshape(-1)
    return project_blocks(gathered, starts, [w for pair in zip(got, swapped) for w in pair])


def solution(mesh):
    n_seq = mesh.shape["seq"]
    n_head = mesh.shape["head"]
    fine = Mesh(mesh.devices.reshape(n_seq // 2, 2, n_head), ("chip", "core", "head"))
    rows = ("chip", "core", "head")
    order = chip_cycle(fine.devices) if n_head == 2 else None
    if order is None:
        body = functools.partial(local_gather, n_chip=n_seq // 2, n_head=n_head)
    else:
        body = functools.partial(local_ring, n_chip=n_seq // 2, n_head=n_head, order=order)
    return jax.shard_map(
        body,
        mesh=fine,
        in_specs=(
            P(rows, None),
            P(rows, None),
            P(rows, None),
            P(("chip", "core"), "head"),
            P("head"),
        ),
        out_specs=P(("chip", "core"), "head"),
        check_vma=False,
    )
```

```python
import functools

import jax
import jax.numpy as jnp
from jax import lax
from jax.experimental import pallas as pl
from jax.experimental.pallas import tpu as pltpu
from jax.sharding import Mesh
from jax.sharding import PartitionSpec as P

HEAD_DIM = 128
SWAP = [(0, 1), (1, 0)]


def exclusive_prefix(state, axis, size):
    total = state
    shift = 1
    while shift < size:
        pairs = [(i, i + shift) for i in range(size - shift)]
        total = total + lax.ppermute(total, axis, pairs)
        shift *= 2
    return total - state


def pair_order(own, other, place, axis):
    first = jnp.where(place == 0, own, other)
    second = jnp.where(place == 0, other, own)
    return jnp.concatenate([first, second], axis=axis)


def head_blocks(arrays, n_head, place):
    if n_head == 2:
        rows = arrays[0].shape[0]
        width = arrays[0].shape[1] // 2
        stacked = jnp.stack(arrays).reshape(len(arrays), rows, 2, width)
        own = lax.dynamic_index_in_dim(stacked, place, 2, False)
        sent = lax.dynamic_index_in_dim(stacked, 1 - place, 2, False)
        other = lax.ppermute(sent, "head", SWAP)
        block = pair_order(own, other, place, 1)
        return [block[i] for i in range(len(arrays))]
    return [
        lax.all_to_all(a, "head", split_axis=1, concat_axis=0, tiled=True) for a in arrays
    ]


def chip_cycle(devices):
    n = devices.shape[0]
    coords = [getattr(devices[j, 0, 0], "coords", None) for j in range(n)]
    if n < 4 or n > 16 or any(c is None for c in coords):
        return None

    def adjacent(a, b):
        return sum(abs(int(u) - int(v)) for u, v in zip(coords[a], coords[b])) == 1

    path = [0]

    def search():
        if len(path) == n:
            return adjacent(path[-1], path[0])
        for k in range(n):
            if k not in path and adjacent(path[-1], k):
                path.append(k)
                if search():
                    return True
                path.pop()
        return False

    return list(path) if search() else None


def ring_links(order):
    n = len(order)
    forward = [(order[i], order[(i + 1) % n]) for i in range(n)]
    backward = [(order[(i + 1) % n], order[i]) for i in range(n)]
    return forward, backward


def ring_step(ahead, behind, order, last=False):
    forward, backward = ring_links(order)
    if last:
        half_rows = ahead.shape[0] // 2
        return lax.ppermute(ahead[:half_rows], "chip", forward), lax.ppermute(
            behind[half_rows:], "chip", backward
        )
    return lax.ppermute(ahead, "chip", forward), lax.ppermute(behind, "chip", backward)


def within_block_part(query_heads, key_heads, value_heads):
    row_count = query_heads.shape[0]
    block_rows = min(512, row_count)
    parts_list = []
    for first_row in range(0, row_count, block_rows):
        last_row = min(first_row + block_rows, row_count)
        scores = jnp.einsum(
            "thd,shd->hts",
            query_heads[first_row:last_row],
            key_heads[:last_row],
            preferred_element_type=jnp.float32,
        )
        row_index = first_row + lax.broadcasted_iota(jnp.int32, (last_row - first_row, last_row), 0)
        col_index = lax.broadcasted_iota(jnp.int32, (last_row - first_row, last_row), 1)
        scores = jnp.where((col_index <= row_index)[None], scores, jnp.zeros_like(scores)).astype(
            jnp.bfloat16
        )
        parts_list.append(
            jnp.einsum(
                "hts,she->the", scores, value_heads[:last_row], preferred_element_type=jnp.float32
            )
        )
    return jnp.concatenate(parts_list, axis=0)


def normalize(query_heads, prefix, within_block, norm_gain):
    heads_dev = query_heads.shape[1]
    carried = jnp.einsum(
        "thd,hde->the", query_heads, prefix.astype(jnp.bfloat16), preferred_element_type=jnp.float32
    )
    attended = carried + within_block
    mean_square = jnp.mean(attended * attended, axis=2, keepdims=True)
    gain_heads = norm_gain.reshape(heads_dev, HEAD_DIM)
    normed = (attended * lax.rsqrt(mean_square + 1e-06) * gain_heads[None]).astype(jnp.bfloat16)
    return normed.reshape(query_heads.shape[0], heads_dev * HEAD_DIM)


def gather_head(normed, n_head, place):
    if n_head == 2:
        other = lax.ppermute(normed, "head", SWAP)
        return pair_order(normed, other, place, 1)
    return lax.all_gather(normed, "head", axis=1, tiled=True)


def chip_scan(kv_state, core, n_chip):
    partner_state = lax.ppermute(kv_state, "core", SWAP)
    chip_state = kv_state + partner_state
    half = kv_state.shape[0] // 2
    chip_half = lax.dynamic_slice_in_dim(chip_state, core * half, half, 0)
    return partner_state, chip_half


def chip_finish(chip_prefix_half, partner_state, core):
    other_half = lax.ppermute(chip_prefix_half, "core", SWAP)
    chip_prefix = pair_order(chip_prefix_half, other_half, core, 0)
    return chip_prefix + jnp.where(core == 1, partner_state, jnp.zeros_like(partner_state))


def split_heads(block, heads_dev):
    return block.reshape(block.shape[0], heads_dev, HEAD_DIM)


def project_blocks(normed, starts, blocks, group=4):
    n = len(blocks)
    rows, cols = blocks[0].shape
    tokens = normed.shape[0]

    def kernel(starts_ref, normed_ref, *refs):
        block_refs = refs[:n]
        out_ref, features, weights, sems, acc = refs[n:]
        copies = []
        for i in range(n):
            start = pl.multiple_of(starts_ref[i], rows)
            copies.append(
                (
                    pltpu.make_async_copy(
                        normed_ref.at[:, pl.ds(start, rows)],
                        features.at[:, pl.ds(i * rows, rows)],
                        sems.at[0, i],
                    ),
                    pltpu.make_async_copy(
                        block_refs[i], weights.at[pl.ds(i * rows, rows), :], sems.at[1, i]
                    ),
                )
            )
        for pair in copies:
            for c in pair:
                c.start()
        for g in range(0, n, group):
            last = min(g + group, n)
            for i in range(g, last):
                for c in copies[i]:
                    c.wait()
            part = jnp.dot(
                features[:, g * rows:last * rows],
                weights[g * rows:last * rows, :],
                preferred_element_type=jnp.float32,
            )
            if g == 0:
                acc[...] = part
            else:
                acc[...] += part
        out_ref[...] = acc[...].astype(out_ref.dtype)

    return pl.pallas_call(
        kernel,
        out_shape=jax.ShapeDtypeStruct((tokens, cols), jnp.bfloat16),
        in_specs=[pl.BlockSpec(memory_space=pltpu.SMEM), pl.BlockSpec(memory_space=pl.ANY)]
        + [pl.BlockSpec(memory_space=pl.ANY)] * n,
        out_specs=pl.BlockSpec(memory_space=pltpu.VMEM),
        scratch_shapes=[
            pltpu.VMEM((tokens, n * rows), normed.dtype),
            pltpu.VMEM((n * rows, cols), blocks[0].dtype),
            pltpu.SemaphoreType.DMA((2, n)),
            pltpu.VMEM((tokens, cols), jnp.float32),
        ],
    )(starts, normed, *blocks)


def local_gather(queries, keys, values, out_weight, norm_gain, n_chip, n_head):
    heads_dev = norm_gain.shape[0] // HEAD_DIM
    core = lax.axis_index("core")
    place = lax.axis_index("head") if n_head == 2 else 0
    weight_own = lax.all_gather(out_weight, "chip", axis=0, tiled=True)
    query_block, key_block, value_block = head_blocks([queries, keys, values], n_head, place)
    query_heads, key_heads, value_heads = (
        split_heads(b, heads_dev) for b in (query_block, key_block, value_block)
    )
    kv_state = jnp.einsum(
        "thd,the->hde", key_heads, value_heads, preferred_element_type=jnp.float32
    )
    partner_state, chip_half = chip_scan(kv_state, core, n_chip)
    prefix = chip_finish(exclusive_prefix(chip_half, "chip", n_chip), partner_state, core)
    within_block = within_block_part(query_heads, key_heads, value_heads)
    normed = normalize(query_heads, prefix, within_block, norm_gain)
    gathered = gather_head(normed, n_head, place)
    row_count = gathered.shape[0]
    split = gathered.reshape(row_count, n_chip, 2, out_weight.shape[0])
    weight_own, split = lax.optimization_barrier((weight_own, split))
    weight_other = lax.ppermute(weight_own, "core", SWAP)
    normed_own = lax.dynamic_index_in_dim(split, core, 2, False).reshape(row_count, -1)
    normed_other = lax.dynamic_index_in_dim(split, 1 - core, 2, False).reshape(row_count, -1)
    outcome = jnp.dot(normed_own, weight_own, preferred_element_type=jnp.float32)
    outcome = outcome + jnp.dot(normed_other, weight_other, preferred_element_type=jnp.float32)
    return outcome.astype(jnp.bfloat16)


def local_ring(queries, keys, values, out_weight, norm_gain, n_chip, n_head, order):
    heads_dev = norm_gain.shape[0] // HEAD_DIM
    core = lax.axis_index("core")
    place = lax.axis_index("head")
    n_steps = n_chip // 2
    barrier = lax.optimization_barrier
    key_block, value_block = head_blocks([keys, values], n_head, place)
    ahead, behind = ring_step(out_weight, out_weight, order)
    ahead, behind, key_block, value_block = barrier((ahead, behind, key_block, value_block))
    got = [out_weight, ahead, behind]
    offsets = [0, 1, -1]
    (query_block,) = head_blocks([queries], n_head, place)
    swapped = [lax.ppermute(w, "core", SWAP) for w in got]
    key_heads, value_heads = split_heads(key_block, heads_dev), split_heads(value_block, heads_dev)
    kv_state = jnp.einsum(
        "thd,the->hde", key_heads, value_heads, preferred_element_type=jnp.float32
    )
    partner_state, chip_half = chip_scan(kv_state, core, n_chip)
    chip_prefix_half = exclusive_prefix(chip_half, "chip", n_chip)
    query_heads = split_heads(query_block, heads_dev)
    within_block = within_block_part(query_heads, key_heads, value_heads)
    swapped += [lax.ppermute(w, "core", SWAP) for w in got[len(swapped):]]
    chip_prefix_half, within_block, swapped = barrier((chip_prefix_half, within_block, swapped))
    for step in range(2, n_steps + 1):
        ahead, behind = ring_step(ahead, behind, order, last=step == n_steps)
        if step == n_steps:
            got.append(jnp.concatenate([ahead, behind], 0))
            offsets.append(step)
        else:
            got += [ahead, behind]
            offsets += [step, -step]
    swapped += [lax.ppermute(w, "core", SWAP) for w in got[len(swapped):]]
    prefix = chip_finish(chip_prefix_half, partner_state, core)
    normed = normalize(query_heads, prefix, within_block, norm_gain)
    gathered = gather_head(normed, n_head, place)
    row_count = gathered.shape[0]
    ring_place = jnp.asarray([order.index(j) for j in range(n_chip)], jnp.int32)[lax.axis_index("chip")]
    sources = jnp.asarray(order, jnp.int32)[(ring_place - jnp.asarray(offsets, jnp.int32)) % n_chip]
    cores = jnp.stack([core, 1 - core]).astype(jnp.int32)
    starts = ((sources[:, None] * 2 + cores[None, :]) * out_weight.shape[0]).reshape(-1)
    return project_blocks(gathered, starts, [w for pair in zip(got, swapped) for w in pair], group=16)


def solution(mesh):
    n_seq = mesh.shape["seq"]
    n_head = mesh.shape["head"]
    fine = Mesh(mesh.devices.reshape(n_seq // 2, 2, n_head), ("chip", "core", "head"))
    rows = ("chip", "core", "head")
    order = chip_cycle(fine.devices) if n_head == 2 else None
    if order is None:
        body = functools.partial(local_gather, n_chip=n_seq // 2, n_head=n_head)
    else:
        body = functools.partial(local_ring, n_chip=n_seq // 2, n_head=n_head, order=order)
    return jax.shard_map(
        body,
        mesh=fine,
        in_specs=(
            P(rows, None),
            P(rows, None),
            P(rows, None),
            P(("chip", "core"), "head"),
            P("head"),
        ),
        out_specs=P(("chip", "core"), "head"),
        check_vma=False,
    )
```

```python
import functools

import jax
import jax.numpy as jnp
from jax import lax
from jax.experimental import pallas as pl
from jax.experimental.pallas import tpu as pltpu
from jax.sharding import Mesh
from jax.sharding import PartitionSpec as P

HEAD_DIM = 128
SWAP = [(0, 1), (1, 0)]


def exclusive_prefix(state, axis, size):
    total = state
    shift = 1
    while shift < size:
        pairs = [(i, i + shift) for i in range(size - shift)]
        total = total + lax.ppermute(total, axis, pairs)
        shift *= 2
    return total - state


def pair_order(own, other, place, axis):
    first = jnp.where(place == 0, own, other)
    second = jnp.where(place == 0, other, own)
    return jnp.concatenate([first, second], axis=axis)


def head_blocks(arrays, n_head, place):
    if n_head == 2:
        rows = arrays[0].shape[0]
        width = arrays[0].shape[1] // 2
        stacked = jnp.stack(arrays).reshape(len(arrays), rows, 2, width)
        own = lax.dynamic_index_in_dim(stacked, place, 2, False)
        sent = lax.dynamic_index_in_dim(stacked, 1 - place, 2, False)
        other = lax.ppermute(sent, "head", SWAP)
        block = pair_order(own, other, place, 1)
        return [block[i] for i in range(len(arrays))]
    return [
        lax.all_to_all(a, "head", split_axis=1, concat_axis=0, tiled=True) for a in arrays
    ]


def chip_cycle(devices):
    n = devices.shape[0]
    coords = [getattr(devices[j, 0, 0], "coords", None) for j in range(n)]
    if n < 4 or n > 16 or any(c is None for c in coords):
        return None

    def adjacent(a, b):
        return sum(abs(int(u) - int(v)) for u, v in zip(coords[a], coords[b])) == 1

    path = [0]

    def search():
        if len(path) == n:
            return adjacent(path[-1], path[0])
        for k in range(n):
            if k not in path and adjacent(path[-1], k):
                path.append(k)
                if search():
                    return True
                path.pop()
        return False

    return list(path) if search() else None


def ring_links(order):
    n = len(order)
    forward = [(order[i], order[(i + 1) % n]) for i in range(n)]
    backward = [(order[(i + 1) % n], order[i]) for i in range(n)]
    return forward, backward


def ring_step(ahead, behind, order, last=False):
    forward, backward = ring_links(order)
    if last:
        half_rows = ahead.shape[0] // 2
        return lax.ppermute(ahead[:half_rows], "chip", forward), lax.ppermute(
            behind[half_rows:], "chip", backward
        )
    return lax.ppermute(ahead, "chip", forward), lax.ppermute(behind, "chip", backward)


def within_block_part(query_heads, key_heads, value_heads):
    row_count = query_heads.shape[0]
    block_rows = min(512, row_count)
    parts_list = []
    for first_row in range(0, row_count, block_rows):
        last_row = min(first_row + block_rows, row_count)
        scores = jnp.einsum(
            "thd,shd->hts",
            query_heads[first_row:last_row],
            key_heads[:last_row],
            preferred_element_type=jnp.float32,
        )
        row_index = first_row + lax.broadcasted_iota(jnp.int32, (last_row - first_row, last_row), 0)
        col_index = lax.broadcasted_iota(jnp.int32, (last_row - first_row, last_row), 1)
        scores = jnp.where((col_index <= row_index)[None], scores, jnp.zeros_like(scores)).astype(
            jnp.bfloat16
        )
        parts_list.append(
            jnp.einsum(
                "hts,she->the", scores, value_heads[:last_row], preferred_element_type=jnp.float32
            )
        )
    return jnp.concatenate(parts_list, axis=0)


def normalize(query_heads, prefix, within_block, norm_gain):
    heads_dev = query_heads.shape[1]
    carried = jnp.einsum(
        "thd,hde->the", query_heads, prefix.astype(jnp.bfloat16), preferred_element_type=jnp.float32
    )
    attended = carried + within_block
    mean_square = jnp.mean(attended * attended, axis=2, keepdims=True)
    gain_heads = norm_gain.reshape(heads_dev, HEAD_DIM)
    normed = (attended * lax.rsqrt(mean_square + 1e-06) * gain_heads[None]).astype(jnp.bfloat16)
    return normed.reshape(query_heads.shape[0], heads_dev * HEAD_DIM)


def gather_head(normed, n_head, place):
    if n_head == 2:
        other = lax.ppermute(normed, "head", SWAP)
        return pair_order(normed, other, place, 1)
    return lax.all_gather(normed, "head", axis=1, tiled=True)


def chip_scan(kv_state, core, n_chip):
    partner_state = lax.ppermute(kv_state, "core", SWAP)
    chip_state = kv_state + partner_state
    half = kv_state.shape[0] // 2
    chip_half = lax.dynamic_slice_in_dim(chip_state, core * half, half, 0)
    return partner_state, chip_half


def chip_finish(chip_prefix_half, partner_state, core):
    other_half = lax.ppermute(chip_prefix_half, "core", SWAP)
    chip_prefix = pair_order(chip_prefix_half, other_half, core, 0)
    return chip_prefix + jnp.where(core == 1, partner_state, jnp.zeros_like(partner_state))


def split_heads(block, heads_dev):
    return block.reshape(block.shape[0], heads_dev, HEAD_DIM)


def project_blocks(normed, starts, blocks, group=4):
    n = len(blocks)
    rows, cols = blocks[0].shape
    tokens = normed.shape[0]

    def kernel(starts_ref, normed_ref, *refs):
        block_refs = refs[:n]
        out_ref, features, weights, sems, acc = refs[n:]
        copies = []
        for i in range(n):
            start = pl.multiple_of(starts_ref[i], rows)
            copies.append(
                (
                    pltpu.make_async_copy(
                        normed_ref.at[:, pl.ds(start, rows)],
                        features.at[:, pl.ds(i * rows, rows)],
                        sems.at[0, i],
                    ),
                    pltpu.make_async_copy(
                        block_refs[i], weights.at[pl.ds(i * rows, rows), :], sems.at[1, i]
                    ),
                )
            )
        for pair in copies:
            for c in pair:
                c.start()
        for g in range(0, n, group):
            last = min(g + group, n)
            for i in range(g, last):
                for c in copies[i]:
                    c.wait()
            part = jnp.dot(
                features[:, g * rows:last * rows],
                weights[g * rows:last * rows, :],
                preferred_element_type=jnp.float32,
            )
            if g == 0:
                acc[...] = part
            else:
                acc[...] += part
        out_ref[...] = acc[...].astype(out_ref.dtype)

    return pl.pallas_call(
        kernel,
        out_shape=jax.ShapeDtypeStruct((tokens, cols), jnp.bfloat16),
        in_specs=[pl.BlockSpec(memory_space=pltpu.SMEM), pl.BlockSpec(memory_space=pl.ANY)]
        + [pl.BlockSpec(memory_space=pl.ANY)] * n,
        out_specs=pl.BlockSpec(memory_space=pltpu.VMEM),
        scratch_shapes=[
            pltpu.VMEM((tokens, n * rows), normed.dtype),
            pltpu.VMEM((n * rows, cols), blocks[0].dtype),
            pltpu.SemaphoreType.DMA((2, n)),
            pltpu.VMEM((tokens, cols), jnp.float32),
        ],
    )(starts, normed, *blocks)


def local_gather(queries, keys, values, out_weight, norm_gain, n_chip, n_head):
    heads_dev = norm_gain.shape[0] // HEAD_DIM
    core = lax.axis_index("core")
    place = lax.axis_index("head") if n_head == 2 else 0
    weight_own = lax.all_gather(out_weight, "chip", axis=0, tiled=True)
    query_block, key_block, value_block = head_blocks([queries, keys, values], n_head, place)
    query_heads, key_heads, value_heads = (
        split_heads(b, heads_dev) for b in (query_block, key_block, value_block)
    )
    kv_state = jnp.einsum(
        "thd,the->hde", key_heads, value_heads, preferred_element_type=jnp.float32
    )
    partner_state, chip_half = chip_scan(kv_state, core, n_chip)
    prefix = chip_finish(exclusive_prefix(chip_half, "chip", n_chip), partner_state, core)
    within_block = within_block_part(query_heads, key_heads, value_heads)
    normed = normalize(query_heads, prefix, within_block, norm_gain)
    gathered = gather_head(normed, n_head, place)
    row_count = gathered.shape[0]
    split = gathered.reshape(row_count, n_chip, 2, out_weight.shape[0])
    weight_own, split = lax.optimization_barrier((weight_own, split))
    weight_other = lax.ppermute(weight_own, "core", SWAP)
    normed_own = lax.dynamic_index_in_dim(split, core, 2, False).reshape(row_count, -1)
    normed_other = lax.dynamic_index_in_dim(split, 1 - core, 2, False).reshape(row_count, -1)
    outcome = jnp.dot(normed_own, weight_own, preferred_element_type=jnp.float32)
    outcome = outcome + jnp.dot(normed_other, weight_other, preferred_element_type=jnp.float32)
    return outcome.astype(jnp.bfloat16)


def local_ring(queries, keys, values, out_weight, norm_gain, n_chip, n_head, order):
    heads_dev = norm_gain.shape[0] // HEAD_DIM
    core = lax.axis_index("core")
    place = lax.axis_index("head")
    n_steps = n_chip // 2
    barrier = lax.optimization_barrier
    key_block, value_block = head_blocks([keys, values], n_head, place)
    ahead, behind = ring_step(out_weight, out_weight, order)
    ahead, behind, key_block, value_block = barrier((ahead, behind, key_block, value_block))
    got = [out_weight, ahead, behind]
    offsets = [0, 1, -1]
    (query_block,) = head_blocks([queries], n_head, place)
    swapped = [lax.ppermute(w, "core", SWAP) for w in got]
    key_heads, value_heads = split_heads(key_block, heads_dev), split_heads(value_block, heads_dev)
    kv_state = jnp.einsum(
        "thd,the->hde", key_heads, value_heads, preferred_element_type=jnp.float32
    )
    partner_state, chip_half = chip_scan(kv_state, core, n_chip)
    chip_prefix_half = exclusive_prefix(chip_half, "chip", n_chip)
    query_heads = split_heads(query_block, heads_dev)
    within_block = within_block_part(query_heads, key_heads, value_heads)
    swapped += [lax.ppermute(w, "core", SWAP) for w in got[len(swapped):]]
    chip_prefix_half, within_block, swapped = barrier((chip_prefix_half, within_block, swapped))
    for step in range(2, n_steps + 1):
        ahead, behind = ring_step(ahead, behind, order, last=step == n_steps)
        if step == n_steps:
            got.append(jnp.concatenate([ahead, behind], 0))
            offsets.append(step)
        else:
            got += [ahead, behind]
            offsets += [step, -step]
    swapped += [lax.ppermute(w, "core", SWAP) for w in got[len(swapped):]]
    prefix = chip_finish(chip_prefix_half, partner_state, core)
    normed = normalize(query_heads, prefix, within_block, norm_gain)
    gathered = gather_head(normed, n_head, place)
    row_count = gathered.shape[0]
    ring_place = jnp.asarray([order.index(j) for j in range(n_chip)], jnp.int32)[lax.axis_index("chip")]
    sources = jnp.asarray(order, jnp.int32)[(ring_place - jnp.asarray(offsets, jnp.int32)) % n_chip]
    cores = jnp.stack([core, 1 - core]).astype(jnp.int32)
    starts = ((sources[:, None] * 2 + cores[None, :]) * out_weight.shape[0]).reshape(-1)
    return project_blocks(gathered, starts, [w for pair in zip(got, swapped) for w in pair], group=2)


def solution(mesh):
    n_seq = mesh.shape["seq"]
    n_head = mesh.shape["head"]
    fine = Mesh(mesh.devices.reshape(n_seq // 2, 2, n_head), ("chip", "core", "head"))
    rows = ("chip", "core", "head")
    order = chip_cycle(fine.devices) if n_head == 2 else None
    if order is None:
        body = functools.partial(local_gather, n_chip=n_seq // 2, n_head=n_head)
    else:
        body = functools.partial(local_ring, n_chip=n_seq // 2, n_head=n_head, order=order)
    return jax.shard_map(
        body,
        mesh=fine,
        in_specs=(
            P(rows, None),
            P(rows, None),
            P(rows, None),
            P(("chip", "core"), "head"),
            P("head"),
        ),
        out_specs=P(("chip", "core"), "head"),
        check_vma=False,
    )
```

```python
import functools

import jax
import jax.numpy as jnp
from jax import lax
from jax.experimental import pallas as pl
from jax.experimental.pallas import tpu as pltpu
from jax.sharding import Mesh
from jax.sharding import PartitionSpec as P

HEAD_DIM = 128
SWAP = [(0, 1), (1, 0)]


def exclusive_prefix(state, axis, size):
    total = state
    shift = 1
    while shift < size:
        pairs = [(i, i + shift) for i in range(size - shift)]
        total = total + lax.ppermute(total, axis, pairs)
        shift *= 2
    return total - state


def pair_order(own, other, place, axis):
    first = jnp.where(place == 0, own, other)
    second = jnp.where(place == 0, other, own)
    return jnp.concatenate([first, second], axis=axis)


def head_blocks(arrays, n_head, place):
    if n_head == 2:
        rows = arrays[0].shape[0]
        width = arrays[0].shape[1] // 2
        stacked = jnp.stack(arrays).reshape(len(arrays), rows, 2, width)
        own = lax.dynamic_index_in_dim(stacked, place, 2, False)
        sent = lax.dynamic_index_in_dim(stacked, 1 - place, 2, False)
        other = lax.ppermute(sent, "head", SWAP)
        block = pair_order(own, other, place, 1)
        return [block[i] for i in range(len(arrays))]
    return [
        lax.all_to_all(a, "head", split_axis=1, concat_axis=0, tiled=True) for a in arrays
    ]


def chip_cycle(devices):
    n = devices.shape[0]
    coords = [getattr(devices[j, 0, 0], "coords", None) for j in range(n)]
    if n < 4 or n > 16 or any(c is None for c in coords):
        return None

    def adjacent(a, b):
        return sum(abs(int(u) - int(v)) for u, v in zip(coords[a], coords[b])) == 1

    path = [0]

    def search():
        if len(path) == n:
            return adjacent(path[-1], path[0])
        for k in range(n):
            if k not in path and adjacent(path[-1], k):
                path.append(k)
                if search():
                    return True
                path.pop()
        return False

    return list(path) if search() else None


def ring_links(order):
    n = len(order)
    forward = [(order[i], order[(i + 1) % n]) for i in range(n)]
    backward = [(order[(i + 1) % n], order[i]) for i in range(n)]
    return forward, backward


def ring_step(ahead, behind, order, last=False):
    forward, backward = ring_links(order)
    if last:
        half_rows = ahead.shape[0] // 2
        return lax.ppermute(ahead[:half_rows], "chip", forward), lax.ppermute(
            behind[half_rows:], "chip", backward
        )
    return lax.ppermute(ahead, "chip", forward), lax.ppermute(behind, "chip", backward)


def within_block_part(query_heads, key_heads, value_heads):
    row_count = query_heads.shape[0]
    block_rows = min(512, row_count)
    parts_list = []
    for first_row in range(0, row_count, block_rows):
        last_row = min(first_row + block_rows, row_count)
        scores = jnp.einsum(
            "thd,shd->hts",
            query_heads[first_row:last_row],
            key_heads[:last_row],
            preferred_element_type=jnp.float32,
        )
        row_index = first_row + lax.broadcasted_iota(jnp.int32, (last_row - first_row, last_row), 0)
        col_index = lax.broadcasted_iota(jnp.int32, (last_row - first_row, last_row), 1)
        scores = jnp.where((col_index <= row_index)[None], scores, jnp.zeros_like(scores)).astype(
            jnp.bfloat16
        )
        parts_list.append(
            jnp.einsum(
                "hts,she->the", scores, value_heads[:last_row], preferred_element_type=jnp.float32
            )
        )
    return jnp.concatenate(parts_list, axis=0)


def normalize(query_heads, prefix, within_block, norm_gain):
    heads_dev = query_heads.shape[1]
    carried = jnp.einsum(
        "thd,hde->the", query_heads, prefix.astype(jnp.bfloat16), preferred_element_type=jnp.float32
    )
    attended = carried + within_block
    mean_square = jnp.mean(attended * attended, axis=2, keepdims=True)
    gain_heads = norm_gain.reshape(heads_dev, HEAD_DIM)
    normed = (attended * lax.rsqrt(mean_square + 1e-06) * gain_heads[None]).astype(jnp.bfloat16)
    return normed.reshape(query_heads.shape[0], heads_dev * HEAD_DIM)


def gather_head(normed, n_head, place):
    if n_head == 2:
        other = lax.ppermute(normed, "head", SWAP)
        return pair_order(normed, other, place, 1)
    return lax.all_gather(normed, "head", axis=1, tiled=True)


def chip_scan(kv_state, core, n_chip):
    partner_state = lax.ppermute(kv_state, "core", SWAP)
    chip_state = kv_state + partner_state
    half = kv_state.shape[0] // 2
    chip_half = lax.dynamic_slice_in_dim(chip_state, core * half, half, 0)
    return partner_state, chip_half


def chip_finish(chip_prefix_half, partner_state, core):
    other_half = lax.ppermute(chip_prefix_half, "core", SWAP)
    chip_prefix = pair_order(chip_prefix_half, other_half, core, 0)
    return chip_prefix + jnp.where(core == 1, partner_state, jnp.zeros_like(partner_state))


def split_heads(block, heads_dev):
    return block.reshape(block.shape[0], heads_dev, HEAD_DIM)


def project_blocks(normed_pair, starts, sources, blocks, group=4):
    n = len(blocks)
    rows, cols = blocks[0].shape
    tokens = normed_pair[0].shape[0]

    def kernel(starts_ref, sources_ref, own_ref, other_ref, *refs):
        block_refs = refs[:n]
        out_ref, features, weights, sems, acc = refs[n:]

        def feature_copy(src_ref, i, start):
            return pltpu.make_async_copy(
                src_ref.at[:, pl.ds(start, rows)],
                features.at[:, pl.ds(i * rows, rows)],
                sems.at[0, i],
            )

        weight_copies = [
            pltpu.make_async_copy(block_refs[i], weights.at[pl.ds(i * rows, rows), :], sems.at[1, i])
            for i in range(n)
        ]
        for i in range(n):
            start = pl.multiple_of(starts_ref[i], rows)

            @pl.when(sources_ref[i] == 0)
            def _():
                feature_copy(own_ref, i, start).start()

            @pl.when(sources_ref[i] != 0)
            def _():
                feature_copy(other_ref, i, start).start()

            weight_copies[i].start()
        for g in range(0, n, group):
            last = min(g + group, n)
            for i in range(g, last):
                feature_copy(own_ref, i, 0).wait()
                weight_copies[i].wait()
            part = jnp.dot(
                features[:, g * rows:last * rows],
                weights[g * rows:last * rows, :],
                preferred_element_type=jnp.float32,
            )
            if g == 0:
                acc[...] = part
            else:
                acc[...] += part
        out_ref[...] = acc[...].astype(out_ref.dtype)

    return pl.pallas_call(
        kernel,
        out_shape=jax.ShapeDtypeStruct((tokens, cols), jnp.bfloat16),
        in_specs=[pl.BlockSpec(memory_space=pltpu.SMEM)] * 2
        + [pl.BlockSpec(memory_space=pl.ANY)] * (2 + n),
        out_specs=pl.BlockSpec(memory_space=pltpu.VMEM),
        scratch_shapes=[
            pltpu.VMEM((tokens, n * rows), blocks[0].dtype),
            pltpu.VMEM((n * rows, cols), blocks[0].dtype),
            pltpu.SemaphoreType.DMA((2, n)),
            pltpu.VMEM((tokens, cols), jnp.float32),
        ],
    )(starts, sources, normed_pair[0], normed_pair[1], *blocks)


def local_gather(queries, keys, values, out_weight, norm_gain, n_chip, n_head):
    heads_dev = norm_gain.shape[0] // HEAD_DIM
    core = lax.axis_index("core")
    place = lax.axis_index("head") if n_head == 2 else 0
    weight_own = lax.all_gather(out_weight, "chip", axis=0, tiled=True)
    query_block, key_block, value_block = head_blocks([queries, keys, values], n_head, place)
    query_heads, key_heads, value_heads = (
        split_heads(b, heads_dev) for b in (query_block, key_block, value_block)
    )
    kv_state = jnp.einsum(
        "thd,the->hde", key_heads, value_heads, preferred_element_type=jnp.float32
    )
    partner_state, chip_half = chip_scan(kv_state, core, n_chip)
    prefix = chip_finish(exclusive_prefix(chip_half, "chip", n_chip), partner_state, core)
    within_block = within_block_part(query_heads, key_heads, value_heads)
    normed = normalize(query_heads, prefix, within_block, norm_gain)
    gathered = gather_head(normed, n_head, place)
    row_count = gathered.shape[0]
    split = gathered.reshape(row_count, n_chip, 2, out_weight.shape[0])
    weight_own, split = lax.optimization_barrier((weight_own, split))
    weight_other = lax.ppermute(weight_own, "core", SWAP)
    normed_own = lax.dynamic_index_in_dim(split, core, 2, False).reshape(row_count, -1)
    normed_other = lax.dynamic_index_in_dim(split, 1 - core, 2, False).reshape(row_count, -1)
    outcome = jnp.dot(normed_own, weight_own, preferred_element_type=jnp.float32)
    outcome = outcome + jnp.dot(normed_other, weight_other, preferred_element_type=jnp.float32)
    return outcome.astype(jnp.bfloat16)


def local_ring(queries, keys, values, out_weight, norm_gain, n_chip, n_head, order):
    heads_dev = norm_gain.shape[0] // HEAD_DIM
    core = lax.axis_index("core")
    place = lax.axis_index("head")
    n_steps = n_chip // 2
    barrier = lax.optimization_barrier
    key_block, value_block = head_blocks([keys, values], n_head, place)
    ahead, behind = ring_step(out_weight, out_weight, order)
    ahead, behind, key_block, value_block = barrier((ahead, behind, key_block, value_block))
    got = [out_weight, ahead, behind]
    offsets = [0, 1, -1]
    (query_block,) = head_blocks([queries], n_head, place)
    swapped = [lax.ppermute(w, "core", SWAP) for w in got]
    key_heads, value_heads = split_heads(key_block, heads_dev), split_heads(value_block, heads_dev)
    kv_state = jnp.einsum(
        "thd,the->hde", key_heads, value_heads, preferred_element_type=jnp.float32
    )
    partner_state, chip_half = chip_scan(kv_state, core, n_chip)
    chip_prefix_half = exclusive_prefix(chip_half, "chip", n_chip)
    query_heads = split_heads(query_block, heads_dev)
    within_block = within_block_part(query_heads, key_heads, value_heads)
    swapped += [lax.ppermute(w, "core", SWAP) for w in got[len(swapped):]]
    chip_prefix_half, within_block, swapped = barrier((chip_prefix_half, within_block, swapped))
    for step in range(2, n_steps + 1):
        ahead, behind = ring_step(ahead, behind, order, last=step == n_steps)
        if step == n_steps:
            got.append(jnp.concatenate([ahead, behind], 0))
            offsets.append(step)
        else:
            got += [ahead, behind]
            offsets += [step, -step]
    swapped += [lax.ppermute(w, "core", SWAP) for w in got[len(swapped):]]
    prefix = chip_finish(chip_prefix_half, partner_state, core)
    normed = normalize(query_heads, prefix, within_block, norm_gain)
    received = lax.ppermute(normed, "head", SWAP)
    width = normed.shape[1]
    ring_place = jnp.asarray([order.index(j) for j in range(n_chip)], jnp.int32)[lax.axis_index("chip")]
    sources = jnp.asarray(order, jnp.int32)[(ring_place - jnp.asarray(offsets, jnp.int32)) % n_chip]
    cores = jnp.stack([core, 1 - core]).astype(jnp.int32)
    starts = ((sources[:, None] * 2 + cores[None, :]) * out_weight.shape[0]).reshape(-1)
    groups = starts // width
    return project_blocks(
        (normed, received),
        starts - groups * width,
        (groups != place).astype(jnp.int32),
        [w for pair in zip(got, swapped) for w in pair],
    )


def solution(mesh):
    n_seq = mesh.shape["seq"]
    n_head = mesh.shape["head"]
    fine = Mesh(mesh.devices.reshape(n_seq // 2, 2, n_head), ("chip", "core", "head"))
    rows = ("chip", "core", "head")
    order = chip_cycle(fine.devices) if n_head == 2 else None
    if order is None:
        body = functools.partial(local_gather, n_chip=n_seq // 2, n_head=n_head)
    else:
        body = functools.partial(local_ring, n_chip=n_seq // 2, n_head=n_head, order=order)
    return jax.shard_map(
        body,
        mesh=fine,
        in_specs=(
            P(rows, None),
            P(rows, None),
            P(rows, None),
            P(("chip", "core"), "head"),
            P("head"),
        ),
        out_specs=P(("chip", "core"), "head"),
        check_vma=False,
    )
```

```python
import functools

import jax
import jax.numpy as jnp
from jax import lax
from jax.experimental import pallas as pl
from jax.experimental.pallas import tpu as pltpu
from jax.sharding import Mesh
from jax.sharding import PartitionSpec as P

HEAD_DIM = 128
SWAP = [(0, 1), (1, 0)]


def exclusive_prefix(state, axis, size):
    total = state
    shift = 1
    while shift < size:
        pairs = [(i, i + shift) for i in range(size - shift)]
        total = total + lax.ppermute(total, axis, pairs)
        shift *= 2
    return total - state


def pair_order(own, other, place, axis):
    first = jnp.where(place == 0, own, other)
    second = jnp.where(place == 0, other, own)
    return jnp.concatenate([first, second], axis=axis)


def head_blocks(arrays, n_head, place):
    if n_head == 2:
        rows = arrays[0].shape[0]
        width = arrays[0].shape[1] // 2
        stacked = jnp.stack(arrays).reshape(len(arrays), rows, 2, width)
        own = lax.dynamic_index_in_dim(stacked, place, 2, False)
        sent = lax.dynamic_index_in_dim(stacked, 1 - place, 2, False)
        other = lax.ppermute(sent, "head", SWAP)
        block = pair_order(own, other, place, 1)
        return [block[i] for i in range(len(arrays))]
    return [
        lax.all_to_all(a, "head", split_axis=1, concat_axis=0, tiled=True) for a in arrays
    ]


def chip_cycle(devices):
    n = devices.shape[0]
    coords = [getattr(devices[j, 0, 0], "coords", None) for j in range(n)]
    if n < 4 or n > 16 or any(c is None for c in coords):
        return None

    def adjacent(a, b):
        return sum(abs(int(u) - int(v)) for u, v in zip(coords[a], coords[b])) == 1

    path = [0]

    def search():
        if len(path) == n:
            return adjacent(path[-1], path[0])
        for k in range(n):
            if k not in path and adjacent(path[-1], k):
                path.append(k)
                if search():
                    return True
                path.pop()
        return False

    return list(path) if search() else None


def ring_links(order):
    n = len(order)
    forward = [(order[i], order[(i + 1) % n]) for i in range(n)]
    backward = [(order[(i + 1) % n], order[i]) for i in range(n)]
    return forward, backward


def ring_step(ahead, behind, order, last=False):
    forward, backward = ring_links(order)
    if last:
        half_rows = ahead.shape[0] // 2
        return lax.ppermute(ahead[:half_rows], "chip", forward), lax.ppermute(
            behind[half_rows:], "chip", backward
        )
    return lax.ppermute(ahead, "chip", forward), lax.ppermute(behind, "chip", backward)


def within_block_part(query_heads, key_heads, value_heads):
    row_count = query_heads.shape[0]
    block_rows = min(512, row_count)
    parts_list = []
    for first_row in range(0, row_count, block_rows):
        last_row = min(first_row + block_rows, row_count)
        scores = jnp.einsum(
            "thd,shd->hts",
            query_heads[first_row:last_row],
            key_heads[:last_row],
            preferred_element_type=jnp.float32,
        )
        row_index = first_row + lax.broadcasted_iota(jnp.int32, (last_row - first_row, last_row), 0)
        col_index = lax.broadcasted_iota(jnp.int32, (last_row - first_row, last_row), 1)
        scores = jnp.where((col_index <= row_index)[None], scores, jnp.zeros_like(scores)).astype(
            jnp.bfloat16
        )
        parts_list.append(
            jnp.einsum(
                "hts,she->the", scores, value_heads[:last_row], preferred_element_type=jnp.float32
            )
        )
    return jnp.concatenate(parts_list, axis=0)


def normalize(query_heads, prefix, within_block, norm_gain):
    heads_dev = query_heads.shape[1]
    carried = jnp.einsum(
        "thd,hde->the", query_heads, prefix.astype(jnp.bfloat16), preferred_element_type=jnp.float32
    )
    attended = carried + within_block
    mean_square = jnp.mean(attended * attended, axis=2, keepdims=True)
    gain_heads = norm_gain.reshape(heads_dev, HEAD_DIM)
    normed = (attended * lax.rsqrt(mean_square + 1e-06) * gain_heads[None]).astype(jnp.bfloat16)
    return normed.reshape(query_heads.shape[0], heads_dev * HEAD_DIM)


def gather_head(normed, n_head, place):
    if n_head == 2:
        other = lax.ppermute(normed, "head", SWAP)
        return pair_order(normed, other, place, 1)
    return lax.all_gather(normed, "head", axis=1, tiled=True)


def chip_scan(kv_state, core, n_chip):
    partner_state = lax.ppermute(kv_state, "core", SWAP)
    chip_state = kv_state + partner_state
    half = kv_state.shape[0] // 2
    chip_half = lax.dynamic_slice_in_dim(chip_state, core * half, half, 0)
    return partner_state, chip_half


def chip_finish(chip_prefix_half, partner_state, core):
    other_half = lax.ppermute(chip_prefix_half, "core", SWAP)
    chip_prefix = pair_order(chip_prefix_half, other_half, core, 0)
    return chip_prefix + jnp.where(core == 1, partner_state, jnp.zeros_like(partner_state))


def split_heads(block, heads_dev):
    return block.reshape(block.shape[0], heads_dev, HEAD_DIM)


def project_blocks(normed_pair, starts, sources, blocks, group=4):
    n = len(blocks)
    rows, cols = blocks[0].shape
    tokens = normed_pair[0].shape[0]

    def kernel(starts_ref, sources_ref, own_ref, other_ref, *refs):
        block_refs = refs[:n]
        out_ref, features, weights, sems, acc = refs[n:]

        def feature_copy(src_ref, i, start):
            return pltpu.make_async_copy(
                src_ref.at[:, pl.ds(start, rows)],
                features.at[:, pl.ds(i * rows, rows)],
                sems.at[0, i],
            )

        weight_copies = [
            pltpu.make_async_copy(block_refs[i], weights.at[pl.ds(i * rows, rows), :], sems.at[1, i])
            for i in range(n)
        ]
        for i in range(n):
            start = pl.multiple_of(starts_ref[i], rows)

            @pl.when(sources_ref[i] == 0)
            def _():
                feature_copy(own_ref, i, start).start()

            @pl.when(sources_ref[i] != 0)
            def _():
                feature_copy(other_ref, i, start).start()

            weight_copies[i].start()
        for g in range(0, n, group):
            last = min(g + group, n)
            for i in range(g, last):
                feature_copy(own_ref, i, 0).wait()
                weight_copies[i].wait()
            part = jnp.dot(
                features[:, g * rows:last * rows],
                weights[g * rows:last * rows, :],
                preferred_element_type=jnp.float32,
            )
            if g == 0:
                acc[...] = part
            else:
                acc[...] += part
        out_ref[...] = acc[...].astype(out_ref.dtype)

    return pl.pallas_call(
        kernel,
        out_shape=jax.ShapeDtypeStruct((tokens, cols), jnp.bfloat16),
        in_specs=[pl.BlockSpec(memory_space=pltpu.SMEM)] * 2
        + [pl.BlockSpec(memory_space=pl.ANY)] * (2 + n),
        out_specs=pl.BlockSpec(memory_space=pltpu.VMEM),
        scratch_shapes=[
            pltpu.VMEM((tokens, n * rows), blocks[0].dtype),
            pltpu.VMEM((n * rows, cols), blocks[0].dtype),
            pltpu.SemaphoreType.DMA((2, n)),
            pltpu.VMEM((tokens, cols), jnp.float32),
        ],
    )(starts, sources, normed_pair[0], normed_pair[1], *blocks)


def local_gather(queries, keys, values, out_weight, norm_gain, n_chip, n_head):
    heads_dev = norm_gain.shape[0] // HEAD_DIM
    core = lax.axis_index("core")
    place = lax.axis_index("head") if n_head == 2 else 0
    weight_own = lax.all_gather(out_weight, "chip", axis=0, tiled=True)
    query_block, key_block, value_block = head_blocks([queries, keys, values], n_head, place)
    query_heads, key_heads, value_heads = (
        split_heads(b, heads_dev) for b in (query_block, key_block, value_block)
    )
    kv_state = jnp.einsum(
        "thd,the->hde", key_heads, value_heads, preferred_element_type=jnp.float32
    )
    partner_state, chip_half = chip_scan(kv_state, core, n_chip)
    prefix = chip_finish(exclusive_prefix(chip_half, "chip", n_chip), partner_state, core)
    within_block = within_block_part(query_heads, key_heads, value_heads)
    normed = normalize(query_heads, prefix, within_block, norm_gain)
    gathered = gather_head(normed, n_head, place)
    row_count = gathered.shape[0]
    split = gathered.reshape(row_count, n_chip, 2, out_weight.shape[0])
    weight_own, split = lax.optimization_barrier((weight_own, split))
    weight_other = lax.ppermute(weight_own, "core", SWAP)
    normed_own = lax.dynamic_index_in_dim(split, core, 2, False).reshape(row_count, -1)
    normed_other = lax.dynamic_index_in_dim(split, 1 - core, 2, False).reshape(row_count, -1)
    outcome = jnp.dot(normed_own, weight_own, preferred_element_type=jnp.float32)
    outcome = outcome + jnp.dot(normed_other, weight_other, preferred_element_type=jnp.float32)
    return outcome.astype(jnp.bfloat16)


def local_ring(queries, keys, values, out_weight, norm_gain, n_chip, n_head, order):
    heads_dev = norm_gain.shape[0] // HEAD_DIM
    core = lax.axis_index("core")
    place = lax.axis_index("head")
    n_steps = n_chip // 2
    barrier = lax.optimization_barrier
    key_block, value_block = head_blocks([keys, values], n_head, place)
    ahead, behind = ring_step(out_weight, out_weight, order)
    ahead, behind, key_block, value_block = barrier((ahead, behind, key_block, value_block))
    got = [out_weight, ahead, behind]
    offsets = [0, 1, -1]
    (query_block,) = head_blocks([queries], n_head, place)
    swapped = [lax.ppermute(w, "core", SWAP) for w in got]
    key_heads, value_heads = split_heads(key_block, heads_dev), split_heads(value_block, heads_dev)
    kv_state = jnp.einsum(
        "thd,the->hde", key_heads, value_heads, preferred_element_type=jnp.float32
    )
    partner_state, chip_half = chip_scan(kv_state, core, n_chip)
    chip_prefix_half = exclusive_prefix(chip_half, "chip", n_chip)
    query_heads = split_heads(query_block, heads_dev)
    within_block = within_block_part(query_heads, key_heads, value_heads)
    swapped += [lax.ppermute(w, "core", SWAP) for w in got[len(swapped):]]
    chip_prefix_half, within_block, swapped = barrier((chip_prefix_half, within_block, swapped))
    prefix = chip_finish(chip_prefix_half, partner_state, core)
    normed = normalize(query_heads, prefix, within_block, norm_gain)
    received = lax.ppermute(normed, "head", SWAP)
    for step in range(2, n_steps + 1):
        if step == 3:
            ahead, behind, received = barrier((ahead, behind, received))
        ahead, behind = ring_step(ahead, behind, order, last=step == n_steps)
        if step == n_steps:
            got.append(jnp.concatenate([ahead, behind], 0))
            offsets.append(step)
        else:
            got += [ahead, behind]
            offsets += [step, -step]
    swapped += [lax.ppermute(w, "core", SWAP) for w in got[len(swapped):]]
    width = normed.shape[1]
    ring_place = jnp.asarray([order.index(j) for j in range(n_chip)], jnp.int32)[lax.axis_index("chip")]
    sources = jnp.asarray(order, jnp.int32)[(ring_place - jnp.asarray(offsets, jnp.int32)) % n_chip]
    cores = jnp.stack([core, 1 - core]).astype(jnp.int32)
    starts = ((sources[:, None] * 2 + cores[None, :]) * out_weight.shape[0]).reshape(-1)
    groups = starts // width
    return project_blocks(
        (normed, received),
        starts - groups * width,
        (groups != place).astype(jnp.int32),
        [w for pair in zip(got, swapped) for w in pair],
    )


def solution(mesh):
    n_seq = mesh.shape["seq"]
    n_head = mesh.shape["head"]
    fine = Mesh(mesh.devices.reshape(n_seq // 2, 2, n_head), ("chip", "core", "head"))
    rows = ("chip", "core", "head")
    order = chip_cycle(fine.devices) if n_head == 2 else None
    if order is None:
        body = functools.partial(local_gather, n_chip=n_seq // 2, n_head=n_head)
    else:
        body = functools.partial(local_ring, n_chip=n_seq // 2, n_head=n_head, order=order)
    return jax.shard_map(
        body,
        mesh=fine,
        in_specs=(
            P(rows, None),
            P(rows, None),
            P(rows, None),
            P(("chip", "core"), "head"),
            P("head"),
        ),
        out_specs=P(("chip", "core"), "head"),
        check_vma=False,
    )
```

```python
import functools

import jax
import jax.numpy as jnp
from jax import lax
from jax.experimental import pallas as pl
from jax.experimental.pallas import tpu as pltpu
from jax.sharding import Mesh
from jax.sharding import PartitionSpec as P

HEAD_DIM = 128
SWAP = [(0, 1), (1, 0)]


def exclusive_prefix(state, axis, size):
    total = state
    shift = 1
    while shift < size:
        pairs = [(i, i + shift) for i in range(size - shift)]
        total = total + lax.ppermute(total, axis, pairs)
        shift *= 2
    return total - state


def pair_order(own, other, place, axis):
    first = jnp.where(place == 0, own, other)
    second = jnp.where(place == 0, other, own)
    return jnp.concatenate([first, second], axis=axis)


def head_blocks(arrays, n_head, place):
    if n_head == 2:
        rows = arrays[0].shape[0]
        width = arrays[0].shape[1] // 2
        stacked = jnp.stack(arrays).reshape(len(arrays), rows, 2, width)
        own = lax.dynamic_index_in_dim(stacked, place, 2, False)
        sent = lax.dynamic_index_in_dim(stacked, 1 - place, 2, False)
        other = lax.ppermute(sent, "head", SWAP)
        block = pair_order(own, other, place, 1)
        return [block[i] for i in range(len(arrays))]
    return [
        lax.all_to_all(a, "head", split_axis=1, concat_axis=0, tiled=True) for a in arrays
    ]


def chip_cycle(devices):
    n = devices.shape[0]
    coords = [getattr(devices[j, 0, 0], "coords", None) for j in range(n)]
    if n < 4 or n > 16 or any(c is None for c in coords):
        return None

    def adjacent(a, b):
        return sum(abs(int(u) - int(v)) for u, v in zip(coords[a], coords[b])) == 1

    path = [0]

    def search():
        if len(path) == n:
            return adjacent(path[-1], path[0])
        for k in range(n):
            if k not in path and adjacent(path[-1], k):
                path.append(k)
                if search():
                    return True
                path.pop()
        return False

    return list(path) if search() else None


def ring_links(order):
    n = len(order)
    forward = [(order[i], order[(i + 1) % n]) for i in range(n)]
    backward = [(order[(i + 1) % n], order[i]) for i in range(n)]
    return forward, backward


def ring_step(ahead, behind, order, last=False):
    forward, backward = ring_links(order)
    if last:
        half_rows = ahead.shape[0] // 2
        return lax.ppermute(ahead[:half_rows], "chip", forward), lax.ppermute(
            behind[half_rows:], "chip", backward
        )
    return lax.ppermute(ahead, "chip", forward), lax.ppermute(behind, "chip", backward)


def within_block_part(query_heads, key_heads, value_heads):
    row_count = query_heads.shape[0]
    block_rows = min(512, row_count)
    parts_list = []
    for first_row in range(0, row_count, block_rows):
        last_row = min(first_row + block_rows, row_count)
        scores = jnp.einsum(
            "thd,shd->hts",
            query_heads[first_row:last_row],
            key_heads[:last_row],
            preferred_element_type=jnp.float32,
        )
        row_index = first_row + lax.broadcasted_iota(jnp.int32, (last_row - first_row, last_row), 0)
        col_index = lax.broadcasted_iota(jnp.int32, (last_row - first_row, last_row), 1)
        scores = jnp.where((col_index <= row_index)[None], scores, jnp.zeros_like(scores)).astype(
            jnp.bfloat16
        )
        parts_list.append(
            jnp.einsum(
                "hts,she->the", scores, value_heads[:last_row], preferred_element_type=jnp.float32
            )
        )
    return jnp.concatenate(parts_list, axis=0)


def normalize(query_heads, prefix, within_block, norm_gain):
    heads_dev = query_heads.shape[1]
    carried = jnp.einsum(
        "thd,hde->the", query_heads, prefix.astype(jnp.bfloat16), preferred_element_type=jnp.float32
    )
    attended = carried + within_block
    mean_square = jnp.mean(attended * attended, axis=2, keepdims=True)
    gain_heads = norm_gain.reshape(heads_dev, HEAD_DIM)
    normed = (attended * lax.rsqrt(mean_square + 1e-06) * gain_heads[None]).astype(jnp.bfloat16)
    return normed.reshape(query_heads.shape[0], heads_dev * HEAD_DIM)


def gather_head(normed, n_head, place):
    if n_head == 2:
        other = lax.ppermute(normed, "head", SWAP)
        return pair_order(normed, other, place, 1)
    return lax.all_gather(normed, "head", axis=1, tiled=True)


def chip_scan(kv_state, core, n_chip):
    partner_state = lax.ppermute(kv_state, "core", SWAP)
    chip_state = kv_state + partner_state
    half = kv_state.shape[0] // 2
    chip_half = lax.dynamic_slice_in_dim(chip_state, core * half, half, 0)
    return partner_state, chip_half


def chip_finish(chip_prefix_half, partner_state, core):
    other_half = lax.ppermute(chip_prefix_half, "core", SWAP)
    chip_prefix = pair_order(chip_prefix_half, other_half, core, 0)
    return chip_prefix + jnp.where(core == 1, partner_state, jnp.zeros_like(partner_state))


def split_heads(block, heads_dev):
    return block.reshape(block.shape[0], heads_dev, HEAD_DIM)


def project_blocks(normed, starts, blocks, group=4):
    n = len(blocks)
    rows, cols = blocks[0].shape
    tokens = normed.shape[0]

    def kernel(starts_ref, normed_ref, *refs):
        block_refs = refs[:n]
        out_ref, features, weights, sems, acc = refs[n:]
        copies = []
        for i in range(n):
            start = pl.multiple_of(starts_ref[i], rows)
            copies.append(
                (
                    pltpu.make_async_copy(
                        normed_ref.at[:, pl.ds(start, rows)],
                        features.at[:, pl.ds(i * rows, rows)],
                        sems.at[0, i],
                    ),
                    pltpu.make_async_copy(
                        block_refs[i], weights.at[pl.ds(i * rows, rows), :], sems.at[1, i]
                    ),
                )
            )
        for pair in copies:
            for c in pair:
                c.start()
        for g in range(0, n, group):
            last = min(g + group, n)
            for i in range(g, last):
                for c in copies[i]:
                    c.wait()
            part = jnp.dot(
                features[:, g * rows:last * rows],
                weights[g * rows:last * rows, :],
                preferred_element_type=jnp.float32,
            )
            if g == 0:
                acc[...] = part
            else:
                acc[...] += part
        out_ref[...] = acc[...].astype(out_ref.dtype)

    return pl.pallas_call(
        kernel,
        out_shape=jax.ShapeDtypeStruct((tokens, cols), jnp.bfloat16),
        in_specs=[pl.BlockSpec(memory_space=pltpu.SMEM), pl.BlockSpec(memory_space=pl.ANY)]
        + [pl.BlockSpec(memory_space=pl.ANY)] * n,
        out_specs=pl.BlockSpec(memory_space=pltpu.VMEM),
        scratch_shapes=[
            pltpu.VMEM((tokens, n * rows), normed.dtype),
            pltpu.VMEM((n * rows, cols), blocks[0].dtype),
            pltpu.SemaphoreType.DMA((2, n)),
            pltpu.VMEM((tokens, cols), jnp.float32),
        ],
    )(starts, normed, *blocks)


def local_gather(queries, keys, values, out_weight, norm_gain, n_chip, n_head):
    heads_dev = norm_gain.shape[0] // HEAD_DIM
    core = lax.axis_index("core")
    place = lax.axis_index("head") if n_head == 2 else 0
    weight_own = lax.all_gather(out_weight, "chip", axis=0, tiled=True)
    query_block, key_block, value_block = head_blocks([queries, keys, values], n_head, place)
    query_heads, key_heads, value_heads = (
        split_heads(b, heads_dev) for b in (query_block, key_block, value_block)
    )
    kv_state = jnp.einsum(
        "thd,the->hde", key_heads, value_heads, preferred_element_type=jnp.float32
    )
    partner_state, chip_half = chip_scan(kv_state, core, n_chip)
    prefix = chip_finish(exclusive_prefix(chip_half, "chip", n_chip), partner_state, core)
    within_block = within_block_part(query_heads, key_heads, value_heads)
    normed = normalize(query_heads, prefix, within_block, norm_gain)
    gathered = gather_head(normed, n_head, place)
    row_count = gathered.shape[0]
    split = gathered.reshape(row_count, n_chip, 2, out_weight.shape[0])
    weight_own, split = lax.optimization_barrier((weight_own, split))
    weight_other = lax.ppermute(weight_own, "core", SWAP)
    normed_own = lax.dynamic_index_in_dim(split, core, 2, False).reshape(row_count, -1)
    normed_other = lax.dynamic_index_in_dim(split, 1 - core, 2, False).reshape(row_count, -1)
    outcome = jnp.dot(normed_own, weight_own, preferred_element_type=jnp.float32)
    outcome = outcome + jnp.dot(normed_other, weight_other, preferred_element_type=jnp.float32)
    return outcome.astype(jnp.bfloat16)


def local_ring(queries, keys, values, out_weight, norm_gain, n_chip, n_head, order):
    heads_dev = norm_gain.shape[0] // HEAD_DIM
    core = lax.axis_index("core")
    place = lax.axis_index("head")
    n_steps = n_chip // 2
    barrier = lax.optimization_barrier
    key_block, value_block = head_blocks([keys, values], n_head, place)
    ahead, behind = ring_step(out_weight, out_weight, order)
    ahead, behind, key_block, value_block = barrier((ahead, behind, key_block, value_block))
    got = [out_weight, ahead, behind]
    offsets = [0, 1, -1]
    (query_block,) = head_blocks([queries], n_head, place)
    swapped = [lax.ppermute(w, "core", SWAP) for w in got]
    key_heads, value_heads = split_heads(key_block, heads_dev), split_heads(value_block, heads_dev)
    kv_state = jnp.einsum(
        "thd,the->hde", key_heads, value_heads, preferred_element_type=jnp.float32
    )
    partner_state, chip_half = chip_scan(kv_state, core, n_chip)
    chip_prefix_half = exclusive_prefix(chip_half, "chip", n_chip)
    query_heads = split_heads(query_block, heads_dev)
    within_block = within_block_part(query_heads, key_heads, value_heads)
    swapped += [lax.ppermute(w, "core", SWAP) for w in got[len(swapped):]]
    chip_prefix_half, within_block, swapped = barrier((chip_prefix_half, within_block, swapped))
    for step in range(2, n_steps + 1):
        if step == n_steps:
            forward, backward = ring_links(order)
            pairs = [(a * 2, b * 2) for a, b in forward] + [(a * 2 + 1, b * 2 + 1) for a, b in backward]
            farthest = jnp.where(core == 0, ahead, behind)
            got.append(lax.ppermute(farthest, ("chip", "core"), pairs))
            offsets.append(step)
            continue
        ahead, behind = ring_step(ahead, behind, order)
        got += [ahead, behind]
        offsets += [step, -step]
    swapped += [lax.ppermute(w, "core", SWAP) for w in got[len(swapped):]]
    prefix = chip_finish(chip_prefix_half, partner_state, core)
    normed = normalize(query_heads, prefix, within_block, norm_gain)
    gathered = gather_head(normed, n_head, place)
    row_count = gathered.shape[0]
    ring_place = jnp.asarray([order.index(j) for j in range(n_chip)], jnp.int32)[lax.axis_index("chip")]
    sources = jnp.asarray(order, jnp.int32)[(ring_place - jnp.asarray(offsets, jnp.int32)) % n_chip]
    cores = jnp.stack([core, 1 - core]).astype(jnp.int32)
    starts = ((sources[:, None] * 2 + cores[None, :]) * out_weight.shape[0]).reshape(-1)
    return project_blocks(gathered, starts, [w for pair in zip(got, swapped) for w in pair])


def solution(mesh):
    n_seq = mesh.shape["seq"]
    n_head = mesh.shape["head"]
    fine = Mesh(mesh.devices.reshape(n_seq // 2, 2, n_head), ("chip", "core", "head"))
    rows = ("chip", "core", "head")
    order = chip_cycle(fine.devices) if n_head == 2 else None
    if order is None:
        body = functools.partial(local_gather, n_chip=n_seq // 2, n_head=n_head)
    else:
        body = functools.partial(local_ring, n_chip=n_seq // 2, n_head=n_head, order=order)
    return jax.shard_map(
        body,
        mesh=fine,
        in_specs=(
            P(rows, None),
            P(rows, None),
            P(rows, None),
            P(("chip", "core"), "head"),
            P("head"),
        ),
        out_specs=P(("chip", "core"), "head"),
        check_vma=False,
    )
```

```python
import functools

import jax
import jax.numpy as jnp
from jax import lax
from jax.experimental import pallas as pl
from jax.experimental.pallas import tpu as pltpu
from jax.sharding import Mesh
from jax.sharding import PartitionSpec as P

HEAD_DIM = 128
SWAP = [(0, 1), (1, 0)]


def exclusive_prefix(state, axis, size):
    total = state
    shift = 1
    while shift < size:
        pairs = [(i, i + shift) for i in range(size - shift)]
        total = total + lax.ppermute(total, axis, pairs)
        shift *= 2
    return total - state


def pair_order(own, other, place, axis):
    first = jnp.where(place == 0, own, other)
    second = jnp.where(place == 0, other, own)
    return jnp.concatenate([first, second], axis=axis)


def head_blocks(arrays, n_head, place):
    if n_head == 2:
        width = arrays[0].shape[1] // 2
        own = [lax.dynamic_slice_in_dim(a, place * width, width, 1) for a in arrays]
        sent = [lax.dynamic_slice_in_dim(a, (1 - place) * width, width, 1) for a in arrays]
        other = lax.ppermute(tuple(sent), "head", SWAP)
        return [pair_order(o, r, place, 0) for o, r in zip(own, other)]
    return [
        lax.all_to_all(a, "head", split_axis=1, concat_axis=0, tiled=True) for a in arrays
    ]


def chip_cycle(devices):
    n = devices.shape[0]
    coords = [getattr(devices[j, 0, 0], "coords", None) for j in range(n)]
    if n < 4 or n > 16 or any(c is None for c in coords):
        return None

    def adjacent(a, b):
        return sum(abs(int(u) - int(v)) for u, v in zip(coords[a], coords[b])) == 1

    path = [0]

    def search():
        if len(path) == n:
            return adjacent(path[-1], path[0])
        for k in range(n):
            if k not in path and adjacent(path[-1], k):
                path.append(k)
                if search():
                    return True
                path.pop()
        return False

    return list(path) if search() else None


def ring_links(order):
    n = len(order)
    forward = [(order[i], order[(i + 1) % n]) for i in range(n)]
    backward = [(order[(i + 1) % n], order[i]) for i in range(n)]
    return forward, backward


def ring_step(ahead, behind, order, last=False):
    forward, backward = ring_links(order)
    if last:
        half_rows = ahead.shape[0] // 2
        return lax.ppermute(ahead[:half_rows], "chip", forward), lax.ppermute(
            behind[half_rows:], "chip", backward
        )
    return lax.ppermute(ahead, "chip", forward), lax.ppermute(behind, "chip", backward)


def within_block_part(query_heads, key_heads, value_heads):
    row_count = query_heads.shape[0]
    block_rows = min(512, row_count)
    parts_list = []
    for first_row in range(0, row_count, block_rows):
        last_row = min(first_row + block_rows, row_count)
        scores = jnp.einsum(
            "thd,shd->hts",
            query_heads[first_row:last_row],
            key_heads[:last_row],
            preferred_element_type=jnp.float32,
        )
        row_index = first_row + lax.broadcasted_iota(jnp.int32, (last_row - first_row, last_row), 0)
        col_index = lax.broadcasted_iota(jnp.int32, (last_row - first_row, last_row), 1)
        scores = jnp.where((col_index <= row_index)[None], scores, jnp.zeros_like(scores)).astype(
            jnp.bfloat16
        )
        parts_list.append(
            jnp.einsum(
                "hts,she->the", scores, value_heads[:last_row], preferred_element_type=jnp.float32
            )
        )
    return jnp.concatenate(parts_list, axis=0)


def normalize(query_heads, prefix, within_block, norm_gain):
    heads_dev = query_heads.shape[1]
    carried = jnp.einsum(
        "thd,hde->the", query_heads, prefix.astype(jnp.bfloat16), preferred_element_type=jnp.float32
    )
    attended = carried + within_block
    mean_square = jnp.mean(attended * attended, axis=2, keepdims=True)
    gain_heads = norm_gain.reshape(heads_dev, HEAD_DIM)
    normed = (attended * lax.rsqrt(mean_square + 1e-06) * gain_heads[None]).astype(jnp.bfloat16)
    return normed.reshape(query_heads.shape[0], heads_dev * HEAD_DIM)


def gather_head(normed, n_head, place):
    if n_head == 2:
        other = lax.ppermute(normed, "head", SWAP)
        return pair_order(normed, other, place, 1)
    return lax.all_gather(normed, "head", axis=1, tiled=True)


def chip_scan(kv_state, core, n_chip):
    partner_state = lax.ppermute(kv_state, "core", SWAP)
    chip_state = kv_state + partner_state
    half = kv_state.shape[0] // 2
    chip_half = lax.dynamic_slice_in_dim(chip_state, core * half, half, 0)
    return partner_state, chip_half


def chip_finish(chip_prefix_half, partner_state, core):
    other_half = lax.ppermute(chip_prefix_half, "core", SWAP)
    chip_prefix = pair_order(chip_prefix_half, other_half, core, 0)
    return chip_prefix + jnp.where(core == 1, partner_state, jnp.zeros_like(partner_state))


def split_heads(block, heads_dev):
    return block.reshape(block.shape[0], heads_dev, HEAD_DIM)


def project_blocks(normed, starts, blocks, group=4):
    n = len(blocks)
    rows, cols = blocks[0].shape
    tokens = normed.shape[0]

    def kernel(starts_ref, normed_ref, *refs):
        block_refs = refs[:n]
        out_ref, features, weights, sems, acc = refs[n:]
        copies = []
        for i in range(n):
            start = pl.multiple_of(starts_ref[i], rows)
            copies.append(
                (
                    pltpu.make_async_copy(
                        normed_ref.at[:, pl.ds(start, rows)],
                        features.at[:, pl.ds(i * rows, rows)],
                        sems.at[0, i],
                    ),
                    pltpu.make_async_copy(
                        block_refs[i], weights.at[pl.ds(i * rows, rows), :], sems.at[1, i]
                    ),
                )
            )
        for pair in copies:
            for c in pair:
                c.start()
        for g in range(0, n, group):
            last = min(g + group, n)
            for i in range(g, last):
                for c in copies[i]:
                    c.wait()
            part = jnp.dot(
                features[:, g * rows:last * rows],
                weights[g * rows:last * rows, :],
                preferred_element_type=jnp.float32,
            )
            if g == 0:
                acc[...] = part
            else:
                acc[...] += part
        out_ref[...] = acc[...].astype(out_ref.dtype)

    return pl.pallas_call(
        kernel,
        out_shape=jax.ShapeDtypeStruct((tokens, cols), jnp.bfloat16),
        in_specs=[pl.BlockSpec(memory_space=pltpu.SMEM), pl.BlockSpec(memory_space=pl.ANY)]
        + [pl.BlockSpec(memory_space=pl.ANY)] * n,
        out_specs=pl.BlockSpec(memory_space=pltpu.VMEM),
        scratch_shapes=[
            pltpu.VMEM((tokens, n * rows), normed.dtype),
            pltpu.VMEM((n * rows, cols), blocks[0].dtype),
            pltpu.SemaphoreType.DMA((2, n)),
            pltpu.VMEM((tokens, cols), jnp.float32),
        ],
    )(starts, normed, *blocks)


def local_gather(queries, keys, values, out_weight, norm_gain, n_chip, n_head):
    heads_dev = norm_gain.shape[0] // HEAD_DIM
    core = lax.axis_index("core")
    place = lax.axis_index("head") if n_head == 2 else 0
    weight_own = lax.all_gather(out_weight, "chip", axis=0, tiled=True)
    query_block, key_block, value_block = head_blocks([queries, keys, values], n_head, place)
    query_heads, key_heads, value_heads = (
        split_heads(b, heads_dev) for b in (query_block, key_block, value_block)
    )
    kv_state = jnp.einsum(
        "thd,the->hde", key_heads, value_heads, preferred_element_type=jnp.float32
    )
    partner_state, chip_half = chip_scan(kv_state, core, n_chip)
    prefix = chip_finish(exclusive_prefix(chip_half, "chip", n_chip), partner_state, core)
    within_block = within_block_part(query_heads, key_heads, value_heads)
    normed = normalize(query_heads, prefix, within_block, norm_gain)
    gathered = gather_head(normed, n_head, place)
    row_count = gathered.shape[0]
    split = gathered.reshape(row_count, n_chip, 2, out_weight.shape[0])
    weight_own, split = lax.optimization_barrier((weight_own, split))
    weight_other = lax.ppermute(weight_own, "core", SWAP)
    normed_own = lax.dynamic_index_in_dim(split, core, 2, False).reshape(row_count, -1)
    normed_other = lax.dynamic_index_in_dim(split, 1 - core, 2, False).reshape(row_count, -1)
    outcome = jnp.dot(normed_own, weight_own, preferred_element_type=jnp.float32)
    outcome = outcome + jnp.dot(normed_other, weight_other, preferred_element_type=jnp.float32)
    return outcome.astype(jnp.bfloat16)


def local_ring(queries, keys, values, out_weight, norm_gain, n_chip, n_head, order):
    heads_dev = norm_gain.shape[0] // HEAD_DIM
    core = lax.axis_index("core")
    place = lax.axis_index("head")
    n_steps = n_chip // 2
    barrier = lax.optimization_barrier
    key_block, value_block = head_blocks([keys, values], n_head, place)
    ahead, behind = ring_step(out_weight, out_weight, order)
    ahead, behind, key_block, value_block = barrier((ahead, behind, key_block, value_block))
    got = [out_weight, ahead, behind]
    offsets = [0, 1, -1]
    (query_block,) = head_blocks([queries], n_head, place)
    swapped = [lax.ppermute(w, "core", SWAP) for w in got]
    key_heads, value_heads = split_heads(key_block, heads_dev), split_heads(value_block, heads_dev)
    kv_state = jnp.einsum(
        "thd,the->hde", key_heads, value_heads, preferred_element_type=jnp.float32
    )
    partner_state, chip_half = chip_scan(kv_state, core, n_chip)
    chip_prefix_half = exclusive_prefix(chip_half, "chip", n_chip)
    query_heads = split_heads(query_block, heads_dev)
    within_block = within_block_part(query_heads, key_heads, value_heads)
    swapped += [lax.ppermute(w, "core", SWAP) for w in got[len(swapped):]]
    chip_prefix_half, within_block, swapped = barrier((chip_prefix_half, within_block, swapped))
    for step in range(2, n_steps + 1):
        if step >= 4:
            early = len(got) - 2
            swapped += [lax.ppermute(w, "core", SWAP) for w in got[len(swapped):early]]
            ahead, behind, swapped = barrier((ahead, behind, swapped))
        ahead, behind = ring_step(ahead, behind, order, last=step == n_steps)
        if step == n_steps:
            got.append(jnp.concatenate([ahead, behind], 0))
            offsets.append(step)
        else:
            got += [ahead, behind]
            offsets += [step, -step]
    swapped += [lax.ppermute(w, "core", SWAP) for w in got[len(swapped):]]
    prefix = chip_finish(chip_prefix_half, partner_state, core)
    normed = normalize(query_heads, prefix, within_block, norm_gain)
    gathered = gather_head(normed, n_head, place)
    row_count = gathered.shape[0]
    ring_place = jnp.asarray([order.index(j) for j in range(n_chip)], jnp.int32)[lax.axis_index("chip")]
    sources = jnp.asarray(order, jnp.int32)[(ring_place - jnp.asarray(offsets, jnp.int32)) % n_chip]
    cores = jnp.stack([core, 1 - core]).astype(jnp.int32)
    starts = ((sources[:, None] * 2 + cores[None, :]) * out_weight.shape[0]).reshape(-1)
    return project_blocks(gathered, starts, [w for pair in zip(got, swapped) for w in pair], group=2)


def solution(mesh):
    n_seq = mesh.shape["seq"]
    n_head = mesh.shape["head"]
    fine = Mesh(mesh.devices.reshape(n_seq // 2, 2, n_head), ("chip", "core", "head"))
    rows = ("chip", "core", "head")
    order = chip_cycle(fine.devices) if n_head == 2 else None
    if order is None:
        body = functools.partial(local_gather, n_chip=n_seq // 2, n_head=n_head)
    else:
        body = functools.partial(local_ring, n_chip=n_seq // 2, n_head=n_head, order=order)
    return jax.shard_map(
        body,
        mesh=fine,
        in_specs=(
            P(rows, None),
            P(rows, None),
            P(rows, None),
            P(("chip", "core"), "head"),
            P("head"),
        ),
        out_specs=P(("chip", "core"), "head"),
        check_vma=False,
    )
```

```python
import functools

import jax
import jax.numpy as jnp
from jax import lax
from jax.experimental import pallas as pl
from jax.experimental.pallas import tpu as pltpu
from jax.sharding import Mesh
from jax.sharding import PartitionSpec as P

HEAD_DIM = 128
SWAP = [(0, 1), (1, 0)]


def exclusive_prefix(state, axis, size):
    total = state
    shift = 1
    while shift < size:
        pairs = [(i, i + shift) for i in range(size - shift)]
        total = total + lax.ppermute(total, axis, pairs)
        shift *= 2
    return total - state


def pair_order(own, other, place, axis):
    first = jnp.where(place == 0, own, other)
    second = jnp.where(place == 0, other, own)
    return jnp.concatenate([first, second], axis=axis)


def head_blocks(arrays, n_head, place):
    if n_head == 2:
        rows = arrays[0].shape[0]
        width = arrays[0].shape[1] // 2
        stacked = jnp.stack(arrays).reshape(len(arrays), rows, 2, width)
        own = lax.dynamic_index_in_dim(stacked, place, 2, False)
        sent = lax.dynamic_index_in_dim(stacked, 1 - place, 2, False)
        other = lax.ppermute(sent, "head", SWAP)
        block = pair_order(own, other, place, 1)
        return [block[i] for i in range(len(arrays))]
    return [
        lax.all_to_all(a, "head", split_axis=1, concat_axis=0, tiled=True) for a in arrays
    ]


def chip_cycle(devices):
    n = devices.shape[0]
    coords = [getattr(devices[j, 0, 0], "coords", None) for j in range(n)]
    if n < 4 or n > 16 or any(c is None for c in coords):
        return None

    def adjacent(a, b):
        return sum(abs(int(u) - int(v)) for u, v in zip(coords[a], coords[b])) == 1

    path = [0]

    def search():
        if len(path) == n:
            return adjacent(path[-1], path[0])
        for k in range(n):
            if k not in path and adjacent(path[-1], k):
                path.append(k)
                if search():
                    return True
                path.pop()
        return False

    return list(path) if search() else None


def ring_links(order):
    n = len(order)
    forward = [(order[i], order[(i + 1) % n]) for i in range(n)]
    backward = [(order[(i + 1) % n], order[i]) for i in range(n)]
    return forward, backward


def ring_step(ahead, behind, order, last=False):
    forward, backward = ring_links(order)
    if last:
        half_rows = ahead.shape[0] // 2
        return lax.ppermute(ahead[:half_rows], "chip", forward), lax.ppermute(
            behind[half_rows:], "chip", backward
        )
    return lax.ppermute(ahead, "chip", forward), lax.ppermute(behind, "chip", backward)


def within_block_part(query_heads, key_heads, value_heads):
    row_count = query_heads.shape[0]
    block_rows = min(512, row_count)
    parts_list = []
    for first_row in range(0, row_count, block_rows):
        last_row = min(first_row + block_rows, row_count)
        scores = jnp.einsum(
            "thd,shd->hts",
            query_heads[first_row:last_row],
            key_heads[:last_row],
            preferred_element_type=jnp.float32,
        )
        row_index = first_row + lax.broadcasted_iota(jnp.int32, (last_row - first_row, last_row), 0)
        col_index = lax.broadcasted_iota(jnp.int32, (last_row - first_row, last_row), 1)
        scores = jnp.where((col_index <= row_index)[None], scores, jnp.zeros_like(scores)).astype(
            jnp.bfloat16
        )
        parts_list.append(
            jnp.einsum(
                "hts,she->the", scores, value_heads[:last_row], preferred_element_type=jnp.float32
            )
        )
    return jnp.concatenate(parts_list, axis=0)


def normalize(query_heads, prefix, within_block, norm_gain):
    heads_dev = query_heads.shape[1]
    carried = jnp.einsum(
        "thd,hde->the", query_heads, prefix.astype(jnp.bfloat16), preferred_element_type=jnp.float32
    )
    attended = carried + within_block
    mean_square = jnp.mean(attended * attended, axis=2, keepdims=True)
    gain_heads = norm_gain.reshape(heads_dev, HEAD_DIM)
    normed = (attended * lax.rsqrt(mean_square + 1e-06) * gain_heads[None]).astype(jnp.bfloat16)
    return normed.reshape(query_heads.shape[0], heads_dev * HEAD_DIM)


def gather_head(normed, n_head, place):
    if n_head == 2:
        other = lax.ppermute(normed, "head", SWAP)
        return pair_order(normed, other, place, 1)
    return lax.all_gather(normed, "head", axis=1, tiled=True)


def chip_scan(kv_state, core, n_chip):
    partner_state = lax.ppermute(kv_state, "core", SWAP)
    chip_state = kv_state + partner_state
    half = kv_state.shape[0] // 2
    chip_half = lax.dynamic_slice_in_dim(chip_state, core * half, half, 0)
    return partner_state, chip_half


def chip_finish(chip_prefix_half, partner_state, core):
    other_half = lax.ppermute(chip_prefix_half, "core", SWAP)
    chip_prefix = pair_order(chip_prefix_half, other_half, core, 0)
    return chip_prefix + jnp.where(core == 1, partner_state, jnp.zeros_like(partner_state))


def split_heads(block, heads_dev):
    return block.reshape(block.shape[0], heads_dev, HEAD_DIM)


def project_blocks(normed, starts, blocks, group=4):
    n = len(blocks)
    rows, cols = blocks[0].shape
    tokens = normed.shape[0]

    def kernel(starts_ref, normed_ref, *refs):
        block_refs = refs[:n]
        out_ref, features, weights, sems, acc = refs[n:]
        copies = []
        for i in range(n):
            start = pl.multiple_of(starts_ref[i], rows)
            copies.append(
                (
                    pltpu.make_async_copy(
                        normed_ref.at[:, pl.ds(start, rows)],
                        features.at[:, pl.ds(i * rows, rows)],
                        sems.at[0, i],
                    ),
                    pltpu.make_async_copy(
                        block_refs[i], weights.at[pl.ds(i * rows, rows), :], sems.at[1, i]
                    ),
                )
            )
        for pair in copies:
            for c in pair:
                c.start()
        for g in range(0, n, group):
            last = min(g + group, n)
            for i in range(g, last):
                for c in copies[i]:
                    c.wait()
            part = jnp.dot(
                features[:, g * rows:last * rows],
                weights[g * rows:last * rows, :],
                preferred_element_type=jnp.float32,
            )
            if g == 0:
                acc[...] = part
            else:
                acc[...] += part
        out_ref[...] = acc[...].astype(out_ref.dtype)

    return pl.pallas_call(
        kernel,
        out_shape=jax.ShapeDtypeStruct((tokens, cols), jnp.bfloat16),
        in_specs=[pl.BlockSpec(memory_space=pltpu.SMEM), pl.BlockSpec(memory_space=pl.ANY)]
        + [pl.BlockSpec(memory_space=pl.ANY)] * n,
        out_specs=pl.BlockSpec(memory_space=pltpu.VMEM),
        scratch_shapes=[
            pltpu.VMEM((tokens, n * rows), normed.dtype),
            pltpu.VMEM((n * rows, cols), blocks[0].dtype),
            pltpu.SemaphoreType.DMA((2, n)),
            pltpu.VMEM((tokens, cols), jnp.float32),
        ],
    )(starts, normed, *blocks)


def local_gather(queries, keys, values, out_weight, norm_gain, n_chip, n_head):
    heads_dev = norm_gain.shape[0] // HEAD_DIM
    core = lax.axis_index("core")
    place = lax.axis_index("head") if n_head == 2 else 0
    weight_own = lax.all_gather(out_weight, "chip", axis=0, tiled=True)
    query_block, key_block, value_block = head_blocks([queries, keys, values], n_head, place)
    query_heads, key_heads, value_heads = (
        split_heads(b, heads_dev) for b in (query_block, key_block, value_block)
    )
    kv_state = jnp.einsum(
        "thd,the->hde", key_heads, value_heads, preferred_element_type=jnp.float32
    )
    partner_state, chip_half = chip_scan(kv_state, core, n_chip)
    prefix = chip_finish(exclusive_prefix(chip_half, "chip", n_chip), partner_state, core)
    within_block = within_block_part(query_heads, key_heads, value_heads)
    normed = normalize(query_heads, prefix, within_block, norm_gain)
    gathered = gather_head(normed, n_head, place)
    row_count = gathered.shape[0]
    split = gathered.reshape(row_count, n_chip, 2, out_weight.shape[0])
    weight_own, split = lax.optimization_barrier((weight_own, split))
    weight_other = lax.ppermute(weight_own, "core", SWAP)
    normed_own = lax.dynamic_index_in_dim(split, core, 2, False).reshape(row_count, -1)
    normed_other = lax.dynamic_index_in_dim(split, 1 - core, 2, False).reshape(row_count, -1)
    outcome = jnp.dot(normed_own, weight_own, preferred_element_type=jnp.float32)
    outcome = outcome + jnp.dot(normed_other, weight_other, preferred_element_type=jnp.float32)
    return outcome.astype(jnp.bfloat16)


def local_ring(queries, keys, values, out_weight, norm_gain, n_chip, n_head, order):
    heads_dev = norm_gain.shape[0] // HEAD_DIM
    core = lax.axis_index("core")
    place = lax.axis_index("head")
    n_steps = n_chip // 2
    barrier = lax.optimization_barrier
    key_block, value_block = head_blocks([keys, values], n_head, place)
    ahead, behind = ring_step(out_weight, out_weight, order)
    ahead, behind, key_block, value_block = barrier((ahead, behind, key_block, value_block))
    got = [out_weight, ahead, behind]
    offsets = [0, 1, -1]
    (query_block,) = head_blocks([queries], n_head, place)
    swapped = [lax.ppermute(w, "core", SWAP) for w in got]
    key_heads, value_heads = split_heads(key_block, heads_dev), split_heads(value_block, heads_dev)
    kv_state = jnp.einsum(
        "thd,the->hde", key_heads, value_heads, preferred_element_type=jnp.float32
    )
    partner_state, chip_half = chip_scan(kv_state, core, n_chip)
    chip_prefix_half = exclusive_prefix(chip_half, "chip", n_chip)
    query_heads = split_heads(query_block, heads_dev)
    within_block = within_block_part(query_heads, key_heads, value_heads)
    swapped += [lax.ppermute(w, "core", SWAP) for w in got[len(swapped):]]
    chip_prefix_half, within_block, swapped = barrier((chip_prefix_half, within_block, swapped))
    for step in range(2, n_steps + 1):
        ahead, behind = ring_step(ahead, behind, order, last=step == n_steps)
        if step == n_steps:
            got.append(jnp.concatenate([ahead, behind], 0))
            offsets.append(step)
        else:
            got += [ahead, behind]
            offsets += [step, -step]
    swapped += [lax.ppermute(w, "core", SWAP) for w in got[len(swapped):]]
    prefix = chip_finish(chip_prefix_half, partner_state, core)
    normed = normalize(query_heads, prefix, within_block, norm_gain)
    gathered = gather_head(normed, n_head, place)
    row_count = gathered.shape[0]
    ring_place = jnp.asarray([order.index(j) for j in range(n_chip)], jnp.int32)[lax.axis_index("chip")]
    sources = jnp.asarray(order, jnp.int32)[(ring_place - jnp.asarray(offsets, jnp.int32)) % n_chip]
    cores = jnp.stack([core, 1 - core]).astype(jnp.int32)
    starts = ((sources[:, None] * 2 + cores[None, :]) * out_weight.shape[0]).reshape(-1)
    return project_blocks(gathered, starts, [w for pair in zip(got, swapped) for w in pair], group=1)


def solution(mesh):
    n_seq = mesh.shape["seq"]
    n_head = mesh.shape["head"]
    fine = Mesh(mesh.devices.reshape(n_seq // 2, 2, n_head), ("chip", "core", "head"))
    rows = ("chip", "core", "head")
    order = chip_cycle(fine.devices) if n_head == 2 else None
    if order is None:
        body = functools.partial(local_gather, n_chip=n_seq // 2, n_head=n_head)
    else:
        body = functools.partial(local_ring, n_chip=n_seq // 2, n_head=n_head, order=order)
    return jax.shard_map(
        body,
        mesh=fine,
        in_specs=(
            P(rows, None),
            P(rows, None),
            P(rows, None),
            P(("chip", "core"), "head"),
            P("head"),
        ),
        out_specs=P(("chip", "core"), "head"),
        check_vma=False,
    )
```
